128 devices in a mesh: row: 8 (over x, core), col: 16 (over y, z).
Axes of the slice: x: 4, y: 4, z: 4, core: 2. Of those that a mesh axis runs over, the one named last changes fastest.
Arguments:
- image: bfloat16 [768, 512, 384], P('row', 'col'), may hold values from -6 to 6
- depth_kernel: bfloat16 [7, 7, 384], replicated, may hold values from -0.875 to 0.875
- weight_in: bfloat16 [384, 1536], replicated, may hold values from -0.3125 to 0.3125
- weight_out: bfloat16 [1536, 384], replicated, may hold values from -0.15625 to 0.15625
- weight_down: bfloat16 [2, 2, 384, 768], replicated, may hold values from -0.15625 to 0.15625
- tissue_mask: int32 [96, 64], P('row', 'col'), may hold values from 0 to 1, as said below
- tile_counts: int32 [8, 16, 16], P('row'), may hold values from 0 to 3, as said below
- tile_owner: int32 [96, 64], P('row', 'col'), may hold values from -1 to 15, as said below
- tile_slot: int32 [96, 64], P('row', 'col'), may hold values from -1 to 17, as said below
- cotangent: bfloat16 [384, 256, 768], P('row', 'col'), may hold values from -6 to 6
Outputs:
- reduced: bfloat16 [384, 256, 768], P('row', 'col')
- grad_image: bfloat16 [768, 512, 384], P('row', 'col')
The draws below stay inside these ranges and needn't reach their ends.
Inputs may be any that keep to these rules, and one draw needn't show every extreme that they name: `tissue_mask`: exactly 288 tiles of each row of devices have tissue; in each row of devices one device, drawn from the seed, is all tissue. `tile_counts`: counts[r, s, o] is the number of tissue tiles of device (r, s) with owner o; each owner receives exactly 18 tiles from its row of devices. `tile_owner`: -1 exactly on tiles without tissue; the tissue tiles of a row of devices, in order of device column and then row-major within a device, go to owners 0, 1, 2, ... in turn. `tile_slot`: -1 exactly on tiles without tissue; else the tile's place among its owner's 18 tiles, in the same order.
All inputs are finite; a program needn't handle non-finite values.
Results may differ from the reference program's by a relative error of at most 0.0057.
Values may be sent and summed in bfloat16 or wider, within the bound.
No kernel may reach another device: no remote copies, remote signals or barrier semaphores. Data moves between devices by JAX's collectives and lax.ppermute only.
A program may use at most 128 MiB of HBM per device.

```python
import jax
import jax.numpy as jnp
from jax import lax

C = 384
FF = 1536
COUT = 768
KS = 7
TRD = 12
TCD = 4
TILES_DEV = 48
LIVE_DEV = 18
LIVE_ROW = 288
CAP = 3
H = 768
W = 512
N_ROW = 8
N_COL = 16


def tile_tables(key):
    folded = jax.random.fold_in(key, 11)
    grouped_tile_list = N_COL * TILES_DEV
    noise_key, weight_key, full_key = jax.random.split(folded, 3)
    random_noise_bits = jax.random.randint(noise_key, (N_ROW, grouped_tile_list), 0, 4096)
    device_load_weight = jax.random.randint(weight_key, (N_ROW, N_COL), 0, 4)
    saturated_device = jax.random.randint(full_key, (N_ROW, 1), 0, N_COL)
    assigned_device = jnp.arange(grouped_tile_list, dtype=jnp.int32) // TILES_DEV
    reward_amount_level = jnp.where(assigned_device[None, :] == saturated_device, 4, device_load_weight[:, assigned_device])
    placement_scores = (reward_amount_level * 4096 + random_noise_bits) * 65536 + jnp.arange(grouped_tile_list, dtype=jnp.int32)[None, :]
    chosen = lax.top_k(placement_scores, LIVE_ROW)[1]
    row_index = jnp.arange(N_ROW, dtype=jnp.int32)[:, None]
    tissue_live = jnp.zeros((N_ROW, grouped_tile_list), jnp.int32).at[row_index, chosen].set(1)
    live_order = jnp.cumsum(tissue_live, axis=1) - 1
    owner_table = jnp.where(tissue_live == 1, live_order % N_COL, -1)
    slot_table = jnp.where(tissue_live == 1, live_order // N_COL, -1)
    owner_hot = (owner_table[:, :, None] == jnp.arange(N_COL)[None, None, :]).astype(jnp.int32)
    device_hot = (assigned_device[:, None] == jnp.arange(N_COL)[None, :]).astype(jnp.int32)
    counts = jnp.sum(device_hot[None, :, :, None] * owner_hot[:, :, None, :], axis=1)
    return (tissue_live, counts, owner_table, slot_table)


def spread(table):
    return table.reshape(N_ROW, N_COL, TRD, TCD).transpose(0, 2, 1, 3).reshape(N_ROW * TRD, N_COL * TCD)


def draw_tissue_mask(key, part):
    return spread(tile_tables(key)[0]).astype(jnp.int32)


def draw_tile_counts(key, part):
    return tile_tables(key)[1].astype(jnp.int32)


def draw_tile_owner(key, part):
    return spread(tile_tables(key)[2]).astype(jnp.int32)


def draw_tile_slot(key, part):
    return spread(tile_tables(key)[3]).astype(jnp.int32)


def shard_levels(stream_key, extent, cuts, least, top_value):
    gain, own = 1.0, jax.random.fold_in(stream_key, 6)
    for position, blocks in cuts:
        draws = jnp.exp(jax.random.uniform(jax.random.fold_in(own, position), (blocks,), jnp.float32, least / len(cuts), top_value / len(cuts)))
        gain = gain * jnp.repeat(draws, extent[position] // blocks).reshape([-1 if axis == position else 1 for axis in range(len(extent))])
    return gain


def noise(rng, extent, deviation, limit, cuts=(), held_as=jnp.bfloat16):
    drawn = deviation * jax.random.normal(rng, extent, jnp.float32)
    if cuts:
        drawn = drawn * shard_levels(rng, extent, cuts, -0.22, 0.18)
    return jnp.clip(drawn, -limit, limit).astype(held_as)


def setup_inputs(seed: int = 0) -> dict:
    keys = jax.random.split(jax.random.key(seed), 11)
    image = noise(keys[0], (H, W, C), 1.0, 6.0, ((0, 8), (1, 16)))
    depth_kernel = noise(keys[1], (KS, KS, C), (KS * KS) ** -0.5, 0.875)
    weight_in = noise(keys[2], (C, FF), C ** -0.5, 0.3125)
    weight_out = noise(keys[3], (FF, C), FF ** -0.5, 0.15625)
    weight_down = noise(keys[4], (2, 2, C, COUT), (4 * C) ** -0.5, 0.15625)
    tissue_mask = draw_tissue_mask(jax.random.fold_in(keys[10], 71), 0)
    tile_counts = draw_tile_counts(jax.random.fold_in(keys[10], 71), 0)
    tile_owner = draw_tile_owner(jax.random.fold_in(keys[10], 71), 0)
    tile_slot = draw_tile_slot(jax.random.fold_in(keys[10], 71), 0)
    cotangent = noise(keys[9], (H // 2, W // 2, COUT), 1.0, 6.0, ((0, 8), (1, 16)))
    return {"image": image, "depth_kernel": depth_kernel, "weight_in": weight_in, "weight_out": weight_out, "weight_down": weight_down, "tissue_mask": tissue_mask, "tile_counts": tile_counts, "tile_owner": tile_owner, "tile_slot": tile_slot, "cotangent": cotangent}


EPSILON = 1e-06
ROOT_HALF = 0.7071067811865476
INV_ROOT_TAU = 0.3989422804014327

def gelu_exact(hidden):
    return 0.5 * hidden * (1.0 + jax.scipy.special.erf(hidden * ROOT_HALF))

def gelu_slope(hidden):
    return 0.5 * (1.0 + jax.scipy.special.erf(hidden * ROOT_HALF)) + hidden * INV_ROOT_TAU * jnp.exp(-0.5 * hidden * hidden)

def depthwise(padded, kernel, height, breadth):
    reach = kernel.shape[0]
    total = jnp.zeros((height, breadth, padded.shape[2]), jnp.float32)
    for shift_r in range(reach):
        for shift_c in range(reach):
            window = padded[shift_r:shift_r + height, shift_c:shift_c + breadth, :].astype(jnp.float32)
            total = total + window * kernel[shift_r, shift_c, :].astype(jnp.float32)
    return total

def normalize(values):
    average = lax.optimization_barrier(jnp.mean(values, axis=-1, keepdims=True))
    centered = values - average
    inv_std = lax.rsqrt(lax.optimization_barrier(jnp.mean(centered * centered, axis=-1, keepdims=True)) + EPSILON)
    return (centered * inv_std, inv_std)

def normalize_back(gradient, normed, inv_std):
    return inv_std * (gradient - lax.optimization_barrier(jnp.mean(gradient, axis=-1, keepdims=True)) - normed * lax.optimization_barrier(jnp.mean(gradient * normed, axis=-1, keepdims=True)))

def to_tiles(field, tile_side):
    height, breadth, channels = field.shape
    blocks = field.reshape(height // tile_side, tile_side, breadth // tile_side, tile_side, channels)
    return blocks.transpose(0, 2, 1, 3, 4).reshape(height // tile_side * (breadth // tile_side), tile_side * tile_side * channels)

def from_tiles(tiles, height, breadth, tile_side, channels):
    blocks = tiles.reshape(height // tile_side, breadth // tile_side, tile_side, tile_side, channels)
    return blocks.transpose(0, 2, 1, 3, 4).reshape(height, breadth, channels)

def to_patches(field):
    height, breadth, channels = field.shape
    return field.reshape(height // 2, 2, breadth // 2, 2, channels).transpose(0, 2, 1, 3, 4).reshape(height // 2 * (breadth // 2), 4 * channels)

def from_patches(patches, height, breadth, channels):
    return patches.reshape(height // 2, breadth // 2, 2, 2, channels).transpose(0, 2, 1, 3, 4).reshape(height, breadth, channels)

def times_transposed(left, right):
    return lax.dot_general(left, right, (((1,), (1,)), ((), ())), preferred_element_type=jnp.float32)

def branch_start(owned, channels, weight_in):
    normed, inv_std = normalize(owned.reshape(-1, channels).astype(jnp.float32))
    hidden = jnp.dot(normed.astype(jnp.bfloat16), weight_in, preferred_element_type=jnp.float32)
    return (normed, inv_std, hidden)

def route(tile_counts, tile_owner, tile_slot):
    tile_rows, tile_cols = tile_owner.shape
    owner_flat = tile_owner.reshape(-1).astype(jnp.int32)
    slot_flat = tile_slot.reshape(-1).astype(jnp.int32)
    tile_ids = jnp.arange(tile_rows * tile_cols, dtype=jnp.int32)
    device_row = tile_ids // tile_cols // TRD
    device_col = tile_ids % tile_cols // TCD
    counts_int = tile_counts.astype(jnp.int32)
    before = (jnp.cumsum(counts_int, axis=1) - counts_int).astype(jnp.int32)
    owner_safe = jnp.clip(owner_flat, 0, N_COL - 1).astype(jnp.int32)
    base_sum = before[device_row, device_col, owner_safe]
    quota_count = counts_int[device_row, device_col, owner_safe]
    offset_rank = slot_flat - base_sum
    routed = (owner_flat >= 0) & (offset_rank >= 0) & (offset_rank < CAP) & (offset_rank < quota_count) & (slot_flat < LIVE_DEV)
    place_index = jnp.where(routed, (device_row * N_COL + owner_safe) * LIVE_DEV + slot_flat, 0).astype(jnp.int32)
    return (routed, place_index)

def collect(tiles, routed, place_index, slot_total):
    retained = jnp.where(routed[:, None], tiles.astype(jnp.float32), jnp.float32(0.0))
    return jnp.zeros((slot_total, tiles.shape[1]), jnp.float32).at[place_index].add(retained).astype(jnp.bfloat16)

def deliver(owned, routed, place_index, mask_column):
    return jnp.where(routed[:, None], owned[place_index].astype(jnp.float32), jnp.float32(0.0)) * mask_column

def reference(image, depth_kernel, weight_in, weight_out, weight_down, tissue_mask, tile_counts, tile_owner, tile_slot, cotangent):
    height, breadth, channels = image.shape
    tile_side = height // tissue_mask.shape[0]
    outputs = weight_down.shape[3]
    tile_width = tile_side * tile_side * channels
    slot_total = N_ROW * N_COL * LIVE_DEV
    reach = KS // 2
    routed, place_index = route(tile_counts, tile_owner, tile_slot)
    mask_column = tissue_mask.reshape(-1, 1).astype(jnp.float32)
    padded = jnp.pad(image, ((reach, reach), (reach, reach), (0, 0)))
    mixed = depthwise(padded, depth_kernel, height, breadth).astype(jnp.bfloat16)
    owned = collect(to_tiles(mixed, tile_side), routed, place_index, slot_total)
    normed, inv_std, hidden = branch_start(owned, channels, weight_in)
    activated = gelu_exact(hidden).astype(jnp.bfloat16)
    branch = jnp.dot(activated, weight_out, preferred_element_type=jnp.float32).astype(jnp.bfloat16)
    branch_tiles = deliver(branch.reshape(slot_total, tile_width), routed, place_index, mask_column)
    summed = (image.astype(jnp.float32) + from_tiles(branch_tiles, height, breadth, tile_side, channels)).astype(jnp.bfloat16)
    down_normed, down_inv = normalize(summed.astype(jnp.float32))
    weight_flat = weight_down.reshape(4 * channels, outputs)
    reduced = jnp.dot(to_patches(down_normed.astype(jnp.bfloat16)), weight_flat, preferred_element_type=jnp.float32)
    reduced = reduced.astype(jnp.bfloat16).reshape(height // 2, breadth // 2, outputs)
    grad_patches = times_transposed(cotangent.reshape(-1, outputs), weight_flat)
    grad_normed = from_patches(grad_patches, height, breadth, channels)
    grad_summed = normalize_back(grad_normed, down_normed, down_inv).astype(jnp.bfloat16)
    grad_owned = collect(to_tiles(grad_summed, tile_side), routed, place_index, slot_total).reshape(-1, channels)
    grad_hidden = (times_transposed(grad_owned, weight_out) * gelu_slope(hidden)).astype(jnp.bfloat16)
    grad_norm_in = times_transposed(grad_hidden, weight_in)
    grad_owned_mixed = normalize_back(grad_norm_in, normed, inv_std).astype(jnp.bfloat16)
    grad_tiles = deliver(grad_owned_mixed.reshape(slot_total, tile_width), routed, place_index, mask_column)
    grad_mixed = from_tiles(grad_tiles, height, breadth, tile_side, channels).astype(jnp.bfloat16)
    grad_padded = jnp.pad(grad_mixed, ((reach, reach), (reach, reach), (0, 0)))
    grad_image = (grad_summed.astype(jnp.float32) + depthwise(grad_padded, depth_kernel[::-1, ::-1, :], height, breadth)).astype(jnp.bfloat16)
    return (reduced, grad_image)
```

```python
import jax
import jax.numpy as jnp
from jax import lax
from jax.sharding import PartitionSpec as P

KS = 7
LIVE_DEV = 18


EPSILON = 1e-06
ROOT_HALF = 0.7071067811865476
INV_ROOT_TAU = 0.3989422804014327


def with_halo(cells, sides, width):
    for axis, dim in sides:
        count = lax.axis_size(axis)
        ends = count - 1
        head = lax.slice_in_dim(cells, 0, width, axis=dim)
        tail = lax.slice_in_dim(cells, cells.shape[dim] - width, cells.shape[dim], axis=dim)
        cells = jnp.concatenate(
            [
                lax.ppermute(tail, axis, [(i, (i + 1) % count) for i in range(ends)]),
                cells,
                lax.ppermute(head, axis, [((i + 1) % count, i) for i in range(ends)]),
            ],
            axis=dim,
        )
    return cells


def depthwise(padded, kernel, height, breadth):
    reach = kernel.shape[0]
    total = jnp.zeros((height, breadth, padded.shape[2]), jnp.float32)
    for shift_r in range(reach):
        for shift_c in range(reach):
            window = padded[shift_r : shift_r + height, shift_c : shift_c + breadth, :].astype(
                jnp.float32
            )
            total = total + window * kernel[shift_r, shift_c, :].astype(jnp.float32)
    return total


def normalize(values):
    average = jnp.mean(values, axis=-1, keepdims=True)
    centered = values - average
    inv_std = lax.rsqrt(jnp.mean(centered * centered, axis=-1, keepdims=True) + EPSILON)
    return (centered * inv_std, inv_std)


def normalize_back(gradient, normed, inv_std):
    return inv_std * (
        gradient
        - jnp.mean(gradient, axis=-1, keepdims=True)
        - normed * jnp.mean(gradient * normed, axis=-1, keepdims=True)
    )


def times_transposed(left, right):
    return lax.dot_general(
        left, right, (((1,), (1,)), ((), ())), preferred_element_type=jnp.float32
    )


def routed_tiles(tile_counts, tile_owner, tile_slot, peer_count, capacity):
    count_table = tile_counts[0]
    before = jnp.cumsum(count_table, axis=0) - count_table
    column_ids = jnp.arange(peer_count, dtype=jnp.int32)
    own_column = column_ids == lax.axis_index("col")
    my_bases = jnp.sum(jnp.where(own_column[:, None], before, 0), axis=0)
    my_counts = jnp.sum(jnp.where(own_column[:, None], count_table, 0), axis=0)
    owner_hits = tile_owner[:, :, None] == column_ids[None, None, :]
    base = jnp.sum(jnp.where(owner_hits, my_bases[None, None, :], 0), axis=2)
    quota = jnp.sum(jnp.where(owner_hits, my_counts[None, None, :], 0), axis=2)
    rank = tile_slot - base
    return (
        (tile_owner >= 0)
        & (rank >= 0)
        & (rank < capacity)
        & (rank < quota)
        & (tile_slot < LIVE_DEV)
    )


def on_device(
    image,
    depth_kernel,
    weight_in,
    weight_out,
    weight_down,
    tissue_mask,
    tile_counts,
    tile_owner,
    tile_slot,
    cotangent,
):
    height, breadth, channels = image.shape
    tile_rows, tile_cols = tissue_mask.shape
    tile_side = height // tile_rows
    outputs = weight_down.shape[3]
    reach = KS // 2
    peer_count = lax.axis_size("col")
    capacity = tile_rows * tile_cols // peer_count
    pixels = height * breadth
    routed = routed_tiles(tile_counts, tile_owner, tile_slot, peer_count, capacity)
    live = routed & (tissue_mask != 0)
    live_px = jnp.broadcast_to(
        live[:, None, :, None], (tile_rows, tile_side, tile_cols, tile_side)
    ).reshape(pixels, 1)
    padded = with_halo(image, (("row", 0), ("col", 1)), reach)
    mixed = depthwise(padded, depth_kernel, height, breadth).astype(jnp.bfloat16)
    normed, inv_std = normalize(mixed.reshape(pixels, channels).astype(jnp.float32))
    hidden = jnp.dot(normed.astype(jnp.bfloat16), weight_in, preferred_element_type=jnp.float32)
    cdf = 0.5 * (1.0 + jax.scipy.special.erf(hidden * ROOT_HALF))
    activated = (hidden * cdf).astype(jnp.bfloat16)
    branch = jnp.dot(activated, weight_out, preferred_element_type=jnp.float32).astype(jnp.bfloat16)
    branch_px = jnp.where(live_px, branch.astype(jnp.float32), 0.0)
    summed = (image.reshape(pixels, channels).astype(jnp.float32) + branch_px).astype(jnp.bfloat16)
    down_normed, down_inv = normalize(summed.astype(jnp.float32))
    down_low = down_normed.astype(jnp.bfloat16).reshape(height // 2, 2, breadth // 2, 2 * channels)
    weight_pair = weight_down.reshape(2, 2 * channels, outputs)
    reduced = jnp.dot(down_low[:, 0], weight_pair[0], preferred_element_type=jnp.float32) + jnp.dot(
        down_low[:, 1], weight_pair[1], preferred_element_type=jnp.float32
    )
    reduced = reduced.astype(jnp.bfloat16)
    grad_pair = [
        lax.dot_general(
            cotangent, weight_pair[a], (((2,), (1,)), ((), ())), preferred_element_type=jnp.float32
        )
        for a in range(2)
    ]
    grad_normed = jnp.stack(grad_pair, axis=1).reshape(pixels, channels)
    grad_summed = normalize_back(grad_normed, down_normed, down_inv).astype(jnp.bfloat16)
    slope = cdf + hidden * INV_ROOT_TAU * jnp.exp(-0.5 * hidden * hidden)
    grad_hidden = (times_transposed(grad_summed, weight_out) * slope).astype(jnp.bfloat16)
    grad_norm_in = times_transposed(grad_hidden, weight_in)
    grad_owned_mixed = normalize_back(grad_norm_in, normed, inv_std).astype(jnp.bfloat16)
    grad_mixed = jnp.where(live_px, grad_owned_mixed, jnp.zeros_like(grad_owned_mixed))
    grad_padded = with_halo(grad_mixed.reshape(height, breadth, channels), (("row", 0), ("col", 1)), reach)
    grad_image = (
        grad_summed.reshape(height, breadth, channels).astype(jnp.float32)
        + depthwise(grad_padded, depth_kernel[::-1, ::-1, :], height, breadth)
    ).astype(jnp.bfloat16)
    return (reduced, grad_image)


def solution(mesh):
    in_specs = (
        P("row", "col", None),
        P(),
        P(),
        P(),
        P(),
        P("row", "col"),
        P("row", None, None),
        P("row", "col"),
        P("row", "col"),
        P("row", "col", None),
    )
    out_specs = (P("row", "col", None), P("row", "col", None))
    return jax.shard_map(
        on_device, mesh=mesh, in_specs=in_specs, out_specs=out_specs, check_vma=False
    )
```

```python
import jax
import jax.numpy as jnp
from jax import lax
from jax.sharding import PartitionSpec as P
from jax.experimental import pallas as pl
from jax.experimental.pallas import tpu as pltpu

KS = 7
LIVE_DEV = 18


EPSILON = 1e-06
ROOT_HALF = 0.7071067811865476
INV_ROOT_TAU = 0.3989422804014327


def with_halo(cells, sides, width):
    for axis, dim in sides:
        count = lax.axis_size(axis)
        ends = count - 1
        head = lax.slice_in_dim(cells, 0, width, axis=dim)
        tail = lax.slice_in_dim(cells, cells.shape[dim] - width, cells.shape[dim], axis=dim)
        cells = jnp.concatenate(
            [
                lax.ppermute(tail, axis, [(i, (i + 1) % count) for i in range(ends)]),
                cells,
                lax.ppermute(head, axis, [((i + 1) % count, i) for i in range(ends)]),
            ],
            axis=dim,
        )
    return cells


def depthwise_kernel(x_ref, k_ref, *rest, reach, chunk):
    if len(rest) == 4:
        base_ref, out_ref, shifted_ref, total_ref = rest
    else:
        base_ref = None
        out_ref, shifted_ref, total_ref = rest
    height, breadth, _ = out_ref.shape
    side = 2 * reach + 1
    for shift_c in range(side):
        shifted_ref[...] = x_ref[:, shift_c : shift_c + breadth, :].astype(jnp.float32)

        def body(step, carry, shift_c=shift_c):
            start = pl.multiple_of(step * chunk, chunk)
            if shift_c > 0:
                total = total_ref[pl.ds(start, chunk)]
            elif base_ref is not None:
                total = base_ref[pl.ds(start, chunk)].astype(jnp.float32)
            else:
                total = jnp.zeros((chunk, breadth, out_ref.shape[2]), jnp.float32)
            for shift_r in range(side):
                tap = k_ref[pl.ds(shift_r * side + shift_c, 1), :]
                total = total + shifted_ref[pl.ds(start + shift_r, chunk)] * tap[None]
            if shift_c == side - 1:
                out_ref[pl.ds(start, chunk)] = total.astype(out_ref.dtype)
            else:
                total_ref[pl.ds(start, chunk)] = total
            return carry

        lax.fori_loop(0, height // chunk, body, 0)


def depthwise(padded, kernel, height, breadth, base=None, lanes=128, chunk=8):
    side = kernel.shape[0]
    reach = side // 2
    channels = padded.shape[2]
    taps = kernel.reshape(side * side, channels).astype(jnp.float32)
    in_specs = [
        pl.BlockSpec((height + 2 * reach, breadth + 2 * reach, lanes), lambda c: (0, 0, c)),
        pl.BlockSpec((side * side, lanes), lambda c: (0, c)),
    ]
    operands = [padded, taps]
    if base is not None:
        in_specs.append(pl.BlockSpec((height, breadth, lanes), lambda c: (0, 0, c)))
        operands.append(base)
    return pl.pallas_call(
        lambda *refs: depthwise_kernel(*refs, reach=reach, chunk=chunk),
        grid=(channels // lanes,),
        in_specs=in_specs,
        out_specs=pl.BlockSpec((height, breadth, lanes), lambda c: (0, 0, c)),
        out_shape=jax.ShapeDtypeStruct((height, breadth, channels), jnp.bfloat16),
        scratch_shapes=[
            pltpu.VMEM((height + 2 * reach, breadth, lanes), jnp.float32),
            pltpu.VMEM((height, breadth, lanes), jnp.float32),
        ],
    )(*operands)


def normalize(values):
    average = jnp.mean(values, axis=-1, keepdims=True)
    centered = values - average
    inv_std = lax.rsqrt(jnp.mean(centered * centered, axis=-1, keepdims=True) + EPSILON)
    return (centered * inv_std, inv_std)


def normalize_back(gradient, normed, inv_std):
    return inv_std * (
        gradient
        - jnp.mean(gradient, axis=-1, keepdims=True)
        - normed * jnp.mean(gradient * normed, axis=-1, keepdims=True)
    )


def times_transposed(left, right):
    return lax.dot_general(
        left, right, (((1,), (1,)), ((), ())), preferred_element_type=jnp.float32
    )


def routed_tiles(tile_counts, tile_owner, tile_slot, peer_count, capacity):
    count_table = tile_counts[0]
    before = jnp.cumsum(count_table, axis=0) - count_table
    column_ids = jnp.arange(peer_count, dtype=jnp.int32)
    own_column = column_ids == lax.axis_index("col")
    my_bases = jnp.sum(jnp.where(own_column[:, None], before, 0), axis=0)
    my_counts = jnp.sum(jnp.where(own_column[:, None], count_table, 0), axis=0)
    owner_hits = tile_owner[:, :, None] == column_ids[None, None, :]
    base = jnp.sum(jnp.where(owner_hits, my_bases[None, None, :], 0), axis=2)
    quota = jnp.sum(jnp.where(owner_hits, my_counts[None, None, :], 0), axis=2)
    rank = tile_slot - base
    return (
        (tile_owner >= 0)
        & (rank >= 0)
        & (rank < capacity)
        & (rank < quota)
        & (tile_slot < LIVE_DEV)
    )


def on_device(
    image,
    depth_kernel,
    weight_in,
    weight_out,
    weight_down,
    tissue_mask,
    tile_counts,
    tile_owner,
    tile_slot,
    cotangent,
):
    height, breadth, channels = image.shape
    tile_rows, tile_cols = tissue_mask.shape
    tile_side = height // tile_rows
    outputs = weight_down.shape[3]
    reach = KS // 2
    peer_count = lax.axis_size("col")
    capacity = tile_rows * tile_cols // peer_count
    pixels = height * breadth
    routed = routed_tiles(tile_counts, tile_owner, tile_slot, peer_count, capacity)
    live = routed & (tissue_mask != 0)
    live_px = jnp.broadcast_to(
        live[:, None, :, None], (tile_rows, tile_side, tile_cols, tile_side)
    ).reshape(pixels, 1)
    padded = with_halo(image, (("row", 0), ("col", 1)), reach)
    mixed = depthwise(padded, depth_kernel, height, breadth)
    normed, inv_std = normalize(mixed.reshape(pixels, channels).astype(jnp.float32))
    hidden = jnp.dot(normed.astype(jnp.bfloat16), weight_in, preferred_element_type=jnp.float32)
    cdf = 0.5 * (1.0 + jax.scipy.special.erf(hidden * ROOT_HALF))
    activated = (hidden * cdf).astype(jnp.bfloat16)
    branch = jnp.dot(activated, weight_out, preferred_element_type=jnp.float32).astype(jnp.bfloat16)
    branch_px = jnp.where(live_px, branch.astype(jnp.float32), 0.0)
    summed = (image.reshape(pixels, channels).astype(jnp.float32) + branch_px).astype(jnp.bfloat16)
    down_normed, down_inv = normalize(summed.astype(jnp.float32))
    down_low = down_normed.astype(jnp.bfloat16).reshape(height // 2, 2, breadth // 2, 2 * channels)
    weight_pair = weight_down.reshape(2, 2 * channels, outputs)
    reduced = jnp.dot(down_low[:, 0], weight_pair[0], preferred_element_type=jnp.float32) + jnp.dot(
        down_low[:, 1], weight_pair[1], preferred_element_type=jnp.float32
    )
    reduced = reduced.astype(jnp.bfloat16)
    grad_pair = [
        lax.dot_general(
            cotangent, weight_pair[a], (((2,), (1,)), ((), ())), preferred_element_type=jnp.float32
        )
        for a in range(2)
    ]
    grad_normed = jnp.stack(grad_pair, axis=1).reshape(pixels, channels)
    grad_summed = normalize_back(grad_normed, down_normed, down_inv).astype(jnp.bfloat16)
    slope = cdf + hidden * INV_ROOT_TAU * jnp.exp(-0.5 * hidden * hidden)
    grad_hidden = (times_transposed(grad_summed, weight_out) * slope).astype(jnp.bfloat16)
    grad_norm_in = times_transposed(grad_hidden, weight_in)
    grad_owned_mixed = normalize_back(grad_norm_in, normed, inv_std).astype(jnp.bfloat16)
    grad_mixed = jnp.where(live_px, grad_owned_mixed, jnp.zeros_like(grad_owned_mixed))
    grad_padded = with_halo(grad_mixed.reshape(height, breadth, channels), (("row", 0), ("col", 1)), reach)
    grad_image = depthwise(
        grad_padded, depth_kernel[::-1, ::-1, :], height, breadth, base=grad_summed.reshape(height, breadth, channels)
    )
    return (reduced, grad_image)


def solution(mesh):
    in_specs = (
        P("row", "col", None),
        P(),
        P(),
        P(),
        P(),
        P("row", "col"),
        P("row", None, None),
        P("row", "col"),
        P("row", "col"),
        P("row", "col", None),
    )
    out_specs = (P("row", "col", None), P("row", "col", None))
    return jax.shard_map(
        on_device, mesh=mesh, in_specs=in_specs, out_specs=out_specs, check_vma=False
    )
```

```python
import jax
import jax.numpy as jnp
from jax import lax
from jax.sharding import PartitionSpec as P
from jax.experimental import pallas as pl
from jax.experimental.pallas import tpu as pltpu

KS = 7
LIVE_DEV = 18


EPSILON = 1e-06
ROOT_HALF = 0.7071067811865476
INV_ROOT_TAU = 0.3989422804014327


def with_halo(cells, sides, width):
    for axis, dim in sides:
        count = lax.axis_size(axis)
        ends = count - 1
        head = lax.slice_in_dim(cells, 0, width, axis=dim)
        tail = lax.slice_in_dim(cells, cells.shape[dim] - width, cells.shape[dim], axis=dim)
        cells = jnp.concatenate(
            [
                lax.ppermute(tail, axis, [(i, (i + 1) % count) for i in range(ends)]),
                cells,
                lax.ppermute(head, axis, [((i + 1) % count, i) for i in range(ends)]),
            ],
            axis=dim,
        )
    return cells


def depthwise_kernel(x_ref, k_ref, *rest, reach, chunk):
    if len(rest) == 4:
        base_ref, out_ref, shifted_ref, total_ref = rest
    else:
        base_ref = None
        out_ref, shifted_ref, total_ref = rest
    height, breadth, _ = out_ref.shape
    side = 2 * reach + 1
    for shift_c in range(side):
        shifted_ref[...] = x_ref[:, shift_c : shift_c + breadth, :].astype(jnp.float32)

        def body(step, carry, shift_c=shift_c):
            start = pl.multiple_of(step * chunk, chunk)
            if shift_c > 0:
                total = total_ref[pl.ds(start, chunk)]
            elif base_ref is not None:
                total = base_ref[pl.ds(start, chunk)].astype(jnp.float32)
            else:
                total = jnp.zeros((chunk, breadth, out_ref.shape[2]), jnp.float32)
            for shift_r in range(side):
                tap = k_ref[pl.ds(shift_r * side + shift_c, 1), :]
                total = total + shifted_ref[pl.ds(start + shift_r, chunk)] * tap[None]
            if shift_c == side - 1:
                out_ref[pl.ds(start, chunk)] = total.astype(out_ref.dtype)
            else:
                total_ref[pl.ds(start, chunk)] = total
            return carry

        lax.fori_loop(0, height // chunk, body, 0)


def depthwise(padded, kernel, height, breadth, base=None, lanes=128, chunk=8):
    side = kernel.shape[0]
    reach = side // 2
    channels = padded.shape[2]
    taps = kernel.reshape(side * side, channels).astype(jnp.float32)
    in_specs = [
        pl.BlockSpec((height + 2 * reach, breadth + 2 * reach, lanes), lambda c: (0, 0, c)),
        pl.BlockSpec((side * side, lanes), lambda c: (0, c)),
    ]
    operands = [padded, taps]
    if base is not None:
        in_specs.append(pl.BlockSpec((height, breadth, lanes), lambda c: (0, 0, c)))
        operands.append(base)
    return pl.pallas_call(
        lambda *refs: depthwise_kernel(*refs, reach=reach, chunk=chunk),
        grid=(channels // lanes,),
        in_specs=in_specs,
        out_specs=pl.BlockSpec((height, breadth, lanes), lambda c: (0, 0, c)),
        out_shape=jax.ShapeDtypeStruct((height, breadth, channels), jnp.bfloat16),
        scratch_shapes=[
            pltpu.VMEM((height + 2 * reach, breadth, lanes), jnp.float32),
            pltpu.VMEM((height, breadth, lanes), jnp.float32),
        ],
    )(*operands)


def normalize(values):
    average = jnp.mean(values, axis=-1, keepdims=True)
    centered = values - average
    inv_std = lax.rsqrt(jnp.mean(centered * centered, axis=-1, keepdims=True) + EPSILON)
    return (centered * inv_std, inv_std)


def normalize_back(gradient, normed, inv_std):
    return inv_std * (
        gradient
        - jnp.mean(gradient, axis=-1, keepdims=True)
        - normed * jnp.mean(gradient * normed, axis=-1, keepdims=True)
    )


def times_transposed(left, right):
    return lax.dot_general(
        left, right, (((1,), (1,)), ((), ())), preferred_element_type=jnp.float32
    )


def routed_tiles(tile_counts, tile_owner, tile_slot, peer_count, capacity):
    count_table = tile_counts[0]
    before = jnp.cumsum(count_table, axis=0) - count_table
    column_ids = jnp.arange(peer_count, dtype=jnp.int32)
    own_column = column_ids == lax.axis_index("col")
    my_bases = jnp.sum(jnp.where(own_column[:, None], before, 0), axis=0)
    my_counts = jnp.sum(jnp.where(own_column[:, None], count_table, 0), axis=0)
    owner_hits = tile_owner[:, :, None] == column_ids[None, None, :]
    base = jnp.sum(jnp.where(owner_hits, my_bases[None, None, :], 0), axis=2)
    quota = jnp.sum(jnp.where(owner_hits, my_counts[None, None, :], 0), axis=2)
    rank = tile_slot - base
    return (
        (tile_owner >= 0)
        & (rank >= 0)
        & (rank < capacity)
        & (rank < quota)
        & (tile_slot < LIVE_DEV)
    )


def mlp_forward_kernel(mixed_ref, image_ref, live_ref, w_in_ref, w_out_ref, summed_ref, low_ref):
    normed, _ = normalize(mixed_ref[...].astype(jnp.float32))
    hidden = jnp.dot(normed.astype(jnp.bfloat16), w_in_ref[...], preferred_element_type=jnp.float32)
    cdf = 0.5 * (1.0 + lax.erf(hidden * ROOT_HALF))
    activated = (hidden * cdf).astype(jnp.bfloat16)
    branch = jnp.dot(activated, w_out_ref[...], preferred_element_type=jnp.float32)
    branch = jnp.where(live_ref[...] > 0, branch.astype(jnp.bfloat16).astype(jnp.float32), 0.0)
    summed = (image_ref[...].astype(jnp.float32) + branch).astype(jnp.bfloat16)
    summed_ref[...] = summed
    down_normed, _ = normalize(summed.astype(jnp.float32))
    low_ref[...] = down_normed.astype(jnp.bfloat16)


def mlp_backward_kernel(
    mixed_ref, summed_ref, grad_ref, live_ref, w_in_ref, w_out_ref, grad_summed_ref, grad_mixed_ref
):
    normed, inv_std = normalize(mixed_ref[...].astype(jnp.float32))
    hidden = jnp.dot(normed.astype(jnp.bfloat16), w_in_ref[...], preferred_element_type=jnp.float32)
    cdf = 0.5 * (1.0 + lax.erf(hidden * ROOT_HALF))
    slope = cdf + hidden * INV_ROOT_TAU * jnp.exp(-0.5 * hidden * hidden)
    down_normed, down_inv = normalize(summed_ref[...].astype(jnp.float32))
    grad_summed = normalize_back(grad_ref[...], down_normed, down_inv).astype(jnp.bfloat16)
    grad_summed_ref[...] = grad_summed
    grad_hidden = (times_transposed(grad_summed, w_out_ref[...]) * slope).astype(jnp.bfloat16)
    grad_norm_in = times_transposed(grad_hidden, w_in_ref[...])
    grad_owned_mixed = normalize_back(grad_norm_in, normed, inv_std)
    grad_mixed_ref[...] = jnp.where(live_ref[...] > 0, grad_owned_mixed, 0.0).astype(jnp.bfloat16)


def pixel_call(kernel, operands, widths, outputs, block=256):
    pixels = operands[0].shape[0]
    specs = []
    for operand, blocked in zip(operands, widths):
        if blocked:
            specs.append(pl.BlockSpec((block, operand.shape[1]), lambda i: (i, 0)))
        else:
            specs.append(pl.BlockSpec(operand.shape, lambda i: (0, 0)))
    return pl.pallas_call(
        kernel,
        grid=(pixels // block,),
        in_specs=specs,
        out_specs=[pl.BlockSpec((block, width), lambda i: (i, 0)) for width, _ in outputs],
        out_shape=[jax.ShapeDtypeStruct((pixels, width), dtype) for width, dtype in outputs],
    )(*operands)


def on_device(
    image,
    depth_kernel,
    weight_in,
    weight_out,
    weight_down,
    tissue_mask,
    tile_counts,
    tile_owner,
    tile_slot,
    cotangent,
):
    height, breadth, channels = image.shape
    tile_rows, tile_cols = tissue_mask.shape
    tile_side = height // tile_rows
    outputs = weight_down.shape[3]
    reach = KS // 2
    peer_count = lax.axis_size("col")
    capacity = tile_rows * tile_cols // peer_count
    pixels = height * breadth
    routed = routed_tiles(tile_counts, tile_owner, tile_slot, peer_count, capacity)
    live = routed & (tissue_mask != 0)
    live_px = jnp.broadcast_to(
        live[:, None, :, None], (tile_rows, tile_side, tile_cols, tile_side)
    ).reshape(pixels, 1)
    padded = with_halo(image, (("row", 0), ("col", 1)), reach)
    mixed = depthwise(padded, depth_kernel, height, breadth)
    live_px = live_px.astype(jnp.float32)
    mixed = mixed.reshape(pixels, channels)
    summed, down_low = pixel_call(
        mlp_forward_kernel,
        (mixed, image.reshape(pixels, channels), live_px, weight_in, weight_out),
        (True, True, True, False, False),
        ((channels, jnp.bfloat16), (channels, jnp.bfloat16)),
    )
    down_low = down_low.reshape(height // 2, 2, breadth // 2, 2 * channels)
    weight_pair = weight_down.reshape(2, 2 * channels, outputs)
    reduced = jnp.dot(down_low[:, 0], weight_pair[0], preferred_element_type=jnp.float32) + jnp.dot(
        down_low[:, 1], weight_pair[1], preferred_element_type=jnp.float32
    )
    reduced = reduced.astype(jnp.bfloat16)
    grad_pair = [
        lax.dot_general(
            cotangent, weight_pair[a], (((2,), (1,)), ((), ())), preferred_element_type=jnp.float32
        )
        for a in range(2)
    ]
    grad_normed = jnp.stack(grad_pair, axis=1).reshape(pixels, channels)
    grad_summed, grad_mixed = pixel_call(
        mlp_backward_kernel,
        (mixed, summed, grad_normed, live_px, weight_in, weight_out),
        (True, True, True, True, False, False),
        ((channels, jnp.bfloat16), (channels, jnp.bfloat16)),
    )
    grad_padded = with_halo(grad_mixed.reshape(height, breadth, channels), (("row", 0), ("col", 1)), reach)
    grad_image = depthwise(
        grad_padded, depth_kernel[::-1, ::-1, :], height, breadth, base=grad_summed.reshape(height, breadth, channels)
    )
    return (reduced, grad_image)


def solution(mesh):
    in_specs = (
        P("row", "col", None),
        P(),
        P(),
        P(),
        P(),
        P("row", "col"),
        P("row", None, None),
        P("row", "col"),
        P("row", "col"),
        P("row", "col", None),
    )
    out_specs = (P("row", "col", None), P("row", "col", None))
    return jax.shard_map(
        on_device, mesh=mesh, in_specs=in_specs, out_specs=out_specs, check_vma=False
    )
```

```python
import jax
import jax.numpy as jnp
from jax import lax
from jax.sharding import PartitionSpec as P
from jax.experimental import pallas as pl
from jax.experimental.pallas import tpu as pltpu

KS = 7
LIVE_DEV = 18


EPSILON = 1e-06
ROOT_HALF = 0.7071067811865476
INV_ROOT_TAU = 0.3989422804014327


def halo_pieces(cells, width):
    rows = lax.axis_size("row")
    cols = lax.axis_size("col")
    down = [(i, i + 1) for i in range(rows - 1)]
    up = [(i + 1, i) for i in range(rows - 1)]
    top = lax.ppermute(cells[cells.shape[0] - width :], "row", down)
    bottom = lax.ppermute(cells[:width], "row", up)
    framed = jnp.concatenate([top, cells, bottom], axis=0)
    left = lax.ppermute(framed[:, cells.shape[1] - width :], "col", [(i, i + 1) for i in range(cols - 1)])
    right = lax.ppermute(framed[:, :width], "col", [(i + 1, i) for i in range(cols - 1)])
    return (cells, top, bottom, left, right)


def depthwise_kernel(
    image_ref, top_ref, bottom_ref, left_ref, right_ref, k_ref, *rest, reach, chunk, flip
):
    if len(rest) == 5:
        base_ref, out_ref, framed_ref, shifted_ref, total_ref = rest
    else:
        base_ref = None
        out_ref, framed_ref, shifted_ref, total_ref = rest
    height, breadth, _ = out_ref.shape
    side = 2 * reach + 1
    framed_ref[reach : reach + height, reach : reach + breadth, :] = image_ref[...].astype(jnp.float32)
    framed_ref[:reach, reach : reach + breadth, :] = top_ref[...].astype(jnp.float32)
    framed_ref[reach + height :, reach : reach + breadth, :] = bottom_ref[...].astype(jnp.float32)
    framed_ref[:, :reach, :] = left_ref[...].astype(jnp.float32)
    framed_ref[:, reach + breadth :, :] = right_ref[...].astype(jnp.float32)
    for shift_c in range(side):
        shifted_ref[...] = framed_ref[:, shift_c : shift_c + breadth, :]

        def body(step, carry, shift_c=shift_c):
            start = pl.multiple_of(step * chunk, chunk)
            if shift_c > 0:
                total = total_ref[pl.ds(start, chunk)]
            elif base_ref is not None:
                total = base_ref[pl.ds(start, chunk)].astype(jnp.float32)
            else:
                total = jnp.zeros((chunk, breadth, out_ref.shape[2]), jnp.float32)
            for shift_r in range(side):
                if flip:
                    index = (side - 1 - shift_r) * side + (side - 1 - shift_c)
                else:
                    index = shift_r * side + shift_c
                tap = k_ref[pl.ds(index, 1), :]
                total = total + shifted_ref[pl.ds(start + shift_r, chunk)] * tap[None]
            if shift_c == side - 1:
                out_ref[pl.ds(start, chunk)] = total.astype(out_ref.dtype)
            else:
                total_ref[pl.ds(start, chunk)] = total
            return carry

        lax.fori_loop(0, height // chunk, body, 0)


def depthwise(pieces, taps, reach, base=None, flip=False, lanes=128, chunk=8):
    image = pieces[0]
    height, breadth, channels = image.shape
    framed = (height + 2 * reach, breadth + 2 * reach)
    in_specs = [
        pl.BlockSpec((height, breadth, lanes), lambda c: (0, 0, c)),
        pl.BlockSpec((reach, breadth, lanes), lambda c: (0, 0, c)),
        pl.BlockSpec((reach, breadth, lanes), lambda c: (0, 0, c)),
        pl.BlockSpec((framed[0], reach, lanes), lambda c: (0, 0, c)),
        pl.BlockSpec((framed[0], reach, lanes), lambda c: (0, 0, c)),
        pl.BlockSpec((taps.shape[0], lanes), lambda c: (0, c)),
    ]
    operands = list(pieces) + [taps]
    if base is not None:
        in_specs.append(pl.BlockSpec((height, breadth, lanes), lambda c: (0, 0, c)))
        operands.append(base)
    return pl.pallas_call(
        lambda *refs: depthwise_kernel(*refs, reach=reach, chunk=chunk, flip=flip),
        grid=(channels // lanes,),
        in_specs=in_specs,
        out_specs=pl.BlockSpec((height, breadth, lanes), lambda c: (0, 0, c)),
        out_shape=jax.ShapeDtypeStruct((height, breadth, channels), jnp.bfloat16),
        scratch_shapes=[
            pltpu.VMEM((framed[0], framed[1], lanes), jnp.float32),
            pltpu.VMEM((framed[0], breadth, lanes), jnp.float32),
            pltpu.VMEM((height, breadth, lanes), jnp.float32),
        ],
    )(*operands)


def normalize(values):
    average = jnp.mean(values, axis=-1, keepdims=True)
    centered = values - average
    inv_std = lax.rsqrt(jnp.mean(centered * centered, axis=-1, keepdims=True) + EPSILON)
    return (centered * inv_std, inv_std)


def normalize_back(gradient, normed, inv_std):
    return inv_std * (
        gradient
        - jnp.mean(gradient, axis=-1, keepdims=True)
        - normed * jnp.mean(gradient * normed, axis=-1, keepdims=True)
    )


def times_transposed(left, right):
    return lax.dot_general(
        left, right, (((1,), (1,)), ((), ())), preferred_element_type=jnp.float32
    )


def routed_tiles(tile_counts, tile_owner, tile_slot, peer_count, capacity):
    count_table = tile_counts[0]
    before = jnp.cumsum(count_table, axis=0) - count_table
    column_ids = jnp.arange(peer_count, dtype=jnp.int32)
    own_column = column_ids == lax.axis_index("col")
    my_bases = jnp.sum(jnp.where(own_column[:, None], before, 0), axis=0)
    my_counts = jnp.sum(jnp.where(own_column[:, None], count_table, 0), axis=0)
    owner_hits = tile_owner[:, :, None] == column_ids[None, None, :]
    base = jnp.sum(jnp.where(owner_hits, my_bases[None, None, :], 0), axis=2)
    quota = jnp.sum(jnp.where(owner_hits, my_counts[None, None, :], 0), axis=2)
    rank = tile_slot - base
    return (
        (tile_owner >= 0)
        & (rank >= 0)
        & (rank < capacity)
        & (rank < quota)
        & (tile_slot < LIVE_DEV)
    )


def mlp_forward_kernel(live, mixed_ref, image_ref, w_in_ref, w_out_ref, summed_ref, low_ref, *, layout):
    normed, _ = normalize(mixed_ref[...].astype(jnp.float32))
    hidden = jnp.dot(normed.astype(jnp.bfloat16), w_in_ref[...], preferred_element_type=jnp.float32)
    cdf = 0.5 * (1.0 + lax.erf(hidden * ROOT_HALF))
    activated = (hidden * cdf).astype(jnp.bfloat16)
    branch = jnp.dot(activated, w_out_ref[...], preferred_element_type=jnp.float32)
    branch = jnp.where(pixel_live(live, layout), branch.astype(jnp.bfloat16).astype(jnp.float32), 0.0)
    summed = (image_ref[...].astype(jnp.float32) + branch).astype(jnp.bfloat16)
    summed_ref[...] = summed
    down_normed, _ = normalize(summed.astype(jnp.float32))
    low_ref[...] = down_normed.astype(jnp.bfloat16)


def mlp_backward_kernel(
    live, mixed_ref, summed_ref, grad_ref, w_in_ref, w_out_ref, grad_summed_ref, grad_mixed_ref, *, layout
):
    normed, inv_std = normalize(mixed_ref[...].astype(jnp.float32))
    hidden = jnp.dot(normed.astype(jnp.bfloat16), w_in_ref[...], preferred_element_type=jnp.float32)
    cdf = 0.5 * (1.0 + lax.erf(hidden * ROOT_HALF))
    slope = cdf + hidden * INV_ROOT_TAU * jnp.exp(-0.5 * hidden * hidden)
    down_normed, down_inv = normalize(summed_ref[...].astype(jnp.float32))
    grad_summed = normalize_back(grad_ref[...], down_normed, down_inv).astype(jnp.bfloat16)
    grad_summed_ref[...] = grad_summed
    grad_hidden = (times_transposed(grad_summed, w_out_ref[...]) * slope).astype(jnp.bfloat16)
    grad_norm_in = times_transposed(grad_hidden, w_in_ref[...])
    grad_owned_mixed = normalize_back(grad_norm_in, normed, inv_std)
    grad_mixed_ref[...] = jnp.where(pixel_live(live, layout), grad_owned_mixed, 0.0).astype(jnp.bfloat16)


def pixel_live(live, layout):
    block, breadth, tile_side, tile_cols = layout
    place = lax.broadcasted_iota(jnp.int32, (block, 1), 0)
    tile = (place % breadth) // tile_side
    first = pl.program_id(0) * tile_cols
    flag = jnp.zeros((block, 1), jnp.int32)
    for column in range(tile_cols):
        flag = jnp.where(tile == column, live[first + column], flag)
    return flag > 0


def pixel_call(kernel, live, operands, widths, outputs, layout):
    block = layout[0]
    pixels = operands[0].shape[0]
    specs = []
    for operand, blocked in zip(operands, widths):
        if blocked:
            specs.append(pl.BlockSpec((block, operand.shape[1]), lambda i, live: (i, 0)))
        else:
            specs.append(pl.BlockSpec(operand.shape, lambda i, live: (0, 0)))
    return pl.pallas_call(
        lambda *refs: kernel(*refs, layout=layout),
        grid_spec=pltpu.PrefetchScalarGridSpec(
            num_scalar_prefetch=1,
            grid=(pixels // block,),
            in_specs=specs,
            out_specs=[pl.BlockSpec((block, width), lambda i, live: (i, 0)) for width, _ in outputs],
        ),
        out_shape=[jax.ShapeDtypeStruct((pixels, width), dtype) for width, dtype in outputs],
    )(live, *operands)


def on_device(
    image,
    depth_kernel,
    weight_in,
    weight_out,
    weight_down,
    tissue_mask,
    tile_counts,
    tile_owner,
    tile_slot,
    cotangent,
):
    height, breadth, channels = image.shape
    tile_rows, tile_cols = tissue_mask.shape
    tile_side = height // tile_rows
    outputs = weight_down.shape[3]
    reach = KS // 2
    peer_count = lax.axis_size("col")
    capacity = tile_rows * tile_cols // peer_count
    pixels = height * breadth
    routed = routed_tiles(tile_counts, tile_owner, tile_slot, peer_count, capacity)
    live = routed & (tissue_mask != 0)
    live = live.reshape(-1).astype(jnp.int32)
    layout = (tile_side * breadth, breadth, tile_side, tile_cols)
    taps = depth_kernel.reshape(KS * KS, channels).astype(jnp.float32)
    mixed = depthwise(halo_pieces(image, reach), taps, reach)
    mixed = mixed.reshape(pixels, channels)
    summed, down_low = pixel_call(
        mlp_forward_kernel,
        live,
        (mixed, image.reshape(pixels, channels), weight_in, weight_out),
        (True, True, False, False),
        ((channels, jnp.bfloat16), (channels, jnp.bfloat16)),
        layout,
    )
    down_low = down_low.reshape(height // 2, 2, breadth // 2, 2 * channels)
    weight_pair = weight_down.reshape(2, 2 * channels, outputs)
    reduced = jnp.dot(down_low[:, 0], weight_pair[0], preferred_element_type=jnp.float32) + jnp.dot(
        down_low[:, 1], weight_pair[1], preferred_element_type=jnp.float32
    )
    reduced = reduced.astype(jnp.bfloat16)
    grad_pair = [
        lax.dot_general(
            cotangent, weight_pair[a], (((2,), (1,)), ((), ())), preferred_element_type=jnp.float32
        )
        for a in range(2)
    ]
    grad_normed = jnp.stack(grad_pair, axis=1).reshape(pixels, channels)
    grad_summed, grad_mixed = pixel_call(
        mlp_backward_kernel,
        live,
        (mixed, summed, grad_normed, weight_in, weight_out),
        (True, True, True, False, False),
        ((channels, jnp.bfloat16), (channels, jnp.bfloat16)),
        layout,
    )
    grad_image = depthwise(
        halo_pieces(grad_mixed.reshape(height, breadth, channels), reach),
        taps,
        reach,
        base=grad_summed.reshape(height, breadth, channels),
        flip=True,
    )
    return (reduced, grad_image)


def solution(mesh):
    in_specs = (
        P("row", "col", None),
        P(),
        P(),
        P(),
        P(),
        P("row", "col"),
        P("row", None, None),
        P("row", "col"),
        P("row", "col"),
        P("row", "col", None),
    )
    out_specs = (P("row", "col", None), P("row", "col", None))
    return jax.shard_map(
        on_device, mesh=mesh, in_specs=in_specs, out_specs=out_specs, check_vma=False
    )
```

```python
import jax
import jax.numpy as jnp
from jax import lax
from jax.sharding import PartitionSpec as P
from jax.experimental import pallas as pl
from jax.experimental.pallas import tpu as pltpu

KS = 7
LIVE_DEV = 18


EPSILON = 1e-06
ROOT_HALF = 0.7071067811865476
INV_ROOT_TAU = 0.3989422804014327


def halo_pieces(cells, width):
    rows = lax.axis_size("row")
    cols = lax.axis_size("col")
    down = [(i, i + 1) for i in range(rows - 1)]
    up = [(i + 1, i) for i in range(rows - 1)]
    top = lax.ppermute(cells[cells.shape[0] - width :], "row", down)
    bottom = lax.ppermute(cells[:width], "row", up)
    framed = jnp.concatenate([top, cells, bottom], axis=0)
    left = lax.ppermute(framed[:, cells.shape[1] - width :], "col", [(i, i + 1) for i in range(cols - 1)])
    right = lax.ppermute(framed[:, :width], "col", [(i + 1, i) for i in range(cols - 1)])
    return (cells, top, bottom, left, right)


def depthwise_kernel(
    image_ref, top_ref, bottom_ref, left_ref, right_ref, k_ref, *rest, reach, chunk, flip
):
    if len(rest) == 5:
        base_ref, out_ref, framed_ref, shifted_ref, total_ref = rest
    else:
        base_ref = None
        out_ref, framed_ref, shifted_ref, total_ref = rest
    height, breadth, _ = out_ref.shape
    side = 2 * reach + 1
    framed_ref[reach : reach + height, reach : reach + breadth, :] = image_ref[...].astype(jnp.float32)
    framed_ref[:reach, reach : reach + breadth, :] = top_ref[...].astype(jnp.float32)
    framed_ref[reach + height :, reach : reach + breadth, :] = bottom_ref[...].astype(jnp.float32)
    framed_ref[:, :reach, :] = left_ref[...].astype(jnp.float32)
    framed_ref[:, reach + breadth :, :] = right_ref[...].astype(jnp.float32)
    for shift_c in range(side):
        shifted_ref[...] = framed_ref[:, shift_c : shift_c + breadth, :]

        def body(step, carry, shift_c=shift_c):
            start = pl.multiple_of(step * chunk, chunk)
            if shift_c > 0:
                total = total_ref[pl.ds(start, chunk)]
            elif base_ref is not None:
                total = base_ref[pl.ds(start, chunk)].astype(jnp.float32)
            else:
                total = jnp.zeros((chunk, breadth, out_ref.shape[2]), jnp.float32)
            for shift_r in range(side):
                if flip:
                    index = (side - 1 - shift_r) * side + (side - 1 - shift_c)
                else:
                    index = shift_r * side + shift_c
                tap = k_ref[pl.ds(index, 1), :]
                total = total + shifted_ref[pl.ds(start + shift_r, chunk)] * tap[None]
            if shift_c == side - 1:
                out_ref[pl.ds(start, chunk)] = total.astype(out_ref.dtype)
            else:
                total_ref[pl.ds(start, chunk)] = total
            return carry

        lax.fori_loop(0, height // chunk, body, 0)


def depthwise(pieces, taps, reach, base=None, flip=False, lanes=128, chunk=8):
    image = pieces[0]
    height, breadth, channels = image.shape
    framed = (height + 2 * reach, breadth + 2 * reach)
    in_specs = [
        pl.BlockSpec((height, breadth, lanes), lambda c: (0, 0, c)),
        pl.BlockSpec((reach, breadth, lanes), lambda c: (0, 0, c)),
        pl.BlockSpec((reach, breadth, lanes), lambda c: (0, 0, c)),
        pl.BlockSpec((framed[0], reach, lanes), lambda c: (0, 0, c)),
        pl.BlockSpec((framed[0], reach, lanes), lambda c: (0, 0, c)),
        pl.BlockSpec((taps.shape[0], lanes), lambda c: (0, c)),
    ]
    operands = list(pieces) + [taps]
    if base is not None:
        in_specs.append(pl.BlockSpec((height, breadth, lanes), lambda c: (0, 0, c)))
        operands.append(base)
    return pl.pallas_call(
        lambda *refs: depthwise_kernel(*refs, reach=reach, chunk=chunk, flip=flip),
        grid=(channels // lanes,),
        in_specs=in_specs,
        out_specs=pl.BlockSpec((height, breadth, lanes), lambda c: (0, 0, c)),
        out_shape=jax.ShapeDtypeStruct((height, breadth, channels), jnp.bfloat16),
        scratch_shapes=[
            pltpu.VMEM((framed[0], framed[1], lanes), jnp.float32),
            pltpu.VMEM((framed[0], breadth, lanes), jnp.float32),
            pltpu.VMEM((height, breadth, lanes), jnp.float32),
        ],
    )(*operands)


def normalize(values):
    average = jnp.mean(values, axis=-1, keepdims=True)
    centered = values - average
    inv_std = lax.rsqrt(jnp.mean(centered * centered, axis=-1, keepdims=True) + EPSILON)
    return (centered * inv_std, inv_std)


def normalize_back(gradient, normed, inv_std):
    return inv_std * (
        gradient
        - jnp.mean(gradient, axis=-1, keepdims=True)
        - normed * jnp.mean(gradient * normed, axis=-1, keepdims=True)
    )


def times_transposed(left, right):
    return lax.dot_general(
        left, right, (((1,), (1,)), ((), ())), preferred_element_type=jnp.float32
    )


def routed_tiles(tile_counts, tile_owner, tile_slot, peer_count, capacity):
    count_table = tile_counts[0]
    before = jnp.cumsum(count_table, axis=0) - count_table
    column_ids = jnp.arange(peer_count, dtype=jnp.int32)
    own_column = column_ids == lax.axis_index("col")
    my_bases = jnp.sum(jnp.where(own_column[:, None], before, 0), axis=0)
    my_counts = jnp.sum(jnp.where(own_column[:, None], count_table, 0), axis=0)
    owner_hits = tile_owner[:, :, None] == column_ids[None, None, :]
    base = jnp.sum(jnp.where(owner_hits, my_bases[None, None, :], 0), axis=2)
    quota = jnp.sum(jnp.where(owner_hits, my_counts[None, None, :], 0), axis=2)
    rank = tile_slot - base
    return (
        (tile_owner >= 0)
        & (rank >= 0)
        & (rank < capacity)
        & (rank < quota)
        & (tile_slot < LIVE_DEV)
    )


def patch_rows(row, column, breadth):
    return pl.ds(row * breadth + column, breadth // 2, stride=2)


def mlp_forward_kernel(
    live, mixed_ref, image_ref, w_in_ref, w_out_ref, w_down_ref, summed_ref, reduced_ref, low_ref,
    *, layout
):
    normed, _ = normalize(mixed_ref[...].astype(jnp.float32))
    hidden = jnp.dot(normed.astype(jnp.bfloat16), w_in_ref[...], preferred_element_type=jnp.float32)
    cdf = 0.5 * (1.0 + lax.erf(hidden * ROOT_HALF))
    activated = (hidden * cdf).astype(jnp.bfloat16)
    branch = jnp.dot(activated, w_out_ref[...], preferred_element_type=jnp.float32)
    branch = jnp.where(pixel_live(live, layout), branch.astype(jnp.bfloat16).astype(jnp.float32), 0.0)
    summed = (image_ref[...].astype(jnp.float32) + branch).astype(jnp.bfloat16)
    summed_ref[...] = summed
    down_normed, _ = normalize(summed.astype(jnp.float32))
    low = down_normed.astype(jnp.bfloat16).astype(jnp.float32)
    for k in range(low_ref.shape[0]):
        low_ref[k] = low[:, k * 128 : (k + 1) * 128]
    breadth = layout[1]
    pair_rows = layout[0] // breadth // 2
    total = jnp.zeros(reduced_ref.shape, jnp.float32)
    for a in range(2):
        for e in range(2):
            patch = jnp.concatenate(
                [
                    jnp.concatenate(
                        [low_ref[k, patch_rows(2 * y + a, e, breadth), :] for k in range(low_ref.shape[0])],
                        axis=1,
                    )
                    for y in range(pair_rows)
                ],
                axis=0,
            )
            total = total + jnp.dot(
                patch.astype(jnp.bfloat16), w_down_ref[2 * a + e], preferred_element_type=jnp.float32
            )
    reduced_ref[...] = total.astype(jnp.bfloat16)


def mlp_backward_kernel(
    live, mixed_ref, summed_ref, cot_ref, w_in_ref, w_out_ref, w_down_ref, grad_summed_ref,
    grad_mixed_ref, grad_ref, *, layout
):
    breadth = layout[1]
    pair_rows = layout[0] // breadth // 2
    half = breadth // 2
    for a in range(2):
        for e in range(2):
            part = times_transposed(cot_ref[...], w_down_ref[2 * a + e])
            for y in range(pair_rows):
                for k in range(grad_ref.shape[0]):
                    grad_ref[k, patch_rows(2 * y + a, e, breadth), :] = part[
                        y * half : (y + 1) * half, k * 128 : (k + 1) * 128
                    ]
    normed, inv_std = normalize(mixed_ref[...].astype(jnp.float32))
    hidden = jnp.dot(normed.astype(jnp.bfloat16), w_in_ref[...], preferred_element_type=jnp.float32)
    cdf = 0.5 * (1.0 + lax.erf(hidden * ROOT_HALF))
    slope = cdf + hidden * INV_ROOT_TAU * jnp.exp(-0.5 * hidden * hidden)
    down_normed, down_inv = normalize(summed_ref[...].astype(jnp.float32))
    grad_normed = jnp.concatenate([grad_ref[k] for k in range(grad_ref.shape[0])], axis=1)
    grad_summed = normalize_back(grad_normed, down_normed, down_inv).astype(jnp.bfloat16)
    grad_summed_ref[...] = grad_summed
    grad_hidden = (times_transposed(grad_summed, w_out_ref[...]) * slope).astype(jnp.bfloat16)
    grad_norm_in = times_transposed(grad_hidden, w_in_ref[...])
    grad_owned_mixed = normalize_back(grad_norm_in, normed, inv_std)
    grad_mixed_ref[...] = jnp.where(pixel_live(live, layout), grad_owned_mixed, 0.0).astype(jnp.bfloat16)


def pixel_live(live, layout):
    block, breadth, tile_side, tile_cols = layout
    place = lax.broadcasted_iota(jnp.int32, (block, 1), 0)
    tile = (place % breadth) // tile_side
    first = pl.program_id(0) * tile_cols
    flag = jnp.zeros((block, 1), jnp.int32)
    for column in range(tile_cols):
        flag = jnp.where(tile == column, live[first + column], flag)
    return flag > 0


def pixel_call(kernel, live, operands, kinds, outputs, layout, scratch):
    block = layout[0]
    steps = operands[0].shape[0] // block
    specs = []
    for operand, kind in zip(operands, kinds):
        if kind == "whole":
            specs.append(pl.BlockSpec(operand.shape, lambda i, live, n=operand.ndim: (0,) * n))
        else:
            rows = operand.shape[0] // steps
            specs.append(pl.BlockSpec((rows, operand.shape[1]), lambda i, live: (i, 0)))
    return pl.pallas_call(
        lambda *refs: kernel(*refs, layout=layout),
        grid_spec=pltpu.PrefetchScalarGridSpec(
            num_scalar_prefetch=1,
            grid=(steps,),
            in_specs=specs,
            out_specs=[
                pl.BlockSpec((rows // steps, width), lambda i, live: (i, 0)) for rows, width, _ in outputs
            ],
            scratch_shapes=[pltpu.VMEM((width // 128, block, 128), jnp.float32) for width in scratch],
        ),
        out_shape=[jax.ShapeDtypeStruct((rows, width), dtype) for rows, width, dtype in outputs],
    )(live, *operands)


def on_device(
    image,
    depth_kernel,
    weight_in,
    weight_out,
    weight_down,
    tissue_mask,
    tile_counts,
    tile_owner,
    tile_slot,
    cotangent,
):
    height, breadth, channels = image.shape
    tile_rows, tile_cols = tissue_mask.shape
    tile_side = height // tile_rows
    outputs = weight_down.shape[3]
    reach = KS // 2
    peer_count = lax.axis_size("col")
    capacity = tile_rows * tile_cols // peer_count
    pixels = height * breadth
    routed = routed_tiles(tile_counts, tile_owner, tile_slot, peer_count, capacity)
    live = routed & (tissue_mask != 0)
    live = live.reshape(-1).astype(jnp.int32)
    layout = (tile_side * breadth, breadth, tile_side, tile_cols)
    taps = depth_kernel.reshape(KS * KS, channels).astype(jnp.float32)
    mixed = depthwise(halo_pieces(image, reach), taps, reach)
    mixed = mixed.reshape(pixels, channels)
    weight_quad = weight_down.reshape(4, channels, outputs)
    patches = pixels // 4
    summed, reduced = pixel_call(
        mlp_forward_kernel,
        live,
        (mixed, image.reshape(pixels, channels), weight_in, weight_out, weight_quad),
        ("rows", "rows", "whole", "whole", "whole"),
        ((pixels, channels, jnp.bfloat16), (patches, outputs, jnp.bfloat16)),
        layout,
        (channels,),
    )
    reduced = reduced.reshape(height // 2, breadth // 2, outputs)
    grad_summed, grad_mixed = pixel_call(
        mlp_backward_kernel,
        live,
        (mixed, summed, cotangent.reshape(patches, outputs), weight_in, weight_out, weight_quad),
        ("rows", "rows", "rows", "whole", "whole", "whole"),
        ((pixels, channels, jnp.bfloat16), (pixels, channels, jnp.bfloat16)),
        layout,
        (channels,),
    )
    grad_image = depthwise(
        halo_pieces(grad_mixed.reshape(height, breadth, channels), reach),
        taps,
        reach,
        base=grad_summed.reshape(height, breadth, channels),
        flip=True,
    )
    return (reduced, grad_image)


def solution(mesh):
    in_specs = (
        P("row", "col", None),
        P(),
        P(),
        P(),
        P(),
        P("row", "col"),
        P("row", None, None),
        P("row", "col"),
        P("row", "col"),
        P("row", "col", None),
    )
    out_specs = (P("row", "col", None), P("row", "col", None))
    return jax.shard_map(
        on_device, mesh=mesh, in_specs=in_specs, out_specs=out_specs, check_vma=False
    )
```

```python
import jax
import jax.numpy as jnp
from jax import lax
from jax.sharding import PartitionSpec as P
from jax.experimental import pallas as pl
from jax.experimental.pallas import tpu as pltpu

KS = 7
LIVE_DEV = 18


EPSILON = 1e-06
ROOT_HALF = 0.7071067811865476
INV_ROOT_TAU = 0.3989422804014327


def halo_pieces(cells, width):
    rows = lax.axis_size("row")
    cols = lax.axis_size("col")
    height, breadth = cells.shape[:2]

    def arrive(piece, down, right):
        pairs = [
            ((r - down) * cols + (c - right), r * cols + c)
            for r in range(rows)
            for c in range(cols)
            if 0 <= r - down < rows and 0 <= c - right < cols
        ]
        if right == 0:
            return lax.ppermute(piece, "row", [(src // cols, dst // cols) for src, dst in pairs if src % cols == 0])
        if down == 0:
            return lax.ppermute(piece, "col", [(src, dst) for src, dst in pairs if src < cols])
        return lax.ppermute(piece, ("row", "col"), pairs)

    low = slice(0, width)
    high_r = slice(height - width, height)
    high_c = slice(breadth - width, breadth)
    return (
        cells,
        arrive(cells[high_r], 1, 0),
        arrive(cells[low], -1, 0),
        arrive(cells[:, high_c], 0, 1),
        arrive(cells[:, low], 0, -1),
        arrive(cells[high_r, high_c], 1, 1),
        arrive(cells[high_r, low], 1, -1),
        arrive(cells[low, high_c], -1, 1),
        arrive(cells[low, low], -1, -1),
    )


def depthwise_kernel(
    image_ref, top_ref, bottom_ref, left_ref, right_ref, tl_ref, tr_ref, bl_ref, br_ref, k_ref, *rest,
    reach, chunk, flip
):
    if len(rest) == 5:
        base_ref, out_ref, framed_ref, shifted_ref, total_ref = rest
    else:
        base_ref = None
        out_ref, framed_ref, shifted_ref, total_ref = rest
    height, breadth, _ = out_ref.shape
    side = 2 * reach + 1
    framed_ref[reach : reach + height, reach : reach + breadth, :] = image_ref[...].astype(jnp.float32)
    framed_ref[:reach, reach : reach + breadth, :] = top_ref[...].astype(jnp.float32)
    framed_ref[reach + height :, reach : reach + breadth, :] = bottom_ref[...].astype(jnp.float32)
    framed_ref[reach : reach + height, :reach, :] = left_ref[...].astype(jnp.float32)
    framed_ref[reach : reach + height, reach + breadth :, :] = right_ref[...].astype(jnp.float32)
    framed_ref[:reach, :reach, :] = tl_ref[...].astype(jnp.float32)
    framed_ref[:reach, reach + breadth :, :] = tr_ref[...].astype(jnp.float32)
    framed_ref[reach + height :, :reach, :] = bl_ref[...].astype(jnp.float32)
    framed_ref[reach + height :, reach + breadth :, :] = br_ref[...].astype(jnp.float32)
    for shift_c in range(side):
        shifted_ref[...] = framed_ref[:, shift_c : shift_c + breadth, :]

        def body(step, carry, shift_c=shift_c):
            start = pl.multiple_of(step * chunk, chunk)
            if shift_c > 0:
                total = total_ref[pl.ds(start, chunk)]
            elif base_ref is not None:
                total = base_ref[pl.ds(start, chunk)].astype(jnp.float32)
            else:
                total = jnp.zeros((chunk, breadth, out_ref.shape[2]), jnp.float32)
            for shift_r in range(side):
                if flip:
                    index = (side - 1 - shift_r) * side + (side - 1 - shift_c)
                else:
                    index = shift_r * side + shift_c
                tap = k_ref[pl.ds(index, 1), :]
                total = total + shifted_ref[pl.ds(start + shift_r, chunk)] * tap[None]
            if shift_c == side - 1:
                out_ref[pl.ds(start, chunk)] = total.astype(out_ref.dtype)
            else:
                total_ref[pl.ds(start, chunk)] = total
            return carry

        lax.fori_loop(0, height // chunk, body, 0)


def depthwise(pieces, taps, reach, base=None, flip=False, lanes=128, chunk=8):
    image = pieces[0]
    height, breadth, channels = image.shape
    framed = (height + 2 * reach, breadth + 2 * reach)
    in_specs = [
        pl.BlockSpec((height, breadth, lanes), lambda c: (0, 0, c)),
        pl.BlockSpec((reach, breadth, lanes), lambda c: (0, 0, c)),
        pl.BlockSpec((reach, breadth, lanes), lambda c: (0, 0, c)),
        pl.BlockSpec((height, reach, lanes), lambda c: (0, 0, c)),
        pl.BlockSpec((height, reach, lanes), lambda c: (0, 0, c)),
    ] + [pl.BlockSpec((reach, reach, lanes), lambda c: (0, 0, c))] * 4 + [
        pl.BlockSpec((taps.shape[0], lanes), lambda c: (0, c)),
    ]
    operands = list(pieces) + [taps]
    if base is not None:
        in_specs.append(pl.BlockSpec((height, breadth, lanes), lambda c: (0, 0, c)))
        operands.append(base)
    return pl.pallas_call(
        lambda *refs: depthwise_kernel(*refs, reach=reach, chunk=chunk, flip=flip),
        grid=(channels // lanes,),
        in_specs=in_specs,
        out_specs=pl.BlockSpec((height, breadth, lanes), lambda c: (0, 0, c)),
        out_shape=jax.ShapeDtypeStruct((height, breadth, channels), jnp.bfloat16),
        scratch_shapes=[
            pltpu.VMEM((framed[0], framed[1], lanes), jnp.float32),
            pltpu.VMEM((framed[0], breadth, lanes), jnp.float32),
            pltpu.VMEM((height, breadth, lanes), jnp.float32),
        ],
    )(*operands)


def normalize(values):
    average = jnp.mean(values, axis=-1, keepdims=True)
    centered = values - average
    inv_std = lax.rsqrt(jnp.mean(centered * centered, axis=-1, keepdims=True) + EPSILON)
    return (centered * inv_std, inv_std)


def normalize_back(gradient, normed, inv_std):
    return inv_std * (
        gradient
        - jnp.mean(gradient, axis=-1, keepdims=True)
        - normed * jnp.mean(gradient * normed, axis=-1, keepdims=True)
    )


def times_transposed(left, right):
    return lax.dot_general(
        left, right, (((1,), (1,)), ((), ())), preferred_element_type=jnp.float32
    )


def routed_tiles(tile_counts, tile_owner, tile_slot, peer_count, capacity):
    count_table = tile_counts[0]
    before = jnp.cumsum(count_table, axis=0) - count_table
    column_ids = jnp.arange(peer_count, dtype=jnp.int32)
    own_column = column_ids == lax.axis_index("col")
    my_bases = jnp.sum(jnp.where(own_column[:, None], before, 0), axis=0)
    my_counts = jnp.sum(jnp.where(own_column[:, None], count_table, 0), axis=0)
    owner_hits = tile_owner[:, :, None] == column_ids[None, None, :]
    base = jnp.sum(jnp.where(owner_hits, my_bases[None, None, :], 0), axis=2)
    quota = jnp.sum(jnp.where(owner_hits, my_counts[None, None, :], 0), axis=2)
    rank = tile_slot - base
    return (
        (tile_owner >= 0)
        & (rank >= 0)
        & (rank < capacity)
        & (rank < quota)
        & (tile_slot < LIVE_DEV)
    )


def patch_rows(row, column, breadth):
    return pl.ds(row * breadth + column, breadth // 2, stride=2)


def mlp_forward_kernel(
    live, mixed_ref, image_ref, w_in_ref, w_out_ref, w_down_ref, summed_ref, reduced_ref, low_ref,
    *, layout
):
    normed, _ = normalize(mixed_ref[...].astype(jnp.float32))
    hidden = jnp.dot(normed.astype(jnp.bfloat16), w_in_ref[...], preferred_element_type=jnp.float32)
    cdf = 0.5 * (1.0 + lax.erf(hidden * ROOT_HALF))
    activated = (hidden * cdf).astype(jnp.bfloat16)
    branch = jnp.dot(activated, w_out_ref[...], preferred_element_type=jnp.float32)
    branch = jnp.where(pixel_live(live, layout), branch.astype(jnp.bfloat16).astype(jnp.float32), 0.0)
    summed = (image_ref[...].astype(jnp.float32) + branch).astype(jnp.bfloat16)
    summed_ref[...] = summed
    down_normed, _ = normalize(summed.astype(jnp.float32))
    low = down_normed.astype(jnp.bfloat16).astype(jnp.float32)
    for k in range(low_ref.shape[0]):
        low_ref[k] = low[:, k * 128 : (k + 1) * 128]
    breadth = layout[1]
    pair_rows = layout[0] // breadth // 2
    total = jnp.zeros(reduced_ref.shape, jnp.float32)
    for a in range(2):
        for e in range(2):
            patch = jnp.concatenate(
                [
                    jnp.concatenate(
                        [low_ref[k, patch_rows(2 * y + a, e, breadth), :] for k in range(low_ref.shape[0])],
                        axis=1,
                    )
                    for y in range(pair_rows)
                ],
                axis=0,
            )
            total = total + jnp.dot(
                patch.astype(jnp.bfloat16), w_down_ref[2 * a + e], preferred_element_type=jnp.float32
            )
    reduced_ref[...] = total.astype(jnp.bfloat16)


def mlp_backward_kernel(
    live, mixed_ref, summed_ref, cot_ref, w_in_ref, w_out_ref, w_down_ref, grad_summed_ref,
    grad_mixed_ref, grad_ref, *, layout
):
    breadth = layout[1]
    pair_rows = layout[0] // breadth // 2
    half = breadth // 2
    for a in range(2):
        for e in range(2):
            part = times_transposed(cot_ref[...], w_down_ref[2 * a + e])
            for y in range(pair_rows):
                for k in range(grad_ref.shape[0]):
                    grad_ref[k, patch_rows(2 * y + a, e, breadth), :] = part[
                        y * half : (y + 1) * half, k * 128 : (k + 1) * 128
                    ]
    normed, inv_std = normalize(mixed_ref[...].astype(jnp.float32))
    hidden = jnp.dot(normed.astype(jnp.bfloat16), w_in_ref[...], preferred_element_type=jnp.float32)
    cdf = 0.5 * (1.0 + lax.erf(hidden * ROOT_HALF))
    slope = cdf + hidden * INV_ROOT_TAU * jnp.exp(-0.5 * hidden * hidden)
    down_normed, down_inv = normalize(summed_ref[...].astype(jnp.float32))
    grad_normed = jnp.concatenate([grad_ref[k] for k in range(grad_ref.shape[0])], axis=1)
    grad_summed = normalize_back(grad_normed, down_normed, down_inv).astype(jnp.bfloat16)
    grad_summed_ref[...] = grad_summed
    grad_hidden = (times_transposed(grad_summed, w_out_ref[...]) * slope).astype(jnp.bfloat16)
    grad_norm_in = times_transposed(grad_hidden, w_in_ref[...])
    grad_owned_mixed = normalize_back(grad_norm_in, normed, inv_std)
    grad_mixed_ref[...] = jnp.where(pixel_live(live, layout), grad_owned_mixed, 0.0).astype(jnp.bfloat16)


def pixel_live(live, layout):
    block, breadth, tile_side, tile_cols = layout
    place = lax.broadcasted_iota(jnp.int32, (block, 1), 0)
    tile = (place % breadth) // tile_side
    first = pl.program_id(0) * tile_cols
    flag = jnp.zeros((block, 1), jnp.int32)
    for column in range(tile_cols):
        flag = jnp.where(tile == column, live[first + column], flag)
    return flag > 0


def pixel_call(kernel, live, operands, kinds, outputs, layout, scratch):
    block = layout[0]
    steps = operands[0].shape[0] // block
    specs = []
    for operand, kind in zip(operands, kinds):
        if kind == "whole":
            specs.append(pl.BlockSpec(operand.shape, lambda i, live, n=operand.ndim: (0,) * n))
        else:
            rows = operand.shape[0] // steps
            specs.append(pl.BlockSpec((rows, operand.shape[1]), lambda i, live: (i, 0)))
    return pl.pallas_call(
        lambda *refs: kernel(*refs, layout=layout),
        grid_spec=pltpu.PrefetchScalarGridSpec(
            num_scalar_prefetch=1,
            grid=(steps,),
            in_specs=specs,
            out_specs=[
                pl.BlockSpec((rows // steps, width), lambda i, live: (i, 0)) for rows, width, _ in outputs
            ],
            scratch_shapes=[pltpu.VMEM((width // 128, block, 128), jnp.float32) for width in scratch],
        ),
        out_shape=[jax.ShapeDtypeStruct((rows, width), dtype) for rows, width, dtype in outputs],
    )(live, *operands)


def on_device(
    image,
    depth_kernel,
    weight_in,
    weight_out,
    weight_down,
    tissue_mask,
    tile_counts,
    tile_owner,
    tile_slot,
    cotangent,
):
    height, breadth, channels = image.shape
    tile_rows, tile_cols = tissue_mask.shape
    tile_side = height // tile_rows
    outputs = weight_down.shape[3]
    reach = KS // 2
    peer_count = lax.axis_size("col")
    capacity = tile_rows * tile_cols // peer_count
    pixels = height * breadth
    routed = routed_tiles(tile_counts, tile_owner, tile_slot, peer_count, capacity)
    live = routed & (tissue_mask != 0)
    live = live.reshape(-1).astype(jnp.int32)
    layout = (tile_side * breadth, breadth, tile_side, tile_cols)
    taps = depth_kernel.reshape(KS * KS, channels).astype(jnp.float32)
    mixed = depthwise(halo_pieces(image, reach), taps, reach)
    mixed = mixed.reshape(pixels, channels)
    weight_quad = weight_down.reshape(4, channels, outputs)
    patches = pixels // 4
    summed, reduced = pixel_call(
        mlp_forward_kernel,
        live,
        (mixed, image.reshape(pixels, channels), weight_in, weight_out, weight_quad),
        ("rows", "rows", "whole", "whole", "whole"),
        ((pixels, channels, jnp.bfloat16), (patches, outputs, jnp.bfloat16)),
        layout,
        (channels,),
    )
    reduced = reduced.reshape(height // 2, breadth // 2, outputs)
    grad_summed, grad_mixed = pixel_call(
        mlp_backward_kernel,
        live,
        (mixed, summed, cotangent.reshape(patches, outputs), weight_in, weight_out, weight_quad),
        ("rows", "rows", "rows", "whole", "whole", "whole"),
        ((pixels, channels, jnp.bfloat16), (pixels, channels, jnp.bfloat16)),
        layout,
        (channels,),
    )
    grad_image = depthwise(
        halo_pieces(grad_mixed.reshape(height, breadth, channels), reach),
        taps,
        reach,
        base=grad_summed.reshape(height, breadth, channels),
        flip=True,
    )
    return (reduced, grad_image)


def solution(mesh):
    in_specs = (
        P("row", "col", None),
        P(),
        P(),
        P(),
        P(),
        P("row", "col"),
        P("row", None, None),
        P("row", "col"),
        P("row", "col"),
        P("row", "col", None),
    )
    out_specs = (P("row", "col", None), P("row", "col", None))
    return jax.shard_map(
        on_device, mesh=mesh, in_specs=in_specs, out_specs=out_specs, check_vma=False
    )
```

```python
import jax
import jax.numpy as jnp
from jax import lax
from jax.sharding import PartitionSpec as P
from jax.experimental import pallas as pl
from jax.experimental.pallas import tpu as pltpu

KS = 7
LIVE_DEV = 18


EPSILON = 1e-06
ROOT_HALF = 0.7071067811865476
INV_ROOT_TAU = 0.3989422804014327


def halo_pieces(cells, width):
    rows = lax.axis_size("row")
    cols = lax.axis_size("col")
    down = [(i, i + 1) for i in range(rows - 1)]
    up = [(i + 1, i) for i in range(rows - 1)]
    rightward = [(i, i + 1) for i in range(cols - 1)]
    leftward = [(i + 1, i) for i in range(cols - 1)]
    top = lax.ppermute(cells[cells.shape[0] - width :], "row", down)
    bottom = lax.ppermute(cells[:width], "row", up)
    left = lax.ppermute(cells[:, cells.shape[1] - width :], "col", rightward)
    right = lax.ppermute(cells[:, :width], "col", leftward)
    rims = jnp.concatenate([top, bottom], axis=0)
    left_corners = lax.ppermute(rims[:, cells.shape[1] - width :], "col", rightward)
    right_corners = lax.ppermute(rims[:, :width], "col", leftward)
    return (cells, top, bottom, left, right, left_corners, right_corners)


def depthwise_kernel(
    image_ref, top_ref, bottom_ref, left_ref, right_ref, lc_ref, rc_ref, k_ref, *rest, reach, chunk,
    flip
):
    if len(rest) == 5:
        base_ref, out_ref, framed_ref, shifted_ref, total_ref = rest
    else:
        base_ref = None
        out_ref, framed_ref, shifted_ref, total_ref = rest
    height, breadth, _ = out_ref.shape
    side = 2 * reach + 1
    framed_ref[reach : reach + height, reach : reach + breadth, :] = image_ref[...].astype(jnp.float32)
    framed_ref[:reach, reach : reach + breadth, :] = top_ref[...].astype(jnp.float32)
    framed_ref[reach + height :, reach : reach + breadth, :] = bottom_ref[...].astype(jnp.float32)
    framed_ref[reach : reach + height, :reach, :] = left_ref[...].astype(jnp.float32)
    framed_ref[reach : reach + height, reach + breadth :, :] = right_ref[...].astype(jnp.float32)
    framed_ref[:reach, :reach, :] = lc_ref[:reach].astype(jnp.float32)
    framed_ref[reach + height :, :reach, :] = lc_ref[reach:].astype(jnp.float32)
    framed_ref[:reach, reach + breadth :, :] = rc_ref[:reach].astype(jnp.float32)
    framed_ref[reach + height :, reach + breadth :, :] = rc_ref[reach:].astype(jnp.float32)
    for shift_c in range(side):
        shifted_ref[...] = framed_ref[:, shift_c : shift_c + breadth, :]

        def body(step, carry, shift_c=shift_c):
            start = pl.multiple_of(step * chunk, chunk)
            if shift_c > 0:
                total = total_ref[pl.ds(start, chunk)]
            elif base_ref is not None:
                total = base_ref[pl.ds(start, chunk)].astype(jnp.float32)
            else:
                total = jnp.zeros((chunk, breadth, out_ref.shape[2]), jnp.float32)
            for shift_r in range(side):
                if flip:
                    index = (side - 1 - shift_r) * side + (side - 1 - shift_c)
                else:
                    index = shift_r * side + shift_c
                tap = k_ref[pl.ds(index, 1), :]
                total = total + shifted_ref[pl.ds(start + shift_r, chunk)] * tap[None]
            if shift_c == side - 1:
                out_ref[pl.ds(start, chunk)] = total.astype(out_ref.dtype)
            else:
                total_ref[pl.ds(start, chunk)] = total
            return carry

        lax.fori_loop(0, height // chunk, body, 0)


def depthwise(pieces, taps, reach, base=None, flip=False, lanes=128, chunk=8):
    image = pieces[0]
    height, breadth, channels = image.shape
    framed = (height + 2 * reach, breadth + 2 * reach)
    in_specs = [
        pl.BlockSpec((height, breadth, lanes), lambda c: (0, 0, c)),
        pl.BlockSpec((reach, breadth, lanes), lambda c: (0, 0, c)),
        pl.BlockSpec((reach, breadth, lanes), lambda c: (0, 0, c)),
        pl.BlockSpec((height, reach, lanes), lambda c: (0, 0, c)),
        pl.BlockSpec((height, reach, lanes), lambda c: (0, 0, c)),
        pl.BlockSpec((2 * reach, reach, lanes), lambda c: (0, 0, c)),
        pl.BlockSpec((2 * reach, reach, lanes), lambda c: (0, 0, c)),
        pl.BlockSpec((taps.shape[0], lanes), lambda c: (0, c)),
    ]
    operands = list(pieces) + [taps]
    if base is not None:
        in_specs.append(pl.BlockSpec((height, breadth, lanes), lambda c: (0, 0, c)))
        operands.append(base)
    return pl.pallas_call(
        lambda *refs: depthwise_kernel(*refs, reach=reach, chunk=chunk, flip=flip),
        grid=(channels // lanes,),
        in_specs=in_specs,
        out_specs=pl.BlockSpec((height, breadth, lanes), lambda c: (0, 0, c)),
        out_shape=jax.ShapeDtypeStruct((height, breadth, channels), jnp.bfloat16),
        scratch_shapes=[
            pltpu.VMEM((framed[0], framed[1], lanes), jnp.float32),
            pltpu.VMEM((framed[0], breadth, lanes), jnp.float32),
            pltpu.VMEM((height, breadth, lanes), jnp.float32),
        ],
    )(*operands)


def normalize(values):
    average = jnp.mean(values, axis=-1, keepdims=True)
    centered = values - average
    inv_std = lax.rsqrt(jnp.mean(centered * centered, axis=-1, keepdims=True) + EPSILON)
    return (centered * inv_std, inv_std)


def normalize_back(gradient, normed, inv_std):
    return inv_std * (
        gradient
        - jnp.mean(gradient, axis=-1, keepdims=True)
        - normed * jnp.mean(gradient * normed, axis=-1, keepdims=True)
    )


def times_transposed(left, right):
    return lax.dot_general(
        left, right, (((1,), (1,)), ((), ())), preferred_element_type=jnp.float32
    )


def routed_tiles(tile_counts, tile_owner, tile_slot, peer_count, capacity):
    count_table = tile_counts[0]
    before = jnp.cumsum(count_table, axis=0) - count_table
    column_ids = jnp.arange(peer_count, dtype=jnp.int32)
    own_column = column_ids == lax.axis_index("col")
    my_bases = jnp.sum(jnp.where(own_column[:, None], before, 0), axis=0)
    my_counts = jnp.sum(jnp.where(own_column[:, None], count_table, 0), axis=0)
    owner_hits = tile_owner[:, :, None] == column_ids[None, None, :]
    base = jnp.sum(jnp.where(owner_hits, my_bases[None, None, :], 0), axis=2)
    quota = jnp.sum(jnp.where(owner_hits, my_counts[None, None, :], 0), axis=2)
    rank = tile_slot - base
    return (
        (tile_owner >= 0)
        & (rank >= 0)
        & (rank < capacity)
        & (rank < quota)
        & (tile_slot < LIVE_DEV)
    )


def patch_rows(row, column, breadth):
    return pl.ds(row * breadth + column, breadth // 2, stride=2)


def mlp_forward_kernel(
    live, mixed_ref, image_ref, w_in_ref, w_out_ref, w_down_ref, summed_ref, reduced_ref, low_ref,
    *, layout
):
    normed, _ = normalize(mixed_ref[...].astype(jnp.float32))
    hidden = jnp.dot(normed.astype(jnp.bfloat16), w_in_ref[...], preferred_element_type=jnp.float32)
    cdf = 0.5 * (1.0 + lax.erf(hidden * ROOT_HALF))
    activated = (hidden * cdf).astype(jnp.bfloat16)
    branch = jnp.dot(activated, w_out_ref[...], preferred_element_type=jnp.float32)
    branch = jnp.where(pixel_live(live, layout), branch.astype(jnp.bfloat16).astype(jnp.float32), 0.0)
    summed = (image_ref[...].astype(jnp.float32) + branch).astype(jnp.bfloat16)
    summed_ref[...] = summed
    down_normed, _ = normalize(summed.astype(jnp.float32))
    low = down_normed.astype(jnp.bfloat16).astype(jnp.float32)
    for k in range(low_ref.shape[0]):
        low_ref[k] = low[:, k * 128 : (k + 1) * 128]
    breadth = layout[1]
    pair_rows = layout[0] // breadth // 2
    total = jnp.zeros(reduced_ref.shape, jnp.float32)
    for a in range(2):
        for e in range(2):
            patch = jnp.concatenate(
                [
                    jnp.concatenate(
                        [low_ref[k, patch_rows(2 * y + a, e, breadth), :] for k in range(low_ref.shape[0])],
                        axis=1,
                    )
                    for y in range(pair_rows)
                ],
                axis=0,
            )
            total = total + jnp.dot(
                patch.astype(jnp.bfloat16), w_down_ref[2 * a + e], preferred_element_type=jnp.float32
            )
    reduced_ref[...] = total.astype(jnp.bfloat16)


def mlp_backward_kernel(
    live, mixed_ref, summed_ref, cot_ref, w_in_ref, w_out_ref, w_down_ref, grad_summed_ref,
    grad_mixed_ref, grad_ref, *, layout
):
    breadth = layout[1]
    pair_rows = layout[0] // breadth // 2
    half = breadth // 2
    for a in range(2):
        for e in range(2):
            part = times_transposed(cot_ref[...], w_down_ref[2 * a + e])
            for y in range(pair_rows):
                for k in range(grad_ref.shape[0]):
                    grad_ref[k, patch_rows(2 * y + a, e, breadth), :] = part[
                        y * half : (y + 1) * half, k * 128 : (k + 1) * 128
                    ]
    normed, inv_std = normalize(mixed_ref[...].astype(jnp.float32))
    hidden = jnp.dot(normed.astype(jnp.bfloat16), w_in_ref[...], preferred_element_type=jnp.float32)
    cdf = 0.5 * (1.0 + lax.erf(hidden * ROOT_HALF))
    slope = cdf + hidden * INV_ROOT_TAU * jnp.exp(-0.5 * hidden * hidden)
    down_normed, down_inv = normalize(summed_ref[...].astype(jnp.float32))
    grad_normed = jnp.concatenate([grad_ref[k] for k in range(grad_ref.shape[0])], axis=1)
    grad_summed = normalize_back(grad_normed, down_normed, down_inv).astype(jnp.bfloat16)
    grad_summed_ref[...] = grad_summed
    grad_hidden = (times_transposed(grad_summed, w_out_ref[...]) * slope).astype(jnp.bfloat16)
    grad_norm_in = times_transposed(grad_hidden, w_in_ref[...])
    grad_owned_mixed = normalize_back(grad_norm_in, normed, inv_std)
    grad_mixed_ref[...] = jnp.where(pixel_live(live, layout), grad_owned_mixed, 0.0).astype(jnp.bfloat16)


def pixel_live(live, layout):
    block, breadth, tile_side, tile_cols = layout
    place = lax.broadcasted_iota(jnp.int32, (block, 1), 0)
    tile = (place % breadth) // tile_side
    first = pl.program_id(0) * tile_cols
    flag = jnp.zeros((block, 1), jnp.int32)
    for column in range(tile_cols):
        flag = jnp.where(tile == column, live[first + column], flag)
    return flag > 0


def pixel_call(kernel, live, operands, kinds, outputs, layout, scratch):
    block = layout[0]
    steps = operands[0].shape[0] // block
    specs = []
    for operand, kind in zip(operands, kinds):
        if kind == "whole":
            specs.append(pl.BlockSpec(operand.shape, lambda i, live, n=operand.ndim: (0,) * n))
        else:
            rows = operand.shape[0] // steps
            specs.append(pl.BlockSpec((rows, operand.shape[1]), lambda i, live: (i, 0)))
    return pl.pallas_call(
        lambda *refs: kernel(*refs, layout=layout),
        grid_spec=pltpu.PrefetchScalarGridSpec(
            num_scalar_prefetch=1,
            grid=(steps,),
            in_specs=specs,
            out_specs=[
                pl.BlockSpec((rows // steps, width), lambda i, live: (i, 0)) for rows, width, _ in outputs
            ],
            scratch_shapes=[pltpu.VMEM((width // 128, block, 128), jnp.float32) for width in scratch],
        ),
        out_shape=[jax.ShapeDtypeStruct((rows, width), dtype) for rows, width, dtype in outputs],
    )(live, *operands)


def on_device(
    image,
    depth_kernel,
    weight_in,
    weight_out,
    weight_down,
    tissue_mask,
    tile_counts,
    tile_owner,
    tile_slot,
    cotangent,
):
    height, breadth, channels = image.shape
    tile_rows, tile_cols = tissue_mask.shape
    tile_side = height // tile_rows
    outputs = weight_down.shape[3]
    reach = KS // 2
    peer_count = lax.axis_size("col")
    capacity = tile_rows * tile_cols // peer_count
    pixels = height * breadth
    routed = routed_tiles(tile_counts, tile_owner, tile_slot, peer_count, capacity)
    live = routed & (tissue_mask != 0)
    live = live.reshape(-1).astype(jnp.int32)
    layout = (tile_side * breadth, breadth, tile_side, tile_cols)
    taps = depth_kernel.reshape(KS * KS, channels).astype(jnp.float32)
    mixed = depthwise(halo_pieces(image, reach), taps, reach)
    mixed = mixed.reshape(pixels, channels)
    weight_quad = weight_down.reshape(4, channels, outputs)
    patches = pixels // 4
    summed, reduced = pixel_call(
        mlp_forward_kernel,
        live,
        (mixed, image.reshape(pixels, channels), weight_in, weight_out, weight_quad),
        ("rows", "rows", "whole", "whole", "whole"),
        ((pixels, channels, jnp.bfloat16), (patches, outputs, jnp.bfloat16)),
        layout,
        (channels,),
    )
    reduced = reduced.reshape(height // 2, breadth // 2, outputs)
    grad_summed, grad_mixed = pixel_call(
        mlp_backward_kernel,
        live,
        (mixed, summed, cotangent.reshape(patches, outputs), weight_in, weight_out, weight_quad),
        ("rows", "rows", "rows", "whole", "whole", "whole"),
        ((pixels, channels, jnp.bfloat16), (pixels, channels, jnp.bfloat16)),
        layout,
        (channels,),
    )
    grad_image = depthwise(
        halo_pieces(grad_mixed.reshape(height, breadth, channels), reach),
        taps,
        reach,
        base=grad_summed.reshape(height, breadth, channels),
        flip=True,
    )
    return (reduced, grad_image)


def solution(mesh):
    in_specs = (
        P("row", "col", None),
        P(),
        P(),
        P(),
        P(),
        P("row", "col"),
        P("row", None, None),
        P("row", "col"),
        P("row", "col"),
        P("row", "col", None),
    )
    out_specs = (P("row", "col", None), P("row", "col", None))
    return jax.shard_map(
        on_device, mesh=mesh, in_specs=in_specs, out_specs=out_specs, check_vma=False
    )
```

```python
import jax
import jax.numpy as jnp
from jax import lax
from jax.sharding import PartitionSpec as P
from jax.experimental import pallas as pl
from jax.experimental.pallas import tpu as pltpu

KS = 7
LIVE_DEV = 18
SPAN = 512


EPSILON = 1e-06
ROOT_HALF = 0.7071067811865476
INV_ROOT_TAU = 0.3989422804014327


def halo_pieces(cells, width):
    rows = lax.axis_size("row")
    cols = lax.axis_size("col")
    down = [(i, i + 1) for i in range(rows - 1)]
    up = [(i + 1, i) for i in range(rows - 1)]
    top = lax.ppermute(cells[cells.shape[0] - width :], "row", down)
    bottom = lax.ppermute(cells[:width], "row", up)
    framed = jnp.concatenate([top, cells, bottom], axis=0)
    left = lax.ppermute(framed[:, cells.shape[1] - width :], "col", [(i, i + 1) for i in range(cols - 1)])
    right = lax.ppermute(framed[:, :width], "col", [(i + 1, i) for i in range(cols - 1)])
    return (cells, top, bottom, left, right)


def depthwise_kernel(
    image_ref, top_ref, bottom_ref, left_ref, right_ref, k_ref, *rest, reach, chunk, flip
):
    if len(rest) == 5:
        base_ref, out_ref, framed_ref, shifted_ref, total_ref = rest
    else:
        base_ref = None
        out_ref, framed_ref, shifted_ref, total_ref = rest
    height, breadth, _ = out_ref.shape
    side = 2 * reach + 1
    framed_ref[reach : reach + height, reach : reach + breadth, :] = image_ref[...].astype(jnp.float32)
    framed_ref[:reach, reach : reach + breadth, :] = top_ref[...].astype(jnp.float32)
    framed_ref[reach + height :, reach : reach + breadth, :] = bottom_ref[...].astype(jnp.float32)
    framed_ref[:, :reach, :] = left_ref[...].astype(jnp.float32)
    framed_ref[:, reach + breadth :, :] = right_ref[...].astype(jnp.float32)
    for shift_c in range(side):
        shifted_ref[...] = framed_ref[:, shift_c : shift_c + breadth, :]

        def body(step, carry, shift_c=shift_c):
            start = pl.multiple_of(step * chunk, chunk)
            if shift_c > 0:
                total = total_ref[pl.ds(start, chunk)]
            elif base_ref is not None:
                total = base_ref[pl.ds(start, chunk)].astype(jnp.float32)
            else:
                total = jnp.zeros((chunk, breadth, out_ref.shape[2]), jnp.float32)
            for shift_r in range(side):
                if flip:
                    index = (side - 1 - shift_r) * side + (side - 1 - shift_c)
                else:
                    index = shift_r * side + shift_c
                tap = k_ref[pl.ds(index, 1), :]
                total = total + shifted_ref[pl.ds(start + shift_r, chunk)] * tap[None]
            if shift_c == side - 1:
                out_ref[pl.ds(start, chunk)] = total.astype(out_ref.dtype)
            else:
                total_ref[pl.ds(start, chunk)] = total
            return carry

        lax.fori_loop(0, height // chunk, body, 0)


def depthwise(pieces, taps, reach, base=None, flip=False, lanes=128, chunk=8):
    image = pieces[0]
    height, breadth, channels = image.shape
    framed = (height + 2 * reach, breadth + 2 * reach)
    in_specs = [
        pl.BlockSpec((height, breadth, lanes), lambda c: (0, 0, c)),
        pl.BlockSpec((reach, breadth, lanes), lambda c: (0, 0, c)),
        pl.BlockSpec((reach, breadth, lanes), lambda c: (0, 0, c)),
        pl.BlockSpec((framed[0], reach, lanes), lambda c: (0, 0, c)),
        pl.BlockSpec((framed[0], reach, lanes), lambda c: (0, 0, c)),
        pl.BlockSpec((taps.shape[0], lanes), lambda c: (0, c)),
    ]
    operands = list(pieces) + [taps]
    if base is not None:
        in_specs.append(pl.BlockSpec((height, breadth, lanes), lambda c: (0, 0, c)))
        operands.append(base)
    return pl.pallas_call(
        lambda *refs: depthwise_kernel(*refs, reach=reach, chunk=chunk, flip=flip),
        grid=(channels // lanes,),
        in_specs=in_specs,
        out_specs=pl.BlockSpec((height, breadth, lanes), lambda c: (0, 0, c)),
        out_shape=jax.ShapeDtypeStruct((height, breadth, channels), jnp.bfloat16),
        scratch_shapes=[
            pltpu.VMEM((framed[0], framed[1], lanes), jnp.float32),
            pltpu.VMEM((framed[0], breadth, lanes), jnp.float32),
            pltpu.VMEM((height, breadth, lanes), jnp.float32),
        ],
    )(*operands)


def normalize(values):
    average = jnp.mean(values, axis=-1, keepdims=True)
    centered = values - average
    inv_std = lax.rsqrt(jnp.mean(centered * centered, axis=-1, keepdims=True) + EPSILON)
    return (centered * inv_std, inv_std)


def normalize_back(gradient, normed, inv_std):
    return inv_std * (
        gradient
        - jnp.mean(gradient, axis=-1, keepdims=True)
        - normed * jnp.mean(gradient * normed, axis=-1, keepdims=True)
    )


def times_transposed(left, right):
    return lax.dot_general(
        left, right, (((1,), (1,)), ((), ())), preferred_element_type=jnp.float32
    )


def routed_tiles(tile_counts, tile_owner, tile_slot, peer_count, capacity):
    count_table = tile_counts[0]
    before = jnp.cumsum(count_table, axis=0) - count_table
    column_ids = jnp.arange(peer_count, dtype=jnp.int32)
    own_column = column_ids == lax.axis_index("col")
    my_bases = jnp.sum(jnp.where(own_column[:, None], before, 0), axis=0)
    my_counts = jnp.sum(jnp.where(own_column[:, None], count_table, 0), axis=0)
    owner_hits = tile_owner[:, :, None] == column_ids[None, None, :]
    base = jnp.sum(jnp.where(owner_hits, my_bases[None, None, :], 0), axis=2)
    quota = jnp.sum(jnp.where(owner_hits, my_counts[None, None, :], 0), axis=2)
    rank = tile_slot - base
    return (
        (tile_owner >= 0)
        & (rank >= 0)
        & (rank < capacity)
        & (rank < quota)
        & (tile_slot < LIVE_DEV)
    )


def patch_rows(row, column, breadth):
    return pl.ds(row * breadth + column, breadth // 2, stride=2)


def mlp_forward_kernel(
    live, mixed_ref, image_ref, w_in_ref, w_out_ref, w_down_ref, summed_ref, reduced_ref, low_ref,
    *, layout
):
    normed, _ = normalize(mixed_ref[...].astype(jnp.float32))
    normed_low = normed.astype(jnp.bfloat16)
    branch = None
    for start in range(0, w_in_ref.shape[1], SPAN):
        hidden = jnp.dot(
            normed_low, w_in_ref[:, start : start + SPAN], preferred_element_type=jnp.float32
        )
        cdf = 0.5 * (1.0 + lax.erf(hidden * ROOT_HALF))
        activated = (hidden * cdf).astype(jnp.bfloat16)
        part = jnp.dot(
            activated, w_out_ref[start : start + SPAN, :], preferred_element_type=jnp.float32
        )
        branch = part if branch is None else branch + part
    branch = jnp.where(pixel_live(live, layout), branch.astype(jnp.bfloat16).astype(jnp.float32), 0.0)
    summed = (image_ref[...].astype(jnp.float32) + branch).astype(jnp.bfloat16)
    summed_ref[...] = summed
    down_normed, _ = normalize(summed.astype(jnp.float32))
    low = down_normed.astype(jnp.bfloat16).astype(jnp.float32)
    for k in range(low_ref.shape[0]):
        low_ref[k] = low[:, k * 128 : (k + 1) * 128]
    breadth = layout[1]
    pair_rows = layout[0] // breadth // 2
    total = jnp.zeros(reduced_ref.shape, jnp.float32)
    for a in range(2):
        for e in range(2):
            patch = jnp.concatenate(
                [
                    jnp.concatenate(
                        [low_ref[k, patch_rows(2 * y + a, e, breadth), :] for k in range(low_ref.shape[0])],
                        axis=1,
                    )
                    for y in range(pair_rows)
                ],
                axis=0,
            )
            total = total + jnp.dot(
                patch.astype(jnp.bfloat16), w_down_ref[2 * a + e], preferred_element_type=jnp.float32
            )
    reduced_ref[...] = total.astype(jnp.bfloat16)


def mlp_backward_kernel(
    live, mixed_ref, summed_ref, cot_ref, w_in_ref, w_out_ref, w_down_ref, grad_summed_ref,
    grad_mixed_ref, grad_ref, *, layout
):
    breadth = layout[1]
    pair_rows = layout[0] // breadth // 2
    half = breadth // 2
    for a in range(2):
        for e in range(2):
            part = times_transposed(cot_ref[...], w_down_ref[2 * a + e])
            for y in range(pair_rows):
                for k in range(grad_ref.shape[0]):
                    grad_ref[k, patch_rows(2 * y + a, e, breadth), :] = part[
                        y * half : (y + 1) * half, k * 128 : (k + 1) * 128
                    ]
    normed, inv_std = normalize(mixed_ref[...].astype(jnp.float32))
    down_normed, down_inv = normalize(summed_ref[...].astype(jnp.float32))
    grad_normed = jnp.concatenate([grad_ref[k] for k in range(grad_ref.shape[0])], axis=1)
    grad_summed = normalize_back(grad_normed, down_normed, down_inv).astype(jnp.bfloat16)
    grad_summed_ref[...] = grad_summed
    normed_low = normed.astype(jnp.bfloat16)
    grad_norm_in = None
    for start in range(0, w_in_ref.shape[1], SPAN):
        w_in = w_in_ref[:, start : start + SPAN]
        hidden = jnp.dot(normed_low, w_in, preferred_element_type=jnp.float32)
        cdf = 0.5 * (1.0 + lax.erf(hidden * ROOT_HALF))
        slope = cdf + hidden * INV_ROOT_TAU * jnp.exp(-0.5 * hidden * hidden)
        grad_hidden = (
            times_transposed(grad_summed, w_out_ref[start : start + SPAN, :]) * slope
        ).astype(jnp.bfloat16)
        part = times_transposed(grad_hidden, w_in)
        grad_norm_in = part if grad_norm_in is None else grad_norm_in + part
    grad_owned_mixed = normalize_back(grad_norm_in, normed, inv_std)
    grad_mixed_ref[...] = jnp.where(pixel_live(live, layout), grad_owned_mixed, 0.0).astype(jnp.bfloat16)


def pixel_live(live, layout):
    block, breadth, tile_side, tile_cols = layout
    place = lax.broadcasted_iota(jnp.int32, (block, 1), 0)
    tile = (place % breadth) // tile_side
    first = pl.program_id(0) * tile_cols
    flag = jnp.zeros((block, 1), jnp.int32)
    for column in range(tile_cols):
        flag = jnp.where(tile == column, live[first + column], flag)
    return flag > 0


def pixel_call(kernel, live, operands, kinds, outputs, layout, scratch):
    block = layout[0]
    steps = operands[0].shape[0] // block
    specs = []
    for operand, kind in zip(operands, kinds):
        if kind == "whole":
            specs.append(pl.BlockSpec(operand.shape, lambda i, live, n=operand.ndim: (0,) * n))
        else:
            rows = operand.shape[0] // steps
            specs.append(pl.BlockSpec((rows, operand.shape[1]), lambda i, live: (i, 0)))
    return pl.pallas_call(
        lambda *refs: kernel(*refs, layout=layout),
        grid_spec=pltpu.PrefetchScalarGridSpec(
            num_scalar_prefetch=1,
            grid=(steps,),
            in_specs=specs,
            out_specs=[
                pl.BlockSpec((rows // steps, width), lambda i, live: (i, 0)) for rows, width, _ in outputs
            ],
            scratch_shapes=[pltpu.VMEM((width // 128, block, 128), jnp.float32) for width in scratch],
        ),
        out_shape=[jax.ShapeDtypeStruct((rows, width), dtype) for rows, width, dtype in outputs],
    )(live, *operands)


def on_device(
    image,
    depth_kernel,
    weight_in,
    weight_out,
    weight_down,
    tissue_mask,
    tile_counts,
    tile_owner,
    tile_slot,
    cotangent,
):
    height, breadth, channels = image.shape
    tile_rows, tile_cols = tissue_mask.shape
    tile_side = height // tile_rows
    outputs = weight_down.shape[3]
    reach = KS // 2
    peer_count = lax.axis_size("col")
    capacity = tile_rows * tile_cols // peer_count
    pixels = height * breadth
    routed = routed_tiles(tile_counts, tile_owner, tile_slot, peer_count, capacity)
    live = routed & (tissue_mask != 0)
    live = live.reshape(-1).astype(jnp.int32)
    layout = (tile_side * breadth, breadth, tile_side, tile_cols)
    taps = depth_kernel.reshape(KS * KS, channels).astype(jnp.float32)
    mixed = depthwise(halo_pieces(image, reach), taps, reach)
    mixed = mixed.reshape(pixels, channels)
    weight_quad = weight_down.reshape(4, channels, outputs)
    patches = pixels // 4
    summed, reduced = pixel_call(
        mlp_forward_kernel,
        live,
        (mixed, image.reshape(pixels, channels), weight_in, weight_out, weight_quad),
        ("rows", "rows", "whole", "whole", "whole"),
        ((pixels, channels, jnp.bfloat16), (patches, outputs, jnp.bfloat16)),
        layout,
        (channels,),
    )
    reduced = reduced.reshape(height // 2, breadth // 2, outputs)
    grad_summed, grad_mixed = pixel_call(
        mlp_backward_kernel,
        live,
        (mixed, summed, cotangent.reshape(patches, outputs), weight_in, weight_out, weight_quad),
        ("rows", "rows", "rows", "whole", "whole", "whole"),
        ((pixels, channels, jnp.bfloat16), (pixels, channels, jnp.bfloat16)),
        layout,
        (channels,),
    )
    grad_image = depthwise(
        halo_pieces(grad_mixed.reshape(height, breadth, channels), reach),
        taps,
        reach,
        base=grad_summed.reshape(height, breadth, channels),
        flip=True,
    )
    return (reduced, grad_image)


def solution(mesh):
    in_specs = (
        P("row", "col", None),
        P(),
        P(),
        P(),
        P(),
        P("row", "col"),
        P("row", None, None),
        P("row", "col"),
        P("row", "col"),
        P("row", "col", None),
    )
    out_specs = (P("row", "col", None), P("row", "col", None))
    return jax.shard_map(
        on_device, mesh=mesh, in_specs=in_specs, out_specs=out_specs, check_vma=False
    )
```

```python
import jax
import jax.numpy as jnp
from jax import lax
from jax.sharding import PartitionSpec as P
from jax.experimental import pallas as pl
from jax.experimental.pallas import tpu as pltpu

KS = 7
LIVE_DEV = 18


EPSILON = 1e-06
ROOT_HALF = 0.7071067811865476
INV_ROOT_TAU = 0.3989422804014327


def halo_pieces(cells, width):
    rows = lax.axis_size("row")
    cols = lax.axis_size("col")
    down = [(i, i + 1) for i in range(rows - 1)]
    up = [(i + 1, i) for i in range(rows - 1)]
    top = lax.ppermute(cells[cells.shape[0] - width :], "row", down)
    bottom = lax.ppermute(cells[:width], "row", up)
    framed = jnp.concatenate([top, cells, bottom], axis=0)
    left = lax.ppermute(framed[:, cells.shape[1] - width :], "col", [(i, i + 1) for i in range(cols - 1)])
    right = lax.ppermute(framed[:, :width], "col", [(i + 1, i) for i in range(cols - 1)])
    return (cells, top, bottom, left, right)


def depthwise_kernel(
    image_ref, top_ref, bottom_ref, left_ref, right_ref, k_ref, *rest, reach, chunk, flip
):
    if len(rest) == 5:
        base_ref, out_ref, framed_ref, shifted_ref, total_ref = rest
    else:
        base_ref = None
        out_ref, framed_ref, shifted_ref, total_ref = rest
    height, breadth, _ = out_ref.shape
    side = 2 * reach + 1
    framed_ref[reach : reach + height, reach : reach + breadth, :] = image_ref[...].astype(jnp.float32)
    framed_ref[:reach, reach : reach + breadth, :] = top_ref[...].astype(jnp.float32)
    framed_ref[reach + height :, reach : reach + breadth, :] = bottom_ref[...].astype(jnp.float32)
    framed_ref[:, :reach, :] = left_ref[...].astype(jnp.float32)
    framed_ref[:, reach + breadth :, :] = right_ref[...].astype(jnp.float32)
    for shift_c in range(side):
        shifted_ref[...] = framed_ref[:, shift_c : shift_c + breadth, :]

        def body(step, carry, shift_c=shift_c):
            start = pl.multiple_of(step * chunk, chunk)
            if shift_c > 0:
                total = total_ref[pl.ds(start, chunk)]
            elif base_ref is not None:
                total = base_ref[pl.ds(start, chunk)].astype(jnp.float32)
            else:
                total = jnp.zeros((chunk, breadth, out_ref.shape[2]), jnp.float32)
            for shift_r in range(side):
                if flip:
                    index = (side - 1 - shift_r) * side + (side - 1 - shift_c)
                else:
                    index = shift_r * side + shift_c
                tap = k_ref[pl.ds(index, 1), :]
                total = total + shifted_ref[pl.ds(start + shift_r, chunk)] * tap[None]
            if shift_c == side - 1:
                out_ref[pl.ds(start, chunk)] = total.astype(out_ref.dtype)
            else:
                total_ref[pl.ds(start, chunk)] = total
            return carry

        lax.fori_loop(0, height // chunk, body, 0)


def depthwise(pieces, taps, reach, base=None, flip=False, lanes=128, chunk=8):
    image = pieces[0]
    height, breadth, channels = image.shape
    framed = (height + 2 * reach, breadth + 2 * reach)
    in_specs = [
        pl.BlockSpec((height, breadth, lanes), lambda c: (0, 0, c)),
        pl.BlockSpec((reach, breadth, lanes), lambda c: (0, 0, c)),
        pl.BlockSpec((reach, breadth, lanes), lambda c: (0, 0, c)),
        pl.BlockSpec((framed[0], reach, lanes), lambda c: (0, 0, c)),
        pl.BlockSpec((framed[0], reach, lanes), lambda c: (0, 0, c)),
        pl.BlockSpec((taps.shape[0], lanes), lambda c: (0, c)),
    ]
    operands = list(pieces) + [taps]
    if base is not None:
        in_specs.append(pl.BlockSpec((height, breadth, lanes), lambda c: (0, 0, c)))
        operands.append(base)
    return pl.pallas_call(
        lambda *refs: depthwise_kernel(*refs, reach=reach, chunk=chunk, flip=flip),
        grid=(channels // lanes,),
        in_specs=in_specs,
        out_specs=pl.BlockSpec((height, breadth, lanes), lambda c: (0, 0, c)),
        out_shape=jax.ShapeDtypeStruct((height, breadth, channels), jnp.bfloat16),
        scratch_shapes=[
            pltpu.VMEM((framed[0], framed[1], lanes), jnp.float32),
            pltpu.VMEM((framed[0], breadth, lanes), jnp.float32),
            pltpu.VMEM((height, breadth, lanes), jnp.float32),
        ],
    )(*operands)


def normalize(values):
    average = jnp.mean(values, axis=-1, keepdims=True)
    centered = values - average
    inv_std = lax.rsqrt(jnp.mean(centered * centered, axis=-1, keepdims=True) + EPSILON)
    return (centered * inv_std, inv_std)


def normalize_back(gradient, normed, inv_std):
    return inv_std * (
        gradient
        - jnp.mean(gradient, axis=-1, keepdims=True)
        - normed * jnp.mean(gradient * normed, axis=-1, keepdims=True)
    )


def times_transposed(left, right):
    return lax.dot_general(
        left, right, (((1,), (1,)), ((), ())), preferred_element_type=jnp.float32
    )


def routed_tiles(tile_counts, tile_owner, tile_slot, peer_count, capacity):
    count_table = tile_counts[0]
    before = jnp.cumsum(count_table, axis=0) - count_table
    column_ids = jnp.arange(peer_count, dtype=jnp.int32)
    own_column = column_ids == lax.axis_index("col")
    my_bases = jnp.sum(jnp.where(own_column[:, None], before, 0), axis=0)
    my_counts = jnp.sum(jnp.where(own_column[:, None], count_table, 0), axis=0)
    owner_hits = tile_owner[:, :, None] == column_ids[None, None, :]
    base = jnp.sum(jnp.where(owner_hits, my_bases[None, None, :], 0), axis=2)
    quota = jnp.sum(jnp.where(owner_hits, my_counts[None, None, :], 0), axis=2)
    rank = tile_slot - base
    return (
        (tile_owner >= 0)
        & (rank >= 0)
        & (rank < capacity)
        & (rank < quota)
        & (tile_slot < LIVE_DEV)
    )


def patch_rows(row, column, breadth):
    return pl.ds(row * breadth + column, breadth // 2, stride=2)


def mlp_forward_kernel(
    live, mixed_ref, image_ref, w_in_ref, w_out_ref, w_down_ref, summed_ref, reduced_ref, low_ref,
    *, layout
):
    normed, _ = normalize(mixed_ref[...].astype(jnp.float32))
    hidden = jnp.dot(normed.astype(jnp.bfloat16), w_in_ref[...], preferred_element_type=jnp.float32)
    cdf = 0.5 * (1.0 + lax.erf(hidden * ROOT_HALF))
    activated = (hidden * cdf).astype(jnp.bfloat16)
    branch = jnp.dot(activated, w_out_ref[...], preferred_element_type=jnp.float32)
    branch = jnp.where(pixel_live(live, layout), branch.astype(jnp.bfloat16).astype(jnp.float32), 0.0)
    summed = (image_ref[...].astype(jnp.float32) + branch).astype(jnp.bfloat16)
    summed_ref[...] = summed
    down_normed, _ = normalize(summed.astype(jnp.float32))
    low = down_normed.astype(jnp.bfloat16).astype(jnp.float32)
    for k in range(low_ref.shape[0]):
        low_ref[k] = low[:, k * 128 : (k + 1) * 128]
    breadth = layout[1]
    pair_rows = layout[0] // breadth // 2
    total = jnp.zeros(reduced_ref.shape, jnp.float32)
    for a in range(2):
        for e in range(2):
            patch = jnp.concatenate(
                [
                    jnp.concatenate(
                        [low_ref[k, patch_rows(2 * y + a, e, breadth), :] for k in range(low_ref.shape[0])],
                        axis=1,
                    )
                    for y in range(pair_rows)
                ],
                axis=0,
            )
            total = total + jnp.dot(
                patch.astype(jnp.bfloat16), w_down_ref[2 * a + e], preferred_element_type=jnp.float32
            )
    reduced_ref[...] = total.astype(jnp.bfloat16)


def mlp_backward_kernel(
    live, mixed_ref, summed_ref, cot_ref, w_in_ref, w_out_ref, w_down_ref, grad_summed_ref,
    grad_mixed_ref, grad_ref, *, layout
):
    breadth = layout[1]
    pair_rows = layout[0] // breadth // 2
    half = breadth // 2
    for a in range(2):
        for e in range(2):
            part = times_transposed(cot_ref[...], w_down_ref[2 * a + e])
            for y in range(pair_rows):
                for k in range(grad_ref.shape[0]):
                    grad_ref[k, patch_rows(2 * y + a, e, breadth), :] = part[
                        y * half : (y + 1) * half, k * 128 : (k + 1) * 128
                    ]
    normed, inv_std = normalize(mixed_ref[...].astype(jnp.float32))
    hidden = jnp.dot(normed.astype(jnp.bfloat16), w_in_ref[...], preferred_element_type=jnp.float32)
    cdf = 0.5 * (1.0 + lax.erf(hidden * ROOT_HALF))
    slope = cdf + hidden * INV_ROOT_TAU * jnp.exp(-0.5 * hidden * hidden)
    down_normed, down_inv = normalize(summed_ref[...].astype(jnp.float32))
    grad_normed = jnp.concatenate([grad_ref[k] for k in range(grad_ref.shape[0])], axis=1)
    grad_summed = normalize_back(grad_normed, down_normed, down_inv).astype(jnp.bfloat16)
    grad_summed_ref[...] = grad_summed
    grad_hidden = (times_transposed(grad_summed, w_out_ref[...]) * slope).astype(jnp.bfloat16)
    grad_norm_in = times_transposed(grad_hidden, w_in_ref[...])
    grad_owned_mixed = normalize_back(grad_norm_in, normed, inv_std)
    grad_mixed_ref[...] = jnp.where(pixel_live(live, layout), grad_owned_mixed, 0.0).astype(jnp.bfloat16)


def pixel_live(live, layout):
    block, breadth, tile_side, tile_cols = layout
    band = block // breadth // tile_side
    place = lax.broadcasted_iota(jnp.int32, (block, 1), 0)
    tile = (place // breadth // tile_side) * tile_cols + (place % breadth) // tile_side
    first = pl.program_id(0) * band * tile_cols
    flag = jnp.zeros((block, 1), jnp.int32)
    for index in range(band * tile_cols):
        flag = jnp.where(tile == index, live[first + index], flag)
    return flag > 0


def pixel_call(kernel, live, operands, kinds, outputs, layout, scratch):
    block = layout[0]
    steps = operands[0].shape[0] // block
    specs = []
    for operand, kind in zip(operands, kinds):
        if kind == "whole":
            specs.append(pl.BlockSpec(operand.shape, lambda i, live, n=operand.ndim: (0,) * n))
        else:
            rows = operand.shape[0] // steps
            specs.append(pl.BlockSpec((rows, operand.shape[1]), lambda i, live: (i, 0)))
    return pl.pallas_call(
        lambda *refs: kernel(*refs, layout=layout),
        grid_spec=pltpu.PrefetchScalarGridSpec(
            num_scalar_prefetch=1,
            grid=(steps,),
            in_specs=specs,
            out_specs=[
                pl.BlockSpec((rows // steps, width), lambda i, live: (i, 0)) for rows, width, _ in outputs
            ],
            scratch_shapes=[pltpu.VMEM((width // 128, block, 128), jnp.float32) for width in scratch],
        ),
        out_shape=[jax.ShapeDtypeStruct((rows, width), dtype) for rows, width, dtype in outputs],
    )(live, *operands)


def on_device(
    image,
    depth_kernel,
    weight_in,
    weight_out,
    weight_down,
    tissue_mask,
    tile_counts,
    tile_owner,
    tile_slot,
    cotangent,
):
    height, breadth, channels = image.shape
    tile_rows, tile_cols = tissue_mask.shape
    tile_side = height // tile_rows
    outputs = weight_down.shape[3]
    reach = KS // 2
    peer_count = lax.axis_size("col")
    capacity = tile_rows * tile_cols // peer_count
    pixels = height * breadth
    routed = routed_tiles(tile_counts, tile_owner, tile_slot, peer_count, capacity)
    live = routed & (tissue_mask != 0)
    live = live.reshape(-1).astype(jnp.int32)
    band = 2 if tile_rows % 2 == 0 else 1
    layout = (band * tile_side * breadth, breadth, tile_side, tile_cols)
    taps = depth_kernel.reshape(KS * KS, channels).astype(jnp.float32)
    mixed = depthwise(halo_pieces(image, reach), taps, reach)
    mixed = mixed.reshape(pixels, channels)
    weight_quad = weight_down.reshape(4, channels, outputs)
    patches = pixels // 4
    summed, reduced = pixel_call(
        mlp_forward_kernel,
        live,
        (mixed, image.reshape(pixels, channels), weight_in, weight_out, weight_quad),
        ("rows", "rows", "whole", "whole", "whole"),
        ((pixels, channels, jnp.bfloat16), (patches, outputs, jnp.bfloat16)),
        layout,
        (channels,),
    )
    reduced = reduced.reshape(height // 2, breadth // 2, outputs)
    grad_summed, grad_mixed = pixel_call(
        mlp_backward_kernel,
        live,
        (mixed, summed, cotangent.reshape(patches, outputs), weight_in, weight_out, weight_quad),
        ("rows", "rows", "rows", "whole", "whole", "whole"),
        ((pixels, channels, jnp.bfloat16), (pixels, channels, jnp.bfloat16)),
        layout,
        (channels,),
    )
    grad_image = depthwise(
        halo_pieces(grad_mixed.reshape(height, breadth, channels), reach),
        taps,
        reach,
        base=grad_summed.reshape(height, breadth, channels),
        flip=True,
    )
    return (reduced, grad_image)


def solution(mesh):
    in_specs = (
        P("row", "col", None),
        P(),
        P(),
        P(),
        P(),
        P("row", "col"),
        P("row", None, None),
        P("row", "col"),
        P("row", "col"),
        P("row", "col", None),
    )
    out_specs = (P("row", "col", None), P("row", "col", None))
    return jax.shard_map(
        on_device, mesh=mesh, in_specs=in_specs, out_specs=out_specs, check_vma=False
    )
```

```python
import jax
import jax.numpy as jnp
from jax import lax
from jax.sharding import PartitionSpec as P
from jax.experimental import pallas as pl
from jax.experimental.pallas import tpu as pltpu

KS = 7
LIVE_DEV = 18


EPSILON = 1e-06
ROOT_HALF = 0.7071067811865476
INV_ROOT_TAU = 0.3989422804014327


def halo_pieces(cells, width):
    rows = lax.axis_size("row")
    cols = lax.axis_size("col")
    down = [(i, i + 1) for i in range(rows - 1)]
    up = [(i + 1, i) for i in range(rows - 1)]
    top = lax.ppermute(cells[cells.shape[0] - width :], "row", down)
    bottom = lax.ppermute(cells[:width], "row", up)
    framed = jnp.concatenate([top, cells, bottom], axis=0)
    left = lax.ppermute(framed[:, cells.shape[1] - width :], "col", [(i, i + 1) for i in range(cols - 1)])
    right = lax.ppermute(framed[:, :width], "col", [(i + 1, i) for i in range(cols - 1)])
    return (cells, top, bottom, left, right)


def depthwise_kernel(
    image_ref, top_ref, bottom_ref, left_ref, right_ref, k_ref, *rest, reach, chunk, flip
):
    if len(rest) == 5:
        base_ref, out_ref, framed_ref, shifted_ref, total_ref = rest
    else:
        base_ref = None
        out_ref, framed_ref, shifted_ref, total_ref = rest
    height, breadth, _ = out_ref.shape
    side = 2 * reach + 1
    framed_ref[reach : reach + height, reach : reach + breadth, :] = image_ref[...].astype(jnp.float32)
    framed_ref[:reach, reach : reach + breadth, :] = top_ref[...].astype(jnp.float32)
    framed_ref[reach + height :, reach : reach + breadth, :] = bottom_ref[...].astype(jnp.float32)
    framed_ref[:, :reach, :] = left_ref[...].astype(jnp.float32)
    framed_ref[:, reach + breadth :, :] = right_ref[...].astype(jnp.float32)
    for shift_c in range(side):
        shifted_ref[...] = framed_ref[:, shift_c : shift_c + breadth, :]

        def body(step, carry, shift_c=shift_c):
            start = pl.multiple_of(step * chunk, chunk)
            if shift_c > 0:
                total = total_ref[pl.ds(start, chunk)]
            elif base_ref is not None:
                total = base_ref[pl.ds(start, chunk)].astype(jnp.float32)
            else:
                total = jnp.zeros((chunk, breadth, out_ref.shape[2]), jnp.float32)
            for shift_r in range(side):
                if flip:
                    index = (side - 1 - shift_r) * side + (side - 1 - shift_c)
                else:
                    index = shift_r * side + shift_c
                tap = k_ref[pl.ds(index, 1), :]
                total = total + shifted_ref[pl.ds(start + shift_r, chunk)] * tap[None]
            if shift_c == side - 1:
                out_ref[pl.ds(start, chunk)] = total.astype(out_ref.dtype)
            else:
                total_ref[pl.ds(start, chunk)] = total
            return carry

        lax.fori_loop(0, height // chunk, body, 0)


def depthwise(pieces, taps, reach, base=None, flip=False, lanes=128, chunk=8):
    image = pieces[0]
    height, breadth, channels = image.shape
    framed = (height + 2 * reach, breadth + 2 * reach)
    in_specs = [
        pl.BlockSpec((height, breadth, lanes), lambda c: (0, 0, c)),
        pl.BlockSpec((reach, breadth, lanes), lambda c: (0, 0, c)),
        pl.BlockSpec((reach, breadth, lanes), lambda c: (0, 0, c)),
        pl.BlockSpec((framed[0], reach, lanes), lambda c: (0, 0, c)),
        pl.BlockSpec((framed[0], reach, lanes), lambda c: (0, 0, c)),
        pl.BlockSpec((taps.shape[0], lanes), lambda c: (0, c)),
    ]
    operands = list(pieces) + [taps]
    if base is not None:
        in_specs.append(pl.BlockSpec((height, breadth, lanes), lambda c: (0, 0, c)))
        operands.append(base)
    return pl.pallas_call(
        lambda *refs: depthwise_kernel(*refs, reach=reach, chunk=chunk, flip=flip),
        grid=(channels // lanes,),
        in_specs=in_specs,
        out_specs=pl.BlockSpec((height, breadth, lanes), lambda c: (0, 0, c)),
        out_shape=jax.ShapeDtypeStruct((height, breadth, channels), jnp.bfloat16),
        scratch_shapes=[
            pltpu.VMEM((framed[0], framed[1], lanes), jnp.float32),
            pltpu.VMEM((framed[0], breadth, lanes), jnp.float32),
            pltpu.VMEM((height, breadth, lanes), jnp.float32),
        ],
    )(*operands)


def normalize(values):
    average = jnp.mean(values, axis=-1, keepdims=True)
    centered = values - average
    inv_std = lax.rsqrt(jnp.mean(centered * centered, axis=-1, keepdims=True) + EPSILON)
    return (centered * inv_std, inv_std)


def normalize_back(gradient, normed, inv_std):
    return inv_std * (
        gradient
        - jnp.mean(gradient, axis=-1, keepdims=True)
        - normed * jnp.mean(gradient * normed, axis=-1, keepdims=True)
    )


def times_transposed(left, right):
    return lax.dot_general(
        left, right, (((1,), (1,)), ((), ())), preferred_element_type=jnp.float32
    )


def routed_tiles(tile_counts, tile_owner, tile_slot, peer_count, capacity):
    count_table = tile_counts[0]
    before = jnp.cumsum(count_table, axis=0) - count_table
    column_ids = jnp.arange(peer_count, dtype=jnp.int32)
    own_column = column_ids == lax.axis_index("col")
    my_bases = jnp.sum(jnp.where(own_column[:, None], before, 0), axis=0)
    my_counts = jnp.sum(jnp.where(own_column[:, None], count_table, 0), axis=0)
    owner_hits = tile_owner[:, :, None] == column_ids[None, None, :]
    base = jnp.sum(jnp.where(owner_hits, my_bases[None, None, :], 0), axis=2)
    quota = jnp.sum(jnp.where(owner_hits, my_counts[None, None, :], 0), axis=2)
    rank = tile_slot - base
    return (
        (tile_owner >= 0)
        & (rank >= 0)
        & (rank < capacity)
        & (rank < quota)
        & (tile_slot < LIVE_DEV)
    )


def patch_rows(row, column, breadth):
    return pl.ds(row * breadth + column, breadth // 2, stride=2)


def mlp_forward_kernel(
    live, mixed_ref, image_ref, w_in_ref, w_out_ref, w_down_ref, summed_ref, reduced_ref, low_ref,
    *, layout
):
    normed, _ = normalize(mixed_ref[...].astype(jnp.float32))
    hidden = jnp.dot(normed.astype(jnp.bfloat16), w_in_ref[...], preferred_element_type=jnp.float32)
    cdf = 0.5 * (1.0 + lax.erf(hidden * ROOT_HALF))
    activated = (hidden * cdf).astype(jnp.bfloat16)
    branch = jnp.dot(activated, w_out_ref[...], preferred_element_type=jnp.float32)
    branch = jnp.where(pixel_live(live, layout), branch.astype(jnp.bfloat16).astype(jnp.float32), 0.0)
    summed = (image_ref[...].astype(jnp.float32) + branch).astype(jnp.bfloat16)
    summed_ref[...] = summed
    down_normed, _ = normalize(summed.astype(jnp.float32))
    low = down_normed.astype(jnp.bfloat16).astype(jnp.float32)
    for k in range(low_ref.shape[0]):
        low_ref[k] = low[:, k * 128 : (k + 1) * 128]
    breadth = layout[1]
    pair_rows = layout[0] // breadth // 2
    total = jnp.zeros(reduced_ref.shape, jnp.float32)
    for a in range(2):
        for e in range(2):
            patch = jnp.concatenate(
                [
                    jnp.concatenate(
                        [low_ref[k, patch_rows(2 * y + a, e, breadth), :] for k in range(low_ref.shape[0])],
                        axis=1,
                    )
                    for y in range(pair_rows)
                ],
                axis=0,
            )
            total = total + jnp.dot(
                patch.astype(jnp.bfloat16), w_down_ref[2 * a + e], preferred_element_type=jnp.float32
            )
    reduced_ref[...] = total.astype(jnp.bfloat16)


def mlp_backward_kernel(
    live, mixed_ref, summed_ref, cot_ref, w_in_ref, w_out_ref, w_down_ref, grad_summed_ref,
    grad_mixed_ref, grad_ref, *, layout
):
    breadth = layout[1]
    pair_rows = layout[0] // breadth // 2
    half = breadth // 2
    for a in range(2):
        for e in range(2):
            part = times_transposed(cot_ref[...], w_down_ref[2 * a + e])
            for y in range(pair_rows):
                for k in range(grad_ref.shape[0]):
                    grad_ref[k, patch_rows(2 * y + a, e, breadth), :] = part[
                        y * half : (y + 1) * half, k * 128 : (k + 1) * 128
                    ]
    normed, inv_std = normalize(mixed_ref[...].astype(jnp.float32))
    hidden = jnp.dot(normed.astype(jnp.bfloat16), w_in_ref[...], preferred_element_type=jnp.float32)
    cdf = 0.5 * (1.0 + lax.erf(hidden * ROOT_HALF))
    slope = cdf + hidden * INV_ROOT_TAU * jnp.exp(-0.5 * hidden * hidden)
    down_normed, down_inv = normalize(summed_ref[...].astype(jnp.float32))
    grad_normed = jnp.concatenate([grad_ref[k] for k in range(grad_ref.shape[0])], axis=1)
    grad_summed = normalize_back(grad_normed, down_normed, down_inv).astype(jnp.bfloat16)
    grad_summed_ref[...] = grad_summed
    grad_hidden = (times_transposed(grad_summed, w_out_ref[...]) * slope).astype(jnp.bfloat16)
    grad_norm_in = times_transposed(grad_hidden, w_in_ref[...])
    grad_owned_mixed = normalize_back(grad_norm_in, normed, inv_std)
    grad_mixed_ref[...] = jnp.where(pixel_live(live, layout), grad_owned_mixed, 0.0).astype(jnp.bfloat16)


def pixel_live(live, layout):
    block, breadth, tile_side, tile_cols = layout
    band = block // breadth // tile_side
    place = lax.broadcasted_iota(jnp.int32, (block, 1), 0)
    tile = (place // breadth // tile_side) * tile_cols + (place % breadth) // tile_side
    first = pl.program_id(0) * band * tile_cols
    flag = jnp.zeros((block, 1), jnp.int32)
    for index in range(band * tile_cols):
        flag = jnp.where(tile == index, live[first + index], flag)
    return flag > 0


def pixel_call(kernel, live, operands, kinds, outputs, layout, scratch):
    block = layout[0]
    steps = operands[0].shape[0] // block
    specs = []
    for operand, kind in zip(operands, kinds):
        if kind == "whole":
            specs.append(pl.BlockSpec(operand.shape, lambda i, live, n=operand.ndim: (0,) * n))
        else:
            rows = operand.shape[0] // steps
            specs.append(pl.BlockSpec((rows, operand.shape[1]), lambda i, live: (i, 0)))
    return pl.pallas_call(
        lambda *refs: kernel(*refs, layout=layout),
        grid_spec=pltpu.PrefetchScalarGridSpec(
            num_scalar_prefetch=1,
            grid=(steps,),
            in_specs=specs,
            out_specs=[
                pl.BlockSpec((rows // steps, width), lambda i, live: (i, 0)) for rows, width, _ in outputs
            ],
            scratch_shapes=[pltpu.VMEM((width // 128, block, 128), jnp.float32) for width in scratch],
        ),
        out_shape=[jax.ShapeDtypeStruct((rows, width), dtype) for rows, width, dtype in outputs],
    )(live, *operands)


def on_device(
    image,
    depth_kernel,
    weight_in,
    weight_out,
    weight_down,
    tissue_mask,
    tile_counts,
    tile_owner,
    tile_slot,
    cotangent,
):
    height, breadth, channels = image.shape
    tile_rows, tile_cols = tissue_mask.shape
    tile_side = height // tile_rows
    outputs = weight_down.shape[3]
    reach = KS // 2
    peer_count = lax.axis_size("col")
    capacity = tile_rows * tile_cols // peer_count
    pixels = height * breadth
    routed = routed_tiles(tile_counts, tile_owner, tile_slot, peer_count, capacity)
    live = routed & (tissue_mask != 0)
    live = live.reshape(-1).astype(jnp.int32)
    band = 4 if tile_rows % 4 == 0 else 1
    layout = (band * tile_side * breadth, breadth, tile_side, tile_cols)
    taps = depth_kernel.reshape(KS * KS, channels).astype(jnp.float32)
    mixed = depthwise(halo_pieces(image, reach), taps, reach)
    mixed = mixed.reshape(pixels, channels)
    weight_quad = weight_down.reshape(4, channels, outputs)
    patches = pixels // 4
    summed, reduced = pixel_call(
        mlp_forward_kernel,
        live,
        (mixed, image.reshape(pixels, channels), weight_in, weight_out, weight_quad),
        ("rows", "rows", "whole", "whole", "whole"),
        ((pixels, channels, jnp.bfloat16), (patches, outputs, jnp.bfloat16)),
        layout,
        (channels,),
    )
    reduced = reduced.reshape(height // 2, breadth // 2, outputs)
    grad_summed, grad_mixed = pixel_call(
        mlp_backward_kernel,
        live,
        (mixed, summed, cotangent.reshape(patches, outputs), weight_in, weight_out, weight_quad),
        ("rows", "rows", "rows", "whole", "whole", "whole"),
        ((pixels, channels, jnp.bfloat16), (pixels, channels, jnp.bfloat16)),
        layout,
        (channels,),
    )
    grad_image = depthwise(
        halo_pieces(grad_mixed.reshape(height, breadth, channels), reach),
        taps,
        reach,
        base=grad_summed.reshape(height, breadth, channels),
        flip=True,
    )
    return (reduced, grad_image)


def solution(mesh):
    in_specs = (
        P("row", "col", None),
        P(),
        P(),
        P(),
        P(),
        P("row", "col"),
        P("row", None, None),
        P("row", "col"),
        P("row", "col"),
        P("row", "col", None),
    )
    out_specs = (P("row", "col", None), P("row", "col", None))
    return jax.shard_map(
        on_device, mesh=mesh, in_specs=in_specs, out_specs=out_specs, check_vma=False
    )
```

```python
import jax
import jax.numpy as jnp
from jax import lax
from jax.sharding import PartitionSpec as P
from jax.experimental import pallas as pl
from jax.experimental.pallas import tpu as pltpu

KS = 7
LIVE_DEV = 18


EPSILON = 1e-06
ROOT_HALF = 0.7071067811865476
INV_ROOT_TAU = 0.3989422804014327


def halo_pieces(cells, width):
    rows = lax.axis_size("row")
    cols = lax.axis_size("col")
    down = [(i, i + 1) for i in range(rows - 1)]
    up = [(i + 1, i) for i in range(rows - 1)]
    top = lax.ppermute(cells[cells.shape[0] - width :], "row", down)
    bottom = lax.ppermute(cells[:width], "row", up)
    framed = jnp.concatenate([top, cells, bottom], axis=0)
    left = lax.ppermute(framed[:, cells.shape[1] - width :], "col", [(i, i + 1) for i in range(cols - 1)])
    right = lax.ppermute(framed[:, :width], "col", [(i + 1, i) for i in range(cols - 1)])
    return (cells, top, bottom, left, right)


def depthwise_kernel(
    image_ref, top_ref, bottom_ref, left_ref, right_ref, k_ref, *rest, reach, chunk, flip
):
    if len(rest) == 5:
        base_ref, out_ref, framed_ref, shifted_ref, total_ref = rest
    else:
        base_ref = None
        out_ref, framed_ref, shifted_ref, total_ref = rest
    height, breadth, _ = out_ref.shape
    side = 2 * reach + 1
    framed_ref[reach : reach + height, reach : reach + breadth, :] = image_ref[...].astype(jnp.float32)
    framed_ref[:reach, reach : reach + breadth, :] = top_ref[...].astype(jnp.float32)
    framed_ref[reach + height :, reach : reach + breadth, :] = bottom_ref[...].astype(jnp.float32)
    framed_ref[:, :reach, :] = left_ref[...].astype(jnp.float32)
    framed_ref[:, reach + breadth :, :] = right_ref[...].astype(jnp.float32)
    for shift_c in range(side):
        shifted_ref[...] = framed_ref[:, shift_c : shift_c + breadth, :]

        def body(step, carry, shift_c=shift_c):
            start = pl.multiple_of(step * chunk, chunk)
            if shift_c > 0:
                total = total_ref[pl.ds(start, chunk)]
            elif base_ref is not None:
                total = base_ref[pl.ds(start, chunk)].astype(jnp.float32)
            else:
                total = jnp.zeros((chunk, breadth, out_ref.shape[2]), jnp.float32)
            for shift_r in range(side):
                if flip:
                    index = (side - 1 - shift_r) * side + (side - 1 - shift_c)
                else:
                    index = shift_r * side + shift_c
                tap = k_ref[pl.ds(index, 1), :]
                total = total + shifted_ref[pl.ds(start + shift_r, chunk)] * tap[None]
            if shift_c == side - 1:
                out_ref[pl.ds(start, chunk)] = total.astype(out_ref.dtype)
            else:
                total_ref[pl.ds(start, chunk)] = total
            return carry

        lax.fori_loop(0, height // chunk, body, 0, unroll=2)


def depthwise(pieces, taps, reach, base=None, flip=False, lanes=128, chunk=8):
    image = pieces[0]
    height, breadth, channels = image.shape
    framed = (height + 2 * reach, breadth + 2 * reach)
    in_specs = [
        pl.BlockSpec((height, breadth, lanes), lambda c: (0, 0, c)),
        pl.BlockSpec((reach, breadth, lanes), lambda c: (0, 0, c)),
        pl.BlockSpec((reach, breadth, lanes), lambda c: (0, 0, c)),
        pl.BlockSpec((framed[0], reach, lanes), lambda c: (0, 0, c)),
        pl.BlockSpec((framed[0], reach, lanes), lambda c: (0, 0, c)),
        pl.BlockSpec((taps.shape[0], lanes), lambda c: (0, c)),
    ]
    operands = list(pieces) + [taps]
    if base is not None:
        in_specs.append(pl.BlockSpec((height, breadth, lanes), lambda c: (0, 0, c)))
        operands.append(base)
    return pl.pallas_call(
        lambda *refs: depthwise_kernel(*refs, reach=reach, chunk=chunk, flip=flip),
        grid=(channels // lanes,),
        in_specs=in_specs,
        out_specs=pl.BlockSpec((height, breadth, lanes), lambda c: (0, 0, c)),
        out_shape=jax.ShapeDtypeStruct((height, breadth, channels), jnp.bfloat16),
        scratch_shapes=[
            pltpu.VMEM((framed[0], framed[1], lanes), jnp.float32),
            pltpu.VMEM((framed[0], breadth, lanes), jnp.float32),
            pltpu.VMEM((height, breadth, lanes), jnp.float32),
        ],
    )(*operands)


def normalize(values):
    average = jnp.mean(values, axis=-1, keepdims=True)
    centered = values - average
    inv_std = lax.rsqrt(jnp.mean(centered * centered, axis=-1, keepdims=True) + EPSILON)
    return (centered * inv_std, inv_std)


def normalize_back(gradient, normed, inv_std):
    return inv_std * (
        gradient
        - jnp.mean(gradient, axis=-1, keepdims=True)
        - normed * jnp.mean(gradient * normed, axis=-1, keepdims=True)
    )


def times_transposed(left, right):
    return lax.dot_general(
        left, right, (((1,), (1,)), ((), ())), preferred_element_type=jnp.float32
    )


def routed_tiles(tile_counts, tile_owner, tile_slot, peer_count, capacity):
    count_table = tile_counts[0]
    before = jnp.cumsum(count_table, axis=0) - count_table
    column_ids = jnp.arange(peer_count, dtype=jnp.int32)
    own_column = column_ids == lax.axis_index("col")
    my_bases = jnp.sum(jnp.where(own_column[:, None], before, 0), axis=0)
    my_counts = jnp.sum(jnp.where(own_column[:, None], count_table, 0), axis=0)
    owner_hits = tile_owner[:, :, None] == column_ids[None, None, :]
    base = jnp.sum(jnp.where(owner_hits, my_bases[None, None, :], 0), axis=2)
    quota = jnp.sum(jnp.where(owner_hits, my_counts[None, None, :], 0), axis=2)
    rank = tile_slot - base
    return (
        (tile_owner >= 0)
        & (rank >= 0)
        & (rank < capacity)
        & (rank < quota)
        & (tile_slot < LIVE_DEV)
    )


def patch_rows(row, column, breadth):
    return pl.ds(row * breadth + column, breadth // 2, stride=2)


def mlp_forward_kernel(
    live, mixed_ref, image_ref, w_in_ref, w_out_ref, w_down_ref, summed_ref, reduced_ref, low_ref,
    *, layout
):
    normed, _ = normalize(mixed_ref[...].astype(jnp.float32))
    hidden = jnp.dot(normed.astype(jnp.bfloat16), w_in_ref[...], preferred_element_type=jnp.float32)
    cdf = 0.5 * (1.0 + lax.erf(hidden * ROOT_HALF))
    activated = (hidden * cdf).astype(jnp.bfloat16)
    branch = jnp.dot(activated, w_out_ref[...], preferred_element_type=jnp.float32)
    branch = jnp.where(pixel_live(live, layout), branch.astype(jnp.bfloat16).astype(jnp.float32), 0.0)
    summed = (image_ref[...].astype(jnp.float32) + branch).astype(jnp.bfloat16)
    summed_ref[...] = summed
    down_normed, _ = normalize(summed.astype(jnp.float32))
    low = down_normed.astype(jnp.bfloat16).astype(jnp.float32)
    for k in range(low_ref.shape[0]):
        low_ref[k] = low[:, k * 128 : (k + 1) * 128]
    breadth = layout[1]
    pair_rows = layout[0] // breadth // 2
    total = jnp.zeros(reduced_ref.shape, jnp.float32)
    for a in range(2):
        for e in range(2):
            patch = jnp.concatenate(
                [
                    jnp.concatenate(
                        [low_ref[k, patch_rows(2 * y + a, e, breadth), :] for k in range(low_ref.shape[0])],
                        axis=1,
                    )
                    for y in range(pair_rows)
                ],
                axis=0,
            )
            total = total + jnp.dot(
                patch.astype(jnp.bfloat16), w_down_ref[2 * a + e], preferred_element_type=jnp.float32
            )
    reduced_ref[...] = total.astype(jnp.bfloat16)


def mlp_backward_kernel(
    live, mixed_ref, summed_ref, cot_ref, w_in_ref, w_out_ref, w_down_ref, grad_summed_ref,
    grad_mixed_ref, grad_ref, *, layout
):
    breadth = layout[1]
    pair_rows = layout[0] // breadth // 2
    half = breadth // 2
    for a in range(2):
        for e in range(2):
            part = times_transposed(cot_ref[...], w_down_ref[2 * a + e])
            for y in range(pair_rows):
                for k in range(grad_ref.shape[0]):
                    grad_ref[k, patch_rows(2 * y + a, e, breadth), :] = part[
                        y * half : (y + 1) * half, k * 128 : (k + 1) * 128
                    ]
    normed, inv_std = normalize(mixed_ref[...].astype(jnp.float32))
    hidden = jnp.dot(normed.astype(jnp.bfloat16), w_in_ref[...], preferred_element_type=jnp.float32)
    cdf = 0.5 * (1.0 + lax.erf(hidden * ROOT_HALF))
    slope = cdf + hidden * INV_ROOT_TAU * jnp.exp(-0.5 * hidden * hidden)
    down_normed, down_inv = normalize(summed_ref[...].astype(jnp.float32))
    grad_normed = jnp.concatenate([grad_ref[k] for k in range(grad_ref.shape[0])], axis=1)
    grad_summed = normalize_back(grad_normed, down_normed, down_inv).astype(jnp.bfloat16)
    grad_summed_ref[...] = grad_summed
    grad_hidden = (times_transposed(grad_summed, w_out_ref[...]) * slope).astype(jnp.bfloat16)
    grad_norm_in = times_transposed(grad_hidden, w_in_ref[...])
    grad_owned_mixed = normalize_back(grad_norm_in, normed, inv_std)
    grad_mixed_ref[...] = jnp.where(pixel_live(live, layout), grad_owned_mixed, 0.0).astype(jnp.bfloat16)


def pixel_live(live, layout):
    block, breadth, tile_side, tile_cols = layout
    band = block // breadth // tile_side
    place = lax.broadcasted_iota(jnp.int32, (block, 1), 0)
    tile = (place // breadth // tile_side) * tile_cols + (place % breadth) // tile_side
    first = pl.program_id(0) * band * tile_cols
    flag = jnp.zeros((block, 1), jnp.int32)
    for index in range(band * tile_cols):
        flag = jnp.where(tile == index, live[first + index], flag)
    return flag > 0


def pixel_call(kernel, live, operands, kinds, outputs, layout, scratch):
    block = layout[0]
    steps = operands[0].shape[0] // block
    specs = []
    for operand, kind in zip(operands, kinds):
        if kind == "whole":
            specs.append(pl.BlockSpec(operand.shape, lambda i, live, n=operand.ndim: (0,) * n))
        else:
            rows = operand.shape[0] // steps
            specs.append(pl.BlockSpec((rows, operand.shape[1]), lambda i, live: (i, 0)))
    return pl.pallas_call(
        lambda *refs: kernel(*refs, layout=layout),
        grid_spec=pltpu.PrefetchScalarGridSpec(
            num_scalar_prefetch=1,
            grid=(steps,),
            in_specs=specs,
            out_specs=[
                pl.BlockSpec((rows // steps, width), lambda i, live: (i, 0)) for rows, width, _ in outputs
            ],
            scratch_shapes=[pltpu.VMEM((width // 128, block, 128), jnp.float32) for width in scratch],
        ),
        out_shape=[jax.ShapeDtypeStruct((rows, width), dtype) for rows, width, dtype in outputs],
    )(live, *operands)


def on_device(
    image,
    depth_kernel,
    weight_in,
    weight_out,
    weight_down,
    tissue_mask,
    tile_counts,
    tile_owner,
    tile_slot,
    cotangent,
):
    height, breadth, channels = image.shape
    tile_rows, tile_cols = tissue_mask.shape
    tile_side = height // tile_rows
    outputs = weight_down.shape[3]
    reach = KS // 2
    peer_count = lax.axis_size("col")
    capacity = tile_rows * tile_cols // peer_count
    pixels = height * breadth
    routed = routed_tiles(tile_counts, tile_owner, tile_slot, peer_count, capacity)
    live = routed & (tissue_mask != 0)
    live = live.reshape(-1).astype(jnp.int32)
    band = 2 if tile_rows % 2 == 0 else 1
    layout = (band * tile_side * breadth, breadth, tile_side, tile_cols)
    taps = depth_kernel.reshape(KS * KS, channels).astype(jnp.float32)
    mixed = depthwise(halo_pieces(image, reach), taps, reach)
    mixed = mixed.reshape(pixels, channels)
    weight_quad = weight_down.reshape(4, channels, outputs)
    patches = pixels // 4
    summed, reduced = pixel_call(
        mlp_forward_kernel,
        live,
        (mixed, image.reshape(pixels, channels), weight_in, weight_out, weight_quad),
        ("rows", "rows", "whole", "whole", "whole"),
        ((pixels, channels, jnp.bfloat16), (patches, outputs, jnp.bfloat16)),
        layout,
        (channels,),
    )
    reduced = reduced.reshape(height // 2, breadth // 2, outputs)
    grad_summed, grad_mixed = pixel_call(
        mlp_backward_kernel,
        live,
        (mixed, summed, cotangent.reshape(patches, outputs), weight_in, weight_out, weight_quad),
        ("rows", "rows", "rows", "whole", "whole", "whole"),
        ((pixels, channels, jnp.bfloat16), (pixels, channels, jnp.bfloat16)),
        layout,
        (channels,),
    )
    grad_image = depthwise(
        halo_pieces(grad_mixed.reshape(height, breadth, channels), reach),
        taps,
        reach,
        base=grad_summed.reshape(height, breadth, channels),
        flip=True,
    )
    return (reduced, grad_image)


def solution(mesh):
    in_specs = (
        P("row", "col", None),
        P(),
        P(),
        P(),
        P(),
        P("row", "col"),
        P("row", None, None),
        P("row", "col"),
        P("row", "col"),
        P("row", "col", None),
    )
    out_specs = (P("row", "col", None), P("row", "col", None))
    return jax.shard_map(
        on_device, mesh=mesh, in_specs=in_specs, out_specs=out_specs, check_vma=False
    )
```

```python
import jax
import jax.numpy as jnp
from jax import lax
from jax.sharding import PartitionSpec as P
from jax.experimental import pallas as pl
from jax.experimental.pallas import tpu as pltpu

KS = 7
LIVE_DEV = 18


EPSILON = 1e-06
ROOT_HALF = 0.7071067811865476
INV_ROOT_TAU = 0.3989422804014327


def halo_pieces(cells, width):
    rows = lax.axis_size("row")
    cols = lax.axis_size("col")
    down = [(i, i + 1) for i in range(rows - 1)]
    up = [(i + 1, i) for i in range(rows - 1)]
    top = lax.ppermute(cells[cells.shape[0] - width :], "row", down)
    bottom = lax.ppermute(cells[:width], "row", up)
    framed = jnp.concatenate([top, cells, bottom], axis=0)
    left = lax.ppermute(framed[:, cells.shape[1] - width :], "col", [(i, i + 1) for i in range(cols - 1)])
    right = lax.ppermute(framed[:, :width], "col", [(i + 1, i) for i in range(cols - 1)])
    return (cells, top, bottom, left, right)


def depthwise_kernel(
    image_ref, top_ref, bottom_ref, left_ref, right_ref, k_ref, *rest, reach, chunk, flip
):
    if len(rest) == 5:
        base_ref, out_ref, framed_ref, shifted_ref, total_ref = rest
    else:
        base_ref = None
        out_ref, framed_ref, shifted_ref, total_ref = rest
    height, breadth, _ = out_ref.shape
    side = 2 * reach + 1
    framed_ref[reach : reach + height, reach : reach + breadth, :] = image_ref[...].astype(jnp.float32)
    framed_ref[:reach, reach : reach + breadth, :] = top_ref[...].astype(jnp.float32)
    framed_ref[reach + height :, reach : reach + breadth, :] = bottom_ref[...].astype(jnp.float32)
    framed_ref[:, :reach, :] = left_ref[...].astype(jnp.float32)
    framed_ref[:, reach + breadth :, :] = right_ref[...].astype(jnp.float32)
    for shift_c in range(side):
        shifted_ref[...] = framed_ref[:, shift_c : shift_c + breadth, :]

        def body(step, carry, shift_c=shift_c):
            start = pl.multiple_of(step * chunk, chunk)
            if shift_c > 0:
                total = total_ref[pl.ds(start, chunk)]
            elif base_ref is not None:
                total = base_ref[pl.ds(start, chunk)].astype(jnp.float32)
            else:
                total = jnp.zeros((chunk, breadth, out_ref.shape[2]), jnp.float32)
            for shift_r in range(side):
                if flip:
                    index = (side - 1 - shift_r) * side + (side - 1 - shift_c)
                else:
                    index = shift_r * side + shift_c
                tap = k_ref[pl.ds(index, 1), :]
                total = total + shifted_ref[pl.ds(start + shift_r, chunk)] * tap[None]
            if shift_c == side - 1:
                out_ref[pl.ds(start, chunk)] = total.astype(out_ref.dtype)
            else:
                total_ref[pl.ds(start, chunk)] = total
            return carry

        lax.fori_loop(0, height // chunk, body, 0, unroll=4)


def depthwise(pieces, taps, reach, base=None, flip=False, lanes=128, chunk=8):
    image = pieces[0]
    height, breadth, channels = image.shape
    framed = (height + 2 * reach, breadth + 2 * reach)
    in_specs = [
        pl.BlockSpec((height, breadth, lanes), lambda c: (0, 0, c)),
        pl.BlockSpec((reach, breadth, lanes), lambda c: (0, 0, c)),
        pl.BlockSpec((reach, breadth, lanes), lambda c: (0, 0, c)),
        pl.BlockSpec((framed[0], reach, lanes), lambda c: (0, 0, c)),
        pl.BlockSpec((framed[0], reach, lanes), lambda c: (0, 0, c)),
        pl.BlockSpec((taps.shape[0], lanes), lambda c: (0, c)),
    ]
    operands = list(pieces) + [taps]
    if base is not None:
        in_specs.append(pl.BlockSpec((height, breadth, lanes), lambda c: (0, 0, c)))
        operands.append(base)
    return pl.pallas_call(
        lambda *refs: depthwise_kernel(*refs, reach=reach, chunk=chunk, flip=flip),
        grid=(channels // lanes,),
        in_specs=in_specs,
        out_specs=pl.BlockSpec((height, breadth, lanes), lambda c: (0, 0, c)),
        out_shape=jax.ShapeDtypeStruct((height, breadth, channels), jnp.bfloat16),
        scratch_shapes=[
            pltpu.VMEM((framed[0], framed[1], lanes), jnp.float32),
            pltpu.VMEM((framed[0], breadth, lanes), jnp.float32),
            pltpu.VMEM((height, breadth, lanes), jnp.float32),
        ],
    )(*operands)


def normalize(values):
    average = jnp.mean(values, axis=-1, keepdims=True)
    centered = values - average
    inv_std = lax.rsqrt(jnp.mean(centered * centered, axis=-1, keepdims=True) + EPSILON)
    return (centered * inv_std, inv_std)


def normalize_back(gradient, normed, inv_std):
    return inv_std * (
        gradient
        - jnp.mean(gradient, axis=-1, keepdims=True)
        - normed * jnp.mean(gradient * normed, axis=-1, keepdims=True)
    )


def times_transposed(left, right):
    return lax.dot_general(
        left, right, (((1,), (1,)), ((), ())), preferred_element_type=jnp.float32
    )


def routed_tiles(tile_counts, tile_owner, tile_slot, peer_count, capacity):
    count_table = tile_counts[0]
    before = jnp.cumsum(count_table, axis=0) - count_table
    column_ids = jnp.arange(peer_count, dtype=jnp.int32)
    own_column = column_ids == lax.axis_index("col")
    my_bases = jnp.sum(jnp.where(own_column[:, None], before, 0), axis=0)
    my_counts = jnp.sum(jnp.where(own_column[:, None], count_table, 0), axis=0)
    owner_hits = tile_owner[:, :, None] == column_ids[None, None, :]
    base = jnp.sum(jnp.where(owner_hits, my_bases[None, None, :], 0), axis=2)
    quota = jnp.sum(jnp.where(owner_hits, my_counts[None, None, :], 0), axis=2)
    rank = tile_slot - base
    return (
        (tile_owner >= 0)
        & (rank >= 0)
        & (rank < capacity)
        & (rank < quota)
        & (tile_slot < LIVE_DEV)
    )


def patch_rows(row, column, breadth):
    return pl.ds(row * breadth + column, breadth // 2, stride=2)


def mlp_forward_kernel(
    live, mixed_ref, image_ref, w_in_ref, w_out_ref, w_down_ref, summed_ref, reduced_ref, low_ref,
    *, layout
):
    normed, _ = normalize(mixed_ref[...].astype(jnp.float32))
    hidden = jnp.dot(normed.astype(jnp.bfloat16), w_in_ref[...], preferred_element_type=jnp.float32)
    cdf = 0.5 * (1.0 + lax.erf(hidden * ROOT_HALF))
    activated = (hidden * cdf).astype(jnp.bfloat16)
    branch = jnp.dot(activated, w_out_ref[...], preferred_element_type=jnp.float32)
    branch = jnp.where(pixel_live(live, layout), branch.astype(jnp.bfloat16).astype(jnp.float32), 0.0)
    summed = (image_ref[...].astype(jnp.float32) + branch).astype(jnp.bfloat16)
    summed_ref[...] = summed
    down_normed, _ = normalize(summed.astype(jnp.float32))
    low = down_normed.astype(jnp.bfloat16).astype(jnp.float32)
    for k in range(low_ref.shape[0]):
        low_ref[k] = low[:, k * 128 : (k + 1) * 128]
    breadth = layout[1]
    pair_rows = layout[0] // breadth // 2
    total = jnp.zeros(reduced_ref.shape, jnp.float32)
    for a in range(2):
        for e in range(2):
            patch = jnp.concatenate(
                [
                    jnp.concatenate(
                        [low_ref[k, patch_rows(2 * y + a, e, breadth), :] for k in range(low_ref.shape[0])],
                        axis=1,
                    )
                    for y in range(pair_rows)
                ],
                axis=0,
            )
            total = total + jnp.dot(
                patch.astype(jnp.bfloat16), w_down_ref[2 * a + e], preferred_element_type=jnp.float32
            )
    reduced_ref[...] = total.astype(jnp.bfloat16)


def mlp_backward_kernel(
    live, mixed_ref, summed_ref, cot_ref, w_in_ref, w_out_ref, w_down_ref, grad_summed_ref,
    grad_mixed_ref, grad_ref, *, layout
):
    breadth = layout[1]
    pair_rows = layout[0] // breadth // 2
    half = breadth // 2
    for a in range(2):
        for e in range(2):
            part = times_transposed(cot_ref[...], w_down_ref[2 * a + e])
            for y in range(pair_rows):
                for k in range(grad_ref.shape[0]):
                    grad_ref[k, patch_rows(2 * y + a, e, breadth), :] = part[
                        y * half : (y + 1) * half, k * 128 : (k + 1) * 128
                    ]
    normed, inv_std = normalize(mixed_ref[...].astype(jnp.float32))
    hidden = jnp.dot(normed.astype(jnp.bfloat16), w_in_ref[...], preferred_element_type=jnp.float32)
    cdf = 0.5 * (1.0 + lax.erf(hidden * ROOT_HALF))
    slope = cdf + hidden * INV_ROOT_TAU * jnp.exp(-0.5 * hidden * hidden)
    down_normed, down_inv = normalize(summed_ref[...].astype(jnp.float32))
    grad_normed = jnp.concatenate([grad_ref[k] for k in range(grad_ref.shape[0])], axis=1)
    grad_summed = normalize_back(grad_normed, down_normed, down_inv).astype(jnp.bfloat16)
    grad_summed_ref[...] = grad_summed
    grad_hidden = (times_transposed(grad_summed, w_out_ref[...]) * slope).astype(jnp.bfloat16)
    grad_norm_in = times_transposed(grad_hidden, w_in_ref[...])
    grad_owned_mixed = normalize_back(grad_norm_in, normed, inv_std)
    grad_mixed_ref[...] = jnp.where(pixel_live(live, layout), grad_owned_mixed, 0.0).astype(jnp.bfloat16)


def pixel_live(live, layout):
    block, breadth, tile_side, tile_cols = layout
    band = block // breadth // tile_side
    place = lax.broadcasted_iota(jnp.int32, (block, 1), 0)
    tile = (place // breadth // tile_side) * tile_cols + (place % breadth) // tile_side
    first = pl.program_id(0) * band * tile_cols
    flag = jnp.zeros((block, 1), jnp.int32)
    for index in range(band * tile_cols):
        flag = jnp.where(tile == index, live[first + index], flag)
    return flag > 0


def pixel_call(kernel, live, operands, kinds, outputs, layout, scratch):
    block = layout[0]
    steps = operands[0].shape[0] // block
    specs = []
    for operand, kind in zip(operands, kinds):
        if kind == "whole":
            specs.append(pl.BlockSpec(operand.shape, lambda i, live, n=operand.ndim: (0,) * n))
        else:
            rows = operand.shape[0] // steps
            specs.append(pl.BlockSpec((rows, operand.shape[1]), lambda i, live: (i, 0)))
    return pl.pallas_call(
        lambda *refs: kernel(*refs, layout=layout),
        grid_spec=pltpu.PrefetchScalarGridSpec(
            num_scalar_prefetch=1,
            grid=(steps,),
            in_specs=specs,
            out_specs=[
                pl.BlockSpec((rows // steps, width), lambda i, live: (i, 0)) for rows, width, _ in outputs
            ],
            scratch_shapes=[pltpu.VMEM((width // 128, block, 128), jnp.float32) for width in scratch],
        ),
        out_shape=[jax.ShapeDtypeStruct((rows, width), dtype) for rows, width, dtype in outputs],
    )(live, *operands)


def on_device(
    image,
    depth_kernel,
    weight_in,
    weight_out,
    weight_down,
    tissue_mask,
    tile_counts,
    tile_owner,
    tile_slot,
    cotangent,
):
    height, breadth, channels = image.shape
    tile_rows, tile_cols = tissue_mask.shape
    tile_side = height // tile_rows
    outputs = weight_down.shape[3]
    reach = KS // 2
    peer_count = lax.axis_size("col")
    capacity = tile_rows * tile_cols // peer_count
    pixels = height * breadth
    routed = routed_tiles(tile_counts, tile_owner, tile_slot, peer_count, capacity)
    live = routed & (tissue_mask != 0)
    live = live.reshape(-1).astype(jnp.int32)
    band = 2 if tile_rows % 2 == 0 else 1
    layout = (band * tile_side * breadth, breadth, tile_side, tile_cols)
    taps = depth_kernel.reshape(KS * KS, channels).astype(jnp.float32)
    mixed = depthwise(halo_pieces(image, reach), taps, reach)
    mixed = mixed.reshape(pixels, channels)
    weight_quad = weight_down.reshape(4, channels, outputs)
    patches = pixels // 4
    summed, reduced = pixel_call(
        mlp_forward_kernel,
        live,
        (mixed, image.reshape(pixels, channels), weight_in, weight_out, weight_quad),
        ("rows", "rows", "whole", "whole", "whole"),
        ((pixels, channels, jnp.bfloat16), (patches, outputs, jnp.bfloat16)),
        layout,
        (channels,),
    )
    reduced = reduced.reshape(height // 2, breadth // 2, outputs)
    grad_summed, grad_mixed = pixel_call(
        mlp_backward_kernel,
        live,
        (mixed, summed, cotangent.reshape(patches, outputs), weight_in, weight_out, weight_quad),
        ("rows", "rows", "rows", "whole", "whole", "whole"),
        ((pixels, channels, jnp.bfloat16), (pixels, channels, jnp.bfloat16)),
        layout,
        (channels,),
    )
    grad_image = depthwise(
        halo_pieces(grad_mixed.reshape(height, breadth, channels), reach),
        taps,
        reach,
        base=grad_summed.reshape(height, breadth, channels),
        flip=True,
    )
    return (reduced, grad_image)


def solution(mesh):
    in_specs = (
        P("row", "col", None),
        P(),
        P(),
        P(),
        P(),
        P("row", "col"),
        P("row", None, None),
        P("row", "col"),
        P("row", "col"),
        P("row", "col", None),
    )
    out_specs = (P("row", "col", None), P("row", "col", None))
    return jax.shard_map(
        on_device, mesh=mesh, in_specs=in_specs, out_specs=out_specs, check_vma=False
    )
```

```python
import jax
import jax.numpy as jnp
from jax import lax
from jax.sharding import PartitionSpec as P
from jax.experimental import pallas as pl
from jax.experimental.pallas import tpu as pltpu

KS = 7
LIVE_DEV = 18


EPSILON = 1e-06
ROOT_HALF = 0.7071067811865476
INV_ROOT_TAU = 0.3989422804014327


def halo_pieces(cells, width):
    rows = lax.axis_size("row")
    cols = lax.axis_size("col")
    down = [(i, i + 1) for i in range(rows - 1)]
    up = [(i + 1, i) for i in range(rows - 1)]
    top = lax.ppermute(cells[cells.shape[0] - width :], "row", down)
    bottom = lax.ppermute(cells[:width], "row", up)
    framed = jnp.concatenate([top, cells, bottom], axis=0)
    left = lax.ppermute(framed[:, cells.shape[1] - width :], "col", [(i, i + 1) for i in range(cols - 1)])
    right = lax.ppermute(framed[:, :width], "col", [(i + 1, i) for i in range(cols - 1)])
    return (cells, top, bottom, left, right)


def depthwise_kernel(
    image_ref, top_ref, bottom_ref, left_ref, right_ref, k_ref, *rest, reach, chunk, flip
):
    if len(rest) == 5:
        base_ref, out_ref, framed_ref, shifted_ref, total_ref = rest
    else:
        base_ref = None
        out_ref, framed_ref, shifted_ref, total_ref = rest
    height, breadth, _ = out_ref.shape
    side = 2 * reach + 1
    framed_ref[reach : reach + height, reach : reach + breadth, :] = image_ref[...].astype(jnp.float32)
    framed_ref[:reach, reach : reach + breadth, :] = top_ref[...].astype(jnp.float32)
    framed_ref[reach + height :, reach : reach + breadth, :] = bottom_ref[...].astype(jnp.float32)
    framed_ref[:, :reach, :] = left_ref[...].astype(jnp.float32)
    framed_ref[:, reach + breadth :, :] = right_ref[...].astype(jnp.float32)
    for shift_c in range(side):
        shifted_ref[...] = framed_ref[:, shift_c : shift_c + breadth, :]

        def body(step, carry, shift_c=shift_c):
            start = pl.multiple_of(step * chunk, chunk)
            if shift_c > 0:
                total = total_ref[pl.ds(start, chunk)]
            elif base_ref is not None:
                total = base_ref[pl.ds(start, chunk)].astype(jnp.float32)
            else:
                total = jnp.zeros((chunk, breadth, out_ref.shape[2]), jnp.float32)
            for shift_r in range(side):
                if flip:
                    index = (side - 1 - shift_r) * side + (side - 1 - shift_c)
                else:
                    index = shift_r * side + shift_c
                tap = k_ref[pl.ds(index, 1), :]
                total = total + shifted_ref[pl.ds(start + shift_r, chunk)] * tap[None]
            if shift_c == side - 1:
                out_ref[pl.ds(start, chunk)] = total.astype(out_ref.dtype)
            else:
                total_ref[pl.ds(start, chunk)] = total
            return carry

        lax.fori_loop(0, height // chunk, body, 0, unroll=True)


def depthwise(pieces, taps, reach, base=None, flip=False, lanes=128, chunk=8):
    image = pieces[0]
    height, breadth, channels = image.shape
    framed = (height + 2 * reach, breadth + 2 * reach)
    in_specs = [
        pl.BlockSpec((height, breadth, lanes), lambda c: (0, 0, c)),
        pl.BlockSpec((reach, breadth, lanes), lambda c: (0, 0, c)),
        pl.BlockSpec((reach, breadth, lanes), lambda c: (0, 0, c)),
        pl.BlockSpec((framed[0], reach, lanes), lambda c: (0, 0, c)),
        pl.BlockSpec((framed[0], reach, lanes), lambda c: (0, 0, c)),
        pl.BlockSpec((taps.shape[0], lanes), lambda c: (0, c)),
    ]
    operands = list(pieces) + [taps]
    if base is not None:
        in_specs.append(pl.BlockSpec((height, breadth, lanes), lambda c: (0, 0, c)))
        operands.append(base)
    return pl.pallas_call(
        lambda *refs: depthwise_kernel(*refs, reach=reach, chunk=chunk, flip=flip),
        grid=(channels // lanes,),
        in_specs=in_specs,
        out_specs=pl.BlockSpec((height, breadth, lanes), lambda c: (0, 0, c)),
        out_shape=jax.ShapeDtypeStruct((height, breadth, channels), jnp.bfloat16),
        scratch_shapes=[
            pltpu.VMEM((framed[0], framed[1], lanes), jnp.float32),
            pltpu.VMEM((framed[0], breadth, lanes), jnp.float32),
            pltpu.VMEM((height, breadth, lanes), jnp.float32),
        ],
    )(*operands)


def normalize(values):
    average = jnp.mean(values, axis=-1, keepdims=True)
    centered = values - average
    inv_std = lax.rsqrt(jnp.mean(centered * centered, axis=-1, keepdims=True) + EPSILON)
    return (centered * inv_std, inv_std)


def normalize_back(gradient, normed, inv_std):
    return inv_std * (
        gradient
        - jnp.mean(gradient, axis=-1, keepdims=True)
        - normed * jnp.mean(gradient * normed, axis=-1, keepdims=True)
    )


def times_transposed(left, right):
    return lax.dot_general(
        left, right, (((1,), (1,)), ((), ())), preferred_element_type=jnp.float32
    )


def routed_tiles(tile_counts, tile_owner, tile_slot, peer_count, capacity):
    count_table = tile_counts[0]
    before = jnp.cumsum(count_table, axis=0) - count_table
    column_ids = jnp.arange(peer_count, dtype=jnp.int32)
    own_column = column_ids == lax.axis_index("col")
    my_bases = jnp.sum(jnp.where(own_column[:, None], before, 0), axis=0)
    my_counts = jnp.sum(jnp.where(own_column[:, None], count_table, 0), axis=0)
    owner_hits = tile_owner[:, :, None] == column_ids[None, None, :]
    base = jnp.sum(jnp.where(owner_hits, my_bases[None, None, :], 0), axis=2)
    quota = jnp.sum(jnp.where(owner_hits, my_counts[None, None, :], 0), axis=2)
    rank = tile_slot - base
    return (
        (tile_owner >= 0)
        & (rank >= 0)
        & (rank < capacity)
        & (rank < quota)
        & (tile_slot < LIVE_DEV)
    )


def patch_rows(row, column, breadth):
    return pl.ds(row * breadth + column, breadth // 2, stride=2)


def mlp_forward_kernel(
    live, mixed_ref, image_ref, w_in_ref, w_out_ref, w_down_ref, summed_ref, reduced_ref, low_ref,
    *, layout
):
    normed, _ = normalize(mixed_ref[...].astype(jnp.float32))
    hidden = jnp.dot(normed.astype(jnp.bfloat16), w_in_ref[...], preferred_element_type=jnp.float32)
    cdf = 0.5 * (1.0 + lax.erf(hidden * ROOT_HALF))
    activated = (hidden * cdf).astype(jnp.bfloat16)
    branch = jnp.dot(activated, w_out_ref[...], preferred_element_type=jnp.float32)
    branch = jnp.where(pixel_live(live, layout), branch.astype(jnp.bfloat16).astype(jnp.float32), 0.0)
    summed = (image_ref[...].astype(jnp.float32) + branch).astype(jnp.bfloat16)
    summed_ref[...] = summed
    down_normed, _ = normalize(summed.astype(jnp.float32))
    low = down_normed.astype(jnp.bfloat16).astype(jnp.float32)
    for k in range(low_ref.shape[0]):
        low_ref[k] = low[:, k * 128 : (k + 1) * 128]
    breadth = layout[1]
    pair_rows = layout[0] // breadth // 2
    total = jnp.zeros(reduced_ref.shape, jnp.float32)
    for a in range(2):
        for e in range(2):
            patch = jnp.concatenate(
                [
                    jnp.concatenate(
                        [low_ref[k, patch_rows(2 * y + a, e, breadth), :] for k in range(low_ref.shape[0])],
                        axis=1,
                    )
                    for y in range(pair_rows)
                ],
                axis=0,
            )
            total = total + jnp.dot(
                patch.astype(jnp.bfloat16), w_down_ref[2 * a + e], preferred_element_type=jnp.float32
            )
    reduced_ref[...] = total.astype(jnp.bfloat16)


def mlp_backward_kernel(
    live, mixed_ref, summed_ref, cot_ref, w_in_ref, w_out_ref, w_down_ref, grad_summed_ref,
    grad_mixed_ref, grad_ref, *, layout
):
    breadth = layout[1]
    pair_rows = layout[0] // breadth // 2
    half = breadth // 2
    for a in range(2):
        for e in range(2):
            part = times_transposed(cot_ref[...], w_down_ref[2 * a + e])
            for y in range(pair_rows):
                for k in range(grad_ref.shape[0]):
                    grad_ref[k, patch_rows(2 * y + a, e, breadth), :] = part[
                        y * half : (y + 1) * half, k * 128 : (k + 1) * 128
                    ]
    normed, inv_std = normalize(mixed_ref[...].astype(jnp.float32))
    hidden = jnp.dot(normed.astype(jnp.bfloat16), w_in_ref[...], preferred_element_type=jnp.float32)
    cdf = 0.5 * (1.0 + lax.erf(hidden * ROOT_HALF))
    slope = cdf + hidden * INV_ROOT_TAU * jnp.exp(-0.5 * hidden * hidden)
    down_normed, down_inv = normalize(summed_ref[...].astype(jnp.float32))
    grad_normed = jnp.concatenate([grad_ref[k] for k in range(grad_ref.shape[0])], axis=1)
    grad_summed = normalize_back(grad_normed, down_normed, down_inv).astype(jnp.bfloat16)
    grad_summed_ref[...] = grad_summed
    grad_hidden = (times_transposed(grad_summed, w_out_ref[...]) * slope).astype(jnp.bfloat16)
    grad_norm_in = times_transposed(grad_hidden, w_in_ref[...])
    grad_owned_mixed = normalize_back(grad_norm_in, normed, inv_std)
    grad_mixed_ref[...] = jnp.where(pixel_live(live, layout), grad_owned_mixed, 0.0).astype(jnp.bfloat16)


def pixel_live(live, layout):
    block, breadth, tile_side, tile_cols = layout
    band = block // breadth // tile_side
    place = lax.broadcasted_iota(jnp.int32, (block, 1), 0)
    tile = (place // breadth // tile_side) * tile_cols + (place % breadth) // tile_side
    first = pl.program_id(0) * band * tile_cols
    flag = jnp.zeros((block, 1), jnp.int32)
    for index in range(band * tile_cols):
        flag = jnp.where(tile == index, live[first + index], flag)
    return flag > 0


def pixel_call(kernel, live, operands, kinds, outputs, layout, scratch):
    block = layout[0]
    steps = operands[0].shape[0] // block
    specs = []
    for operand, kind in zip(operands, kinds):
        if kind == "whole":
            specs.append(pl.BlockSpec(operand.shape, lambda i, live, n=operand.ndim: (0,) * n))
        else:
            rows = operand.shape[0] // steps
            specs.append(pl.BlockSpec((rows, operand.shape[1]), lambda i, live: (i, 0)))
    return pl.pallas_call(
        lambda *refs: kernel(*refs, layout=layout),
        grid_spec=pltpu.PrefetchScalarGridSpec(
            num_scalar_prefetch=1,
            grid=(steps,),
            in_specs=specs,
            out_specs=[
                pl.BlockSpec((rows // steps, width), lambda i, live: (i, 0)) for rows, width, _ in outputs
            ],
            scratch_shapes=[pltpu.VMEM((width // 128, block, 128), jnp.float32) for width in scratch],
        ),
        out_shape=[jax.ShapeDtypeStruct((rows, width), dtype) for rows, width, dtype in outputs],
    )(live, *operands)


def on_device(
    image,
    depth_kernel,
    weight_in,
    weight_out,
    weight_down,
    tissue_mask,
    tile_counts,
    tile_owner,
    tile_slot,
    cotangent,
):
    height, breadth, channels = image.shape
    tile_rows, tile_cols = tissue_mask.shape
    tile_side = height // tile_rows
    outputs = weight_down.shape[3]
    reach = KS // 2
    peer_count = lax.axis_size("col")
    capacity = tile_rows * tile_cols // peer_count
    pixels = height * breadth
    routed = routed_tiles(tile_counts, tile_owner, tile_slot, peer_count, capacity)
    live = routed & (tissue_mask != 0)
    live = live.reshape(-1).astype(jnp.int32)
    band = 2 if tile_rows % 2 == 0 else 1
    layout = (band * tile_side * breadth, breadth, tile_side, tile_cols)
    taps = depth_kernel.reshape(KS * KS, channels).astype(jnp.float32)
    mixed = depthwise(halo_pieces(image, reach), taps, reach)
    mixed = mixed.reshape(pixels, channels)
    weight_quad = weight_down.reshape(4, channels, outputs)
    patches = pixels // 4
    summed, reduced = pixel_call(
        mlp_forward_kernel,
        live,
        (mixed, image.reshape(pixels, channels), weight_in, weight_out, weight_quad),
        ("rows", "rows", "whole", "whole", "whole"),
        ((pixels, channels, jnp.bfloat16), (patches, outputs, jnp.bfloat16)),
        layout,
        (channels,),
    )
    reduced = reduced.reshape(height // 2, breadth // 2, outputs)
    grad_summed, grad_mixed = pixel_call(
        mlp_backward_kernel,
        live,
        (mixed, summed, cotangent.reshape(patches, outputs), weight_in, weight_out, weight_quad),
        ("rows", "rows", "rows", "whole", "whole", "whole"),
        ((pixels, channels, jnp.bfloat16), (pixels, channels, jnp.bfloat16)),
        layout,
        (channels,),
    )
    grad_image = depthwise(
        halo_pieces(grad_mixed.reshape(height, breadth, channels), reach),
        taps,
        reach,
        base=grad_summed.reshape(height, breadth, channels),
        flip=True,
    )
    return (reduced, grad_image)


def solution(mesh):
    in_specs = (
        P("row", "col", None),
        P(),
        P(),
        P(),
        P(),
        P("row", "col"),
        P("row", None, None),
        P("row", "col"),
        P("row", "col"),
        P("row", "col", None),
    )
    out_specs = (P("row", "col", None), P("row", "col", None))
    return jax.shard_map(
        on_device, mesh=mesh, in_specs=in_specs, out_specs=out_specs, check_vma=False
    )
```

```python
import jax
import jax.numpy as jnp
from jax import lax
from jax.sharding import PartitionSpec as P
from jax.experimental import pallas as pl
from jax.experimental.pallas import tpu as pltpu

KS = 7
LIVE_DEV = 18


EPSILON = 1e-06
ROOT_HALF = 0.7071067811865476
INV_ROOT_TAU = 0.3989422804014327


def halo_pieces(cells, width):
    rows = lax.axis_size("row")
    cols = lax.axis_size("col")
    down = [(i, i + 1) for i in range(rows - 1)]
    up = [(i + 1, i) for i in range(rows - 1)]
    top = lax.ppermute(cells[cells.shape[0] - width :], "row", down)
    bottom = lax.ppermute(cells[:width], "row", up)
    framed = jnp.concatenate([top, cells, bottom], axis=0)
    left = lax.ppermute(framed[:, cells.shape[1] - width :], "col", [(i, i + 1) for i in range(cols - 1)])
    right = lax.ppermute(framed[:, :width], "col", [(i + 1, i) for i in range(cols - 1)])
    return (cells, top, bottom, left, right)


def depthwise_kernel(
    image_ref, top_ref, bottom_ref, left_ref, right_ref, k_ref, *rest, reach, chunk, flip
):
    if len(rest) == 5:
        base_ref, out_ref, framed_ref, shifted_ref, total_ref = rest
    else:
        base_ref = None
        out_ref, framed_ref, shifted_ref, total_ref = rest
    height, breadth, _ = out_ref.shape
    side = 2 * reach + 1
    framed_ref[reach : reach + height, reach : reach + breadth, :] = image_ref[...].astype(jnp.float32)
    framed_ref[:reach, reach : reach + breadth, :] = top_ref[...].astype(jnp.float32)
    framed_ref[reach + height :, reach : reach + breadth, :] = bottom_ref[...].astype(jnp.float32)
    framed_ref[:, :reach, :] = left_ref[...].astype(jnp.float32)
    framed_ref[:, reach + breadth :, :] = right_ref[...].astype(jnp.float32)
    for shift_c in range(side):
        shifted_ref[...] = framed_ref[:, shift_c : shift_c + breadth, :]

        def body(step, carry, shift_c=shift_c):
            start = pl.multiple_of(step * chunk, chunk)
            if shift_c > 0:
                total = total_ref[pl.ds(start, chunk)]
            elif base_ref is not None:
                total = base_ref[pl.ds(start, chunk)].astype(jnp.float32)
            else:
                total = jnp.zeros((chunk, breadth, out_ref.shape[2]), jnp.float32)
            for shift_r in range(side):
                if flip:
                    index = (side - 1 - shift_r) * side + (side - 1 - shift_c)
                else:
                    index = shift_r * side + shift_c
                tap = k_ref[pl.ds(index, 1), :]
                total = total + shifted_ref[pl.ds(start + shift_r, chunk)] * tap[None]
            if shift_c == side - 1:
                out_ref[pl.ds(start, chunk)] = total.astype(out_ref.dtype)
            else:
                total_ref[pl.ds(start, chunk)] = total
            return carry

        lax.fori_loop(0, height // chunk, body, 0, unroll=4)


def depthwise(pieces, taps, reach, base=None, flip=False, lanes=128, chunk=4):
    image = pieces[0]
    height, breadth, channels = image.shape
    framed = (height + 2 * reach, breadth + 2 * reach)
    in_specs = [
        pl.BlockSpec((height, breadth, lanes), lambda c: (0, 0, c)),
        pl.BlockSpec((reach, breadth, lanes), lambda c: (0, 0, c)),
        pl.BlockSpec((reach, breadth, lanes), lambda c: (0, 0, c)),
        pl.BlockSpec((framed[0], reach, lanes), lambda c: (0, 0, c)),
        pl.BlockSpec((framed[0], reach, lanes), lambda c: (0, 0, c)),
        pl.BlockSpec((taps.shape[0], lanes), lambda c: (0, c)),
    ]
    operands = list(pieces) + [taps]
    if base is not None:
        in_specs.append(pl.BlockSpec((height, breadth, lanes), lambda c: (0, 0, c)))
        operands.append(base)
    return pl.pallas_call(
        lambda *refs: depthwise_kernel(*refs, reach=reach, chunk=chunk, flip=flip),
        grid=(channels // lanes,),
        in_specs=in_specs,
        out_specs=pl.BlockSpec((height, breadth, lanes), lambda c: (0, 0, c)),
        out_shape=jax.ShapeDtypeStruct((height, breadth, channels), jnp.bfloat16),
        scratch_shapes=[
            pltpu.VMEM((framed[0], framed[1], lanes), jnp.float32),
            pltpu.VMEM((framed[0], breadth, lanes), jnp.float32),
            pltpu.VMEM((height, breadth, lanes), jnp.float32),
        ],
    )(*operands)


def normalize(values):
    average = jnp.mean(values, axis=-1, keepdims=True)
    centered = values - average
    inv_std = lax.rsqrt(jnp.mean(centered * centered, axis=-1, keepdims=True) + EPSILON)
    return (centered * inv_std, inv_std)


def normalize_back(gradient, normed, inv_std):
    return inv_std * (
        gradient
        - jnp.mean(gradient, axis=-1, keepdims=True)
        - normed * jnp.mean(gradient * normed, axis=-1, keepdims=True)
    )


def times_transposed(left, right):
    return lax.dot_general(
        left, right, (((1,), (1,)), ((), ())), preferred_element_type=jnp.float32
    )


def routed_tiles(tile_counts, tile_owner, tile_slot, peer_count, capacity):
    count_table = tile_counts[0]
    before = jnp.cumsum(count_table, axis=0) - count_table
    column_ids = jnp.arange(peer_count, dtype=jnp.int32)
    own_column = column_ids == lax.axis_index("col")
    my_bases = jnp.sum(jnp.where(own_column[:, None], before, 0), axis=0)
    my_counts = jnp.sum(jnp.where(own_column[:, None], count_table, 0), axis=0)
    owner_hits = tile_owner[:, :, None] == column_ids[None, None, :]
    base = jnp.sum(jnp.where(owner_hits, my_bases[None, None, :], 0), axis=2)
    quota = jnp.sum(jnp.where(owner_hits, my_counts[None, None, :], 0), axis=2)
    rank = tile_slot - base
    return (
        (tile_owner >= 0)
        & (rank >= 0)
        & (rank < capacity)
        & (rank < quota)
        & (tile_slot < LIVE_DEV)
    )


def patch_rows(row, column, breadth):
    return pl.ds(row * breadth + column, breadth // 2, stride=2)


def mlp_forward_kernel(
    live, mixed_ref, image_ref, w_in_ref, w_out_ref, w_down_ref, summed_ref, reduced_ref, low_ref,
    *, layout
):
    normed, _ = normalize(mixed_ref[...].astype(jnp.float32))
    hidden = jnp.dot(normed.astype(jnp.bfloat16), w_in_ref[...], preferred_element_type=jnp.float32)
    cdf = 0.5 * (1.0 + lax.erf(hidden * ROOT_HALF))
    activated = (hidden * cdf).astype(jnp.bfloat16)
    branch = jnp.dot(activated, w_out_ref[...], preferred_element_type=jnp.float32)
    branch = jnp.where(pixel_live(live, layout), branch.astype(jnp.bfloat16).astype(jnp.float32), 0.0)
    summed = (image_ref[...].astype(jnp.float32) + branch).astype(jnp.bfloat16)
    summed_ref[...] = summed
    down_normed, _ = normalize(summed.astype(jnp.float32))
    low = down_normed.astype(jnp.bfloat16).astype(jnp.float32)
    for k in range(low_ref.shape[0]):
        low_ref[k] = low[:, k * 128 : (k + 1) * 128]
    breadth = layout[1]
    pair_rows = layout[0] // breadth // 2
    total = jnp.zeros(reduced_ref.shape, jnp.float32)
    for a in range(2):
        for e in range(2):
            patch = jnp.concatenate(
                [
                    jnp.concatenate(
                        [low_ref[k, patch_rows(2 * y + a, e, breadth), :] for k in range(low_ref.shape[0])],
                        axis=1,
                    )
                    for y in range(pair_rows)
                ],
                axis=0,
            )
            total = total + jnp.dot(
                patch.astype(jnp.bfloat16), w_down_ref[2 * a + e], preferred_element_type=jnp.float32
            )
    reduced_ref[...] = total.astype(jnp.bfloat16)


def mlp_backward_kernel(
    live, mixed_ref, summed_ref, cot_ref, w_in_ref, w_out_ref, w_down_ref, grad_summed_ref,
    grad_mixed_ref, grad_ref, *, layout
):
    breadth = layout[1]
    pair_rows = layout[0] // breadth // 2
    half = breadth // 2
    for a in range(2):
        for e in range(2):
            part = times_transposed(cot_ref[...], w_down_ref[2 * a + e])
            for y in range(pair_rows):
                for k in range(grad_ref.shape[0]):
                    grad_ref[k, patch_rows(2 * y + a, e, breadth), :] = part[
                        y * half : (y + 1) * half, k * 128 : (k + 1) * 128
                    ]
    normed, inv_std = normalize(mixed_ref[...].astype(jnp.float32))
    hidden = jnp.dot(normed.astype(jnp.bfloat16), w_in_ref[...], preferred_element_type=jnp.float32)
    cdf = 0.5 * (1.0 + lax.erf(hidden * ROOT_HALF))
    slope = cdf + hidden * INV_ROOT_TAU * jnp.exp(-0.5 * hidden * hidden)
    down_normed, down_inv = normalize(summed_ref[...].astype(jnp.float32))
    grad_normed = jnp.concatenate([grad_ref[k] for k in range(grad_ref.shape[0])], axis=1)
    grad_summed = normalize_back(grad_normed, down_normed, down_inv).astype(jnp.bfloat16)
    grad_summed_ref[...] = grad_summed
    grad_hidden = (times_transposed(grad_summed, w_out_ref[...]) * slope).astype(jnp.bfloat16)
    grad_norm_in = times_transposed(grad_hidden, w_in_ref[...])
    grad_owned_mixed = normalize_back(grad_norm_in, normed, inv_std)
    grad_mixed_ref[...] = jnp.where(pixel_live(live, layout), grad_owned_mixed, 0.0).astype(jnp.bfloat16)


def pixel_live(live, layout):
    block, breadth, tile_side, tile_cols = layout
    band = block // breadth // tile_side
    place = lax.broadcasted_iota(jnp.int32, (block, 1), 0)
    tile = (place // breadth // tile_side) * tile_cols + (place % breadth) // tile_side
    first = pl.program_id(0) * band * tile_cols
    flag = jnp.zeros((block, 1), jnp.int32)
    for index in range(band * tile_cols):
        flag = jnp.where(tile == index, live[first + index], flag)
    return flag > 0


def pixel_call(kernel, live, operands, kinds, outputs, layout, scratch):
    block = layout[0]
    steps = operands[0].shape[0] // block
    specs = []
    for operand, kind in zip(operands, kinds):
        if kind == "whole":
            specs.append(pl.BlockSpec(operand.shape, lambda i, live, n=operand.ndim: (0,) * n))
        else:
            rows = operand.shape[0] // steps
            specs.append(pl.BlockSpec((rows, operand.shape[1]), lambda i, live: (i, 0)))
    return pl.pallas_call(
        lambda *refs: kernel(*refs, layout=layout),
        grid_spec=pltpu.PrefetchScalarGridSpec(
            num_scalar_prefetch=1,
            grid=(steps,),
            in_specs=specs,
            out_specs=[
                pl.BlockSpec((rows // steps, width), lambda i, live: (i, 0)) for rows, width, _ in outputs
            ],
            scratch_shapes=[pltpu.VMEM((width // 128, block, 128), jnp.float32) for width in scratch],
        ),
        out_shape=[jax.ShapeDtypeStruct((rows, width), dtype) for rows, width, dtype in outputs],
    )(live, *operands)


def on_device(
    image,
    depth_kernel,
    weight_in,
    weight_out,
    weight_down,
    tissue_mask,
    tile_counts,
    tile_owner,
    tile_slot,
    cotangent,
):
    height, breadth, channels = image.shape
    tile_rows, tile_cols = tissue_mask.shape
    tile_side = height // tile_rows
    outputs = weight_down.shape[3]
    reach = KS // 2
    peer_count = lax.axis_size("col")
    capacity = tile_rows * tile_cols // peer_count
    pixels = height * breadth
    routed = routed_tiles(tile_counts, tile_owner, tile_slot, peer_count, capacity)
    live = routed & (tissue_mask != 0)
    live = live.reshape(-1).astype(jnp.int32)
    band = 2 if tile_rows % 2 == 0 else 1
    layout = (band * tile_side * breadth, breadth, tile_side, tile_cols)
    taps = depth_kernel.reshape(KS * KS, channels).astype(jnp.float32)
    mixed = depthwise(halo_pieces(image, reach), taps, reach)
    mixed = mixed.reshape(pixels, channels)
    weight_quad = weight_down.reshape(4, channels, outputs)
    patches = pixels // 4
    summed, reduced = pixel_call(
        mlp_forward_kernel,
        live,
        (mixed, image.reshape(pixels, channels), weight_in, weight_out, weight_quad),
        ("rows", "rows", "whole", "whole", "whole"),
        ((pixels, channels, jnp.bfloat16), (patches, outputs, jnp.bfloat16)),
        layout,
        (channels,),
    )
    reduced = reduced.reshape(height // 2, breadth // 2, outputs)
    grad_summed, grad_mixed = pixel_call(
        mlp_backward_kernel,
        live,
        (mixed, summed, cotangent.reshape(patches, outputs), weight_in, weight_out, weight_quad),
        ("rows", "rows", "rows", "whole", "whole", "whole"),
        ((pixels, channels, jnp.bfloat16), (pixels, channels, jnp.bfloat16)),
        layout,
        (channels,),
    )
    grad_image = depthwise(
        halo_pieces(grad_mixed.reshape(height, breadth, channels), reach),
        taps,
        reach,
        base=grad_summed.reshape(height, breadth, channels),
        flip=True,
    )
    return (reduced, grad_image)


def solution(mesh):
    in_specs = (
        P("row", "col", None),
        P(),
        P(),
        P(),
        P(),
        P("row", "col"),
        P("row", None, None),
        P("row", "col"),
        P("row", "col"),
        P("row", "col", None),
    )
    out_specs = (P("row", "col", None), P("row", "col", None))
    return jax.shard_map(
        on_device, mesh=mesh, in_specs=in_specs, out_specs=out_specs, check_vma=False
    )
```

```python
import jax
import jax.numpy as jnp
from jax import lax
from jax.sharding import PartitionSpec as P
from jax.experimental import pallas as pl
from jax.experimental.pallas import tpu as pltpu

KS = 7
LIVE_DEV = 18


EPSILON = 1e-06
ROOT_HALF = 0.7071067811865476
INV_ROOT_TAU = 0.3989422804014327


def halo_pieces(cells, width):
    rows = lax.axis_size("row")
    cols = lax.axis_size("col")
    down = [(i, i + 1) for i in range(rows - 1)]
    up = [(i + 1, i) for i in range(rows - 1)]
    top = lax.ppermute(cells[cells.shape[0] - width :], "row", down)
    bottom = lax.ppermute(cells[:width], "row", up)
    edge = cells.shape[1] - width
    left_strip = jnp.concatenate([top[:, edge:], cells[:, edge:], bottom[:, edge:]], axis=0)
    right_strip = jnp.concatenate([top[:, :width], cells[:, :width], bottom[:, :width]], axis=0)
    left = lax.ppermute(left_strip, "col", [(i, i + 1) for i in range(cols - 1)])
    right = lax.ppermute(right_strip, "col", [(i + 1, i) for i in range(cols - 1)])
    return (cells, top, bottom, left, right)


def depthwise_kernel(
    image_ref, top_ref, bottom_ref, left_ref, right_ref, k_ref, *rest, reach, chunk, flip
):
    if len(rest) == 5:
        base_ref, out_ref, framed_ref, shifted_ref, total_ref = rest
    else:
        base_ref = None
        out_ref, framed_ref, shifted_ref, total_ref = rest
    height, breadth, _ = out_ref.shape
    side = 2 * reach + 1
    framed_ref[reach : reach + height, reach : reach + breadth, :] = image_ref[...].astype(jnp.float32)
    framed_ref[:reach, reach : reach + breadth, :] = top_ref[...].astype(jnp.float32)
    framed_ref[reach + height :, reach : reach + breadth, :] = bottom_ref[...].astype(jnp.float32)
    framed_ref[:, :reach, :] = left_ref[...].astype(jnp.float32)
    framed_ref[:, reach + breadth :, :] = right_ref[...].astype(jnp.float32)
    for shift_c in range(side):
        shifted_ref[...] = framed_ref[:, shift_c : shift_c + breadth, :]

        def body(step, carry, shift_c=shift_c):
            start = pl.multiple_of(step * chunk, chunk)
            if shift_c > 0:
                total = total_ref[pl.ds(start, chunk)]
            elif base_ref is not None:
                total = base_ref[pl.ds(start, chunk)].astype(jnp.float32)
            else:
                total = jnp.zeros((chunk, breadth, out_ref.shape[2]), jnp.float32)
            for shift_r in range(side):
                if flip:
                    index = (side - 1 - shift_r) * side + (side - 1 - shift_c)
                else:
                    index = shift_r * side + shift_c
                tap = k_ref[pl.ds(index, 1), :]
                total = total + shifted_ref[pl.ds(start + shift_r, chunk)] * tap[None]
            if shift_c == side - 1:
                out_ref[pl.ds(start, chunk)] = total.astype(out_ref.dtype)
            else:
                total_ref[pl.ds(start, chunk)] = total
            return carry

        lax.fori_loop(0, height // chunk, body, 0, unroll=4)


def depthwise(pieces, taps, reach, base=None, flip=False, lanes=128, chunk=8):
    image = pieces[0]
    height, breadth, channels = image.shape
    framed = (height + 2 * reach, breadth + 2 * reach)
    in_specs = [
        pl.BlockSpec((height, breadth, lanes), lambda c: (0, 0, c)),
        pl.BlockSpec((reach, breadth, lanes), lambda c: (0, 0, c)),
        pl.BlockSpec((reach, breadth, lanes), lambda c: (0, 0, c)),
        pl.BlockSpec((framed[0], reach, lanes), lambda c: (0, 0, c)),
        pl.BlockSpec((framed[0], reach, lanes), lambda c: (0, 0, c)),
        pl.BlockSpec((taps.shape[0], lanes), lambda c: (0, c)),
    ]
    operands = list(pieces) + [taps]
    if base is not None:
        in_specs.append(pl.BlockSpec((height, breadth, lanes), lambda c: (0, 0, c)))
        operands.append(base)
    return pl.pallas_call(
        lambda *refs: depthwise_kernel(*refs, reach=reach, chunk=chunk, flip=flip),
        grid=(channels // lanes,),
        in_specs=in_specs,
        out_specs=pl.BlockSpec((height, breadth, lanes), lambda c: (0, 0, c)),
        out_shape=jax.ShapeDtypeStruct((height, breadth, channels), jnp.bfloat16),
        scratch_shapes=[
            pltpu.VMEM((framed[0], framed[1], lanes), jnp.float32),
            pltpu.VMEM((framed[0], breadth, lanes), jnp.float32),
            pltpu.VMEM((height, breadth, lanes), jnp.float32),
        ],
    )(*operands)


def normalize(values):
    average = jnp.mean(values, axis=-1, keepdims=True)
    centered = values - average
    inv_std = lax.rsqrt(jnp.mean(centered * centered, axis=-1, keepdims=True) + EPSILON)
    return (centered * inv_std, inv_std)


def normalize_back(gradient, normed, inv_std):
    return inv_std * (
        gradient
        - jnp.mean(gradient, axis=-1, keepdims=True)
        - normed * jnp.mean(gradient * normed, axis=-1, keepdims=True)
    )


def times_transposed(left, right):
    return lax.dot_general(
        left, right, (((1,), (1,)), ((), ())), preferred_element_type=jnp.float32
    )


def routed_tiles(tile_counts, tile_owner, tile_slot, peer_count, capacity):
    count_table = tile_counts[0]
    before = jnp.cumsum(count_table, axis=0) - count_table
    column_ids = jnp.arange(peer_count, dtype=jnp.int32)
    own_column = column_ids == lax.axis_index("col")
    my_bases = jnp.sum(jnp.where(own_column[:, None], before, 0), axis=0)
    my_counts = jnp.sum(jnp.where(own_column[:, None], count_table, 0), axis=0)
    owner_hits = tile_owner[:, :, None] == column_ids[None, None, :]
    base = jnp.sum(jnp.where(owner_hits, my_bases[None, None, :], 0), axis=2)
    quota = jnp.sum(jnp.where(owner_hits, my_counts[None, None, :], 0), axis=2)
    rank = tile_slot - base
    return (
        (tile_owner >= 0)
        & (rank >= 0)
        & (rank < capacity)
        & (rank < quota)
        & (tile_slot < LIVE_DEV)
    )


def patch_rows(row, column, breadth):
    return pl.ds(row * breadth + column, breadth // 2, stride=2)


def mlp_forward_kernel(
    live, mixed_ref, image_ref, w_in_ref, w_out_ref, w_down_ref, summed_ref, reduced_ref, low_ref,
    *, layout
):
    normed, _ = normalize(mixed_ref[...].astype(jnp.float32))
    hidden = jnp.dot(normed.astype(jnp.bfloat16), w_in_ref[...], preferred_element_type=jnp.float32)
    cdf = 0.5 * (1.0 + lax.erf(hidden * ROOT_HALF))
    activated = (hidden * cdf).astype(jnp.bfloat16)
    branch = jnp.dot(activated, w_out_ref[...], preferred_element_type=jnp.float32)
    branch = jnp.where(pixel_live(live, layout), branch.astype(jnp.bfloat16).astype(jnp.float32), 0.0)
    summed = (image_ref[...].astype(jnp.float32) + branch).astype(jnp.bfloat16)
    summed_ref[...] = summed
    down_normed, _ = normalize(summed.astype(jnp.float32))
    low = down_normed.astype(jnp.bfloat16).astype(jnp.float32)
    for k in range(low_ref.shape[0]):
        low_ref[k] = low[:, k * 128 : (k + 1) * 128]
    breadth = layout[1]
    pair_rows = layout[0] // breadth // 2
    total = jnp.zeros(reduced_ref.shape, jnp.float32)
    for a in range(2):
        for e in range(2):
            patch = jnp.concatenate(
                [
                    jnp.concatenate(
                        [low_ref[k, patch_rows(2 * y + a, e, breadth), :] for k in range(low_ref.shape[0])],
                        axis=1,
                    )
                    for y in range(pair_rows)
                ],
                axis=0,
            )
            total = total + jnp.dot(
                patch.astype(jnp.bfloat16), w_down_ref[2 * a + e], preferred_element_type=jnp.float32
            )
    reduced_ref[...] = total.astype(jnp.bfloat16)


def mlp_backward_kernel(
    live, mixed_ref, summed_ref, cot_ref, w_in_ref, w_out_ref, w_down_ref, grad_summed_ref,
    grad_mixed_ref, grad_ref, *, layout
):
    breadth = layout[1]
    pair_rows = layout[0] // breadth // 2
    half = breadth // 2
    for a in range(2):
        for e in range(2):
            part = times_transposed(cot_ref[...], w_down_ref[2 * a + e])
            for y in range(pair_rows):
                for k in range(grad_ref.shape[0]):
                    grad_ref[k, patch_rows(2 * y + a, e, breadth), :] = part[
                        y * half : (y + 1) * half, k * 128 : (k + 1) * 128
                    ]
    normed, inv_std = normalize(mixed_ref[...].astype(jnp.float32))
    hidden = jnp.dot(normed.astype(jnp.bfloat16), w_in_ref[...], preferred_element_type=jnp.float32)
    cdf = 0.5 * (1.0 + lax.erf(hidden * ROOT_HALF))
    slope = cdf + hidden * INV_ROOT_TAU * jnp.exp(-0.5 * hidden * hidden)
    down_normed, down_inv = normalize(summed_ref[...].astype(jnp.float32))
    grad_normed = jnp.concatenate([grad_ref[k] for k in range(grad_ref.shape[0])], axis=1)
    grad_summed = normalize_back(grad_normed, down_normed, down_inv).astype(jnp.bfloat16)
    grad_summed_ref[...] = grad_summed
    grad_hidden = (times_transposed(grad_summed, w_out_ref[...]) * slope).astype(jnp.bfloat16)
    grad_norm_in = times_transposed(grad_hidden, w_in_ref[...])
    grad_owned_mixed = normalize_back(grad_norm_in, normed, inv_std)
    grad_mixed_ref[...] = jnp.where(pixel_live(live, layout), grad_owned_mixed, 0.0).astype(jnp.bfloat16)


def pixel_live(live, layout):
    block, breadth, tile_side, tile_cols = layout
    band = block // breadth // tile_side
    place = lax.broadcasted_iota(jnp.int32, (block, 1), 0)
    tile = (place // breadth // tile_side) * tile_cols + (place % breadth) // tile_side
    first = pl.program_id(0) * band * tile_cols
    flag = jnp.zeros((block, 1), jnp.int32)
    for index in range(band * tile_cols):
        flag = jnp.where(tile == index, live[first + index], flag)
    return flag > 0


def pixel_call(kernel, live, operands, kinds, outputs, layout, scratch):
    block = layout[0]
    steps = operands[0].shape[0] // block
    specs = []
    for operand, kind in zip(operands, kinds):
        if kind == "whole":
            specs.append(pl.BlockSpec(operand.shape, lambda i, live, n=operand.ndim: (0,) * n))
        else:
            rows = operand.shape[0] // steps
            specs.append(pl.BlockSpec((rows, operand.shape[1]), lambda i, live: (i, 0)))
    return pl.pallas_call(
        lambda *refs: kernel(*refs, layout=layout),
        grid_spec=pltpu.PrefetchScalarGridSpec(
            num_scalar_prefetch=1,
            grid=(steps,),
            in_specs=specs,
            out_specs=[
                pl.BlockSpec((rows // steps, width), lambda i, live: (i, 0)) for rows, width, _ in outputs
            ],
            scratch_shapes=[pltpu.VMEM((width // 128, block, 128), jnp.float32) for width in scratch],
        ),
        out_shape=[jax.ShapeDtypeStruct((rows, width), dtype) for rows, width, dtype in outputs],
    )(live, *operands)


def on_device(
    image,
    depth_kernel,
    weight_in,
    weight_out,
    weight_down,
    tissue_mask,
    tile_counts,
    tile_owner,
    tile_slot,
    cotangent,
):
    height, breadth, channels = image.shape
    tile_rows, tile_cols = tissue_mask.shape
    tile_side = height // tile_rows
    outputs = weight_down.shape[3]
    reach = KS // 2
    peer_count = lax.axis_size("col")
    capacity = tile_rows * tile_cols // peer_count
    pixels = height * breadth
    routed = routed_tiles(tile_counts, tile_owner, tile_slot, peer_count, capacity)
    live = routed & (tissue_mask != 0)
    live = live.reshape(-1).astype(jnp.int32)
    band = 2 if tile_rows % 2 == 0 else 1
    layout = (band * tile_side * breadth, breadth, tile_side, tile_cols)
    taps = depth_kernel.reshape(KS * KS, channels).astype(jnp.float32)
    mixed = depthwise(halo_pieces(image, reach), taps, reach)
    mixed = mixed.reshape(pixels, channels)
    weight_quad = weight_down.reshape(4, channels, outputs)
    patches = pixels // 4
    summed, reduced = pixel_call(
        mlp_forward_kernel,
        live,
        (mixed, image.reshape(pixels, channels), weight_in, weight_out, weight_quad),
        ("rows", "rows", "whole", "whole", "whole"),
        ((pixels, channels, jnp.bfloat16), (patches, outputs, jnp.bfloat16)),
        layout,
        (channels,),
    )
    reduced = reduced.reshape(height // 2, breadth // 2, outputs)
    grad_summed, grad_mixed = pixel_call(
        mlp_backward_kernel,
        live,
        (mixed, summed, cotangent.reshape(patches, outputs), weight_in, weight_out, weight_quad),
        ("rows", "rows", "rows", "whole", "whole", "whole"),
        ((pixels, channels, jnp.bfloat16), (pixels, channels, jnp.bfloat16)),
        layout,
        (channels,),
    )
    grad_image = depthwise(
        halo_pieces(grad_mixed.reshape(height, breadth, channels), reach),
        taps,
        reach,
        base=grad_summed.reshape(height, breadth, channels),
        flip=True,
    )
    return (reduced, grad_image)


def solution(mesh):
    in_specs = (
        P("row", "col", None),
        P(),
        P(),
        P(),
        P(),
        P("row", "col"),
        P("row", None, None),
        P("row", "col"),
        P("row", "col"),
        P("row", "col", None),
    )
    out_specs = (P("row", "col", None), P("row", "col", None))
    return jax.shard_map(
        on_device, mesh=mesh, in_specs=in_specs, out_specs=out_specs, check_vma=False
    )
```

```python
import jax
import jax.numpy as jnp
from jax import lax
from jax.sharding import PartitionSpec as P
from jax.experimental import pallas as pl
from jax.experimental.pallas import tpu as pltpu

KS = 7
LIVE_DEV = 18


EPSILON = 1e-06
ROOT_HALF = 0.7071067811865476
INV_ROOT_TAU = 0.3989422804014327


def halo_pieces(cells, width):
    rows = lax.axis_size("row")
    cols = lax.axis_size("col")
    down = [(i, i + 1) for i in range(rows - 1)]
    up = [(i + 1, i) for i in range(rows - 1)]
    top = lax.ppermute(cells[cells.shape[0] - width :], "row", down)
    bottom = lax.ppermute(cells[:width], "row", up)
    edge = cells.shape[1] - width
    left_strip = jnp.concatenate([top[:, edge:], cells[:, edge:], bottom[:, edge:]], axis=0)
    right_strip = jnp.concatenate([top[:, :width], cells[:, :width], bottom[:, :width]], axis=0)
    left = lax.ppermute(left_strip, "col", [(i, i + 1) for i in range(cols - 1)])
    right = lax.ppermute(right_strip, "col", [(i + 1, i) for i in range(cols - 1)])
    return (cells, top, bottom, left, right)


def depthwise_kernel(
    image_ref, top_ref, bottom_ref, left_ref, right_ref, k_ref, *rest, reach, chunk, flip
):
    if len(rest) == 5:
        base_ref, out_ref, framed_ref, shifted_ref, total_ref = rest
    else:
        base_ref = None
        out_ref, framed_ref, shifted_ref, total_ref = rest
    height, breadth, _ = out_ref.shape
    side = 2 * reach + 1
    framed_ref[reach : reach + height, reach : reach + breadth, :] = image_ref[...].astype(jnp.float32)
    framed_ref[:reach, reach : reach + breadth, :] = top_ref[...].astype(jnp.float32)
    framed_ref[reach + height :, reach : reach + breadth, :] = bottom_ref[...].astype(jnp.float32)
    framed_ref[:, :reach, :] = left_ref[...].astype(jnp.float32)
    framed_ref[:, reach + breadth :, :] = right_ref[...].astype(jnp.float32)
    for shift_c in range(side):
        if shift_c > 0:
            shifted_ref[...] = framed_ref[:, shift_c : shift_c + breadth, :]

        def body(step, carry, shift_c=shift_c):
            start = pl.multiple_of(step * chunk, chunk)
            if shift_c > 0:
                total = total_ref[pl.ds(start, chunk)]
            elif base_ref is not None:
                total = base_ref[pl.ds(start, chunk)].astype(jnp.float32)
            else:
                total = jnp.zeros((chunk, breadth, out_ref.shape[2]), jnp.float32)
            for shift_r in range(side):
                if flip:
                    index = (side - 1 - shift_r) * side + (side - 1 - shift_c)
                else:
                    index = shift_r * side + shift_c
                tap = k_ref[pl.ds(index, 1), :]
                if shift_c > 0:
                    window = shifted_ref[pl.ds(start + shift_r, chunk)]
                else:
                    window = framed_ref[pl.ds(start + shift_r, chunk), pl.ds(0, breadth), :]
                total = total + window * tap[None]
            if shift_c == side - 1:
                out_ref[pl.ds(start, chunk)] = total.astype(out_ref.dtype)
            else:
                total_ref[pl.ds(start, chunk)] = total
            return carry

        lax.fori_loop(0, height // chunk, body, 0, unroll=4)


def depthwise(pieces, taps, reach, base=None, flip=False, lanes=128, chunk=8):
    image = pieces[0]
    height, breadth, channels = image.shape
    framed = (height + 2 * reach, breadth + 2 * reach)
    in_specs = [
        pl.BlockSpec((height, breadth, lanes), lambda c: (0, 0, c)),
        pl.BlockSpec((reach, breadth, lanes), lambda c: (0, 0, c)),
        pl.BlockSpec((reach, breadth, lanes), lambda c: (0, 0, c)),
        pl.BlockSpec((framed[0], reach, lanes), lambda c: (0, 0, c)),
        pl.BlockSpec((framed[0], reach, lanes), lambda c: (0, 0, c)),
        pl.BlockSpec((taps.shape[0], lanes), lambda c: (0, c)),
    ]
    operands = list(pieces) + [taps]
    if base is not None:
        in_specs.append(pl.BlockSpec((height, breadth, lanes), lambda c: (0, 0, c)))
        operands.append(base)
    return pl.pallas_call(
        lambda *refs: depthwise_kernel(*refs, reach=reach, chunk=chunk, flip=flip),
        grid=(channels // lanes,),
        in_specs=in_specs,
        out_specs=pl.BlockSpec((height, breadth, lanes), lambda c: (0, 0, c)),
        out_shape=jax.ShapeDtypeStruct((height, breadth, channels), jnp.bfloat16),
        scratch_shapes=[
            pltpu.VMEM((framed[0], framed[1], lanes), jnp.float32),
            pltpu.VMEM((framed[0], breadth, lanes), jnp.float32),
            pltpu.VMEM((height, breadth, lanes), jnp.float32),
        ],
    )(*operands)


def normalize(values):
    average = jnp.mean(values, axis=-1, keepdims=True)
    centered = values - average
    inv_std = lax.rsqrt(jnp.mean(centered * centered, axis=-1, keepdims=True) + EPSILON)
    return (centered * inv_std, inv_std)


def normalize_back(gradient, normed, inv_std):
    return inv_std * (
        gradient
        - jnp.mean(gradient, axis=-1, keepdims=True)
        - normed * jnp.mean(gradient * normed, axis=-1, keepdims=True)
    )


def times_transposed(left, right):
    return lax.dot_general(
        left, right, (((1,), (1,)), ((), ())), preferred_element_type=jnp.float32
    )


def routed_tiles(tile_counts, tile_owner, tile_slot, peer_count, capacity):
    count_table = tile_counts[0]
    before = jnp.cumsum(count_table, axis=0) - count_table
    column_ids = jnp.arange(peer_count, dtype=jnp.int32)
    own_column = column_ids == lax.axis_index("col")
    my_bases = jnp.sum(jnp.where(own_column[:, None], before, 0), axis=0)
    my_counts = jnp.sum(jnp.where(own_column[:, None], count_table, 0), axis=0)
    owner_hits = tile_owner[:, :, None] == column_ids[None, None, :]
    base = jnp.sum(jnp.where(owner_hits, my_bases[None, None, :], 0), axis=2)
    quota = jnp.sum(jnp.where(owner_hits, my_counts[None, None, :], 0), axis=2)
    rank = tile_slot - base
    return (
        (tile_owner >= 0)
        & (rank >= 0)
        & (rank < capacity)
        & (rank < quota)
        & (tile_slot < LIVE_DEV)
    )


def patch_rows(row, column, breadth):
    return pl.ds(row * breadth + column, breadth // 2, stride=2)


def mlp_forward_kernel(
    live, mixed_ref, image_ref, w_in_ref, w_out_ref, w_down_ref, summed_ref, reduced_ref, low_ref,
    *, layout
):
    normed, _ = normalize(mixed_ref[...].astype(jnp.float32))
    hidden = jnp.dot(normed.astype(jnp.bfloat16), w_in_ref[...], preferred_element_type=jnp.float32)
    cdf = 0.5 * (1.0 + lax.erf(hidden * ROOT_HALF))
    activated = (hidden * cdf).astype(jnp.bfloat16)
    branch = jnp.dot(activated, w_out_ref[...], preferred_element_type=jnp.float32)
    branch = jnp.where(pixel_live(live, layout), branch.astype(jnp.bfloat16).astype(jnp.float32), 0.0)
    summed = (image_ref[...].astype(jnp.float32) + branch).astype(jnp.bfloat16)
    summed_ref[...] = summed
    down_normed, _ = normalize(summed.astype(jnp.float32))
    low = down_normed.astype(jnp.bfloat16).astype(jnp.float32)
    for k in range(low_ref.shape[0]):
        low_ref[k] = low[:, k * 128 : (k + 1) * 128]
    breadth = layout[1]
    pair_rows = layout[0] // breadth // 2
    total = jnp.zeros(reduced_ref.shape, jnp.float32)
    for a in range(2):
        for e in range(2):
            patch = jnp.concatenate(
                [
                    jnp.concatenate(
                        [low_ref[k, patch_rows(2 * y + a, e, breadth), :] for k in range(low_ref.shape[0])],
                        axis=1,
                    )
                    for y in range(pair_rows)
                ],
                axis=0,
            )
            total = total + jnp.dot(
                patch.astype(jnp.bfloat16), w_down_ref[2 * a + e], preferred_element_type=jnp.float32
            )
    reduced_ref[...] = total.astype(jnp.bfloat16)


def mlp_backward_kernel(
    live, mixed_ref, summed_ref, cot_ref, w_in_ref, w_out_ref, w_down_ref, grad_summed_ref,
    grad_mixed_ref, grad_ref, *, layout
):
    breadth = layout[1]
    pair_rows = layout[0] // breadth // 2
    half = breadth // 2
    for a in range(2):
        for e in range(2):
            part = times_transposed(cot_ref[...], w_down_ref[2 * a + e])
            for y in range(pair_rows):
                for k in range(grad_ref.shape[0]):
                    grad_ref[k, patch_rows(2 * y + a, e, breadth), :] = part[
                        y * half : (y + 1) * half, k * 128 : (k + 1) * 128
                    ]
    normed, inv_std = normalize(mixed_ref[...].astype(jnp.float32))
    hidden = jnp.dot(normed.astype(jnp.bfloat16), w_in_ref[...], preferred_element_type=jnp.float32)
    cdf = 0.5 * (1.0 + lax.erf(hidden * ROOT_HALF))
    slope = cdf + hidden * INV_ROOT_TAU * jnp.exp(-0.5 * hidden * hidden)
    down_normed, down_inv = normalize(summed_ref[...].astype(jnp.float32))
    grad_normed = jnp.concatenate([grad_ref[k] for k in range(grad_ref.shape[0])], axis=1)
    grad_summed = normalize_back(grad_normed, down_normed, down_inv).astype(jnp.bfloat16)
    grad_summed_ref[...] = grad_summed
    grad_hidden = (times_transposed(grad_summed, w_out_ref[...]) * slope).astype(jnp.bfloat16)
    grad_norm_in = times_transposed(grad_hidden, w_in_ref[...])
    grad_owned_mixed = normalize_back(grad_norm_in, normed, inv_std)
    grad_mixed_ref[...] = jnp.where(pixel_live(live, layout), grad_owned_mixed, 0.0).astype(jnp.bfloat16)


def pixel_live(live, layout):
    block, breadth, tile_side, tile_cols = layout
    band = block // breadth // tile_side
    place = lax.broadcasted_iota(jnp.int32, (block, 1), 0)
    tile = (place // breadth // tile_side) * tile_cols + (place % breadth) // tile_side
    first = pl.program_id(0) * band * tile_cols
    flag = jnp.zeros((block, 1), jnp.int32)
    for index in range(band * tile_cols):
        flag = jnp.where(tile == index, live[first + index], flag)
    return flag > 0


def pixel_call(kernel, live, operands, kinds, outputs, layout, scratch):
    block = layout[0]
    steps = operands[0].shape[0] // block
    specs = []
    for operand, kind in zip(operands, kinds):
        if kind == "whole":
            specs.append(pl.BlockSpec(operand.shape, lambda i, live, n=operand.ndim: (0,) * n))
        else:
            rows = operand.shape[0] // steps
            specs.append(pl.BlockSpec((rows, operand.shape[1]), lambda i, live: (i, 0)))
    return pl.pallas_call(
        lambda *refs: kernel(*refs, layout=layout),
        grid_spec=pltpu.PrefetchScalarGridSpec(
            num_scalar_prefetch=1,
            grid=(steps,),
            in_specs=specs,
            out_specs=[
                pl.BlockSpec((rows // steps, width), lambda i, live: (i, 0)) for rows, width, _ in outputs
            ],
            scratch_shapes=[pltpu.VMEM((width // 128, block, 128), jnp.float32) for width in scratch],
        ),
        out_shape=[jax.ShapeDtypeStruct((rows, width), dtype) for rows, width, dtype in outputs],
    )(live, *operands)


def on_device(
    image,
    depth_kernel,
    weight_in,
    weight_out,
    weight_down,
    tissue_mask,
    tile_counts,
    tile_owner,
    tile_slot,
    cotangent,
):
    height, breadth, channels = image.shape
    tile_rows, tile_cols = tissue_mask.shape
    tile_side = height // tile_rows
    outputs = weight_down.shape[3]
    reach = KS // 2
    peer_count = lax.axis_size("col")
    capacity = tile_rows * tile_cols // peer_count
    pixels = height * breadth
    routed = routed_tiles(tile_counts, tile_owner, tile_slot, peer_count, capacity)
    live = routed & (tissue_mask != 0)
    live = live.reshape(-1).astype(jnp.int32)
    band = 2 if tile_rows % 2 == 0 else 1
    layout = (band * tile_side * breadth, breadth, tile_side, tile_cols)
    taps = depth_kernel.reshape(KS * KS, channels).astype(jnp.float32)
    mixed = depthwise(halo_pieces(image, reach), taps, reach)
    mixed = mixed.reshape(pixels, channels)
    weight_quad = weight_down.reshape(4, channels, outputs)
    patches = pixels // 4
    summed, reduced = pixel_call(
        mlp_forward_kernel,
        live,
        (mixed, image.reshape(pixels, channels), weight_in, weight_out, weight_quad),
        ("rows", "rows", "whole", "whole", "whole"),
        ((pixels, channels, jnp.bfloat16), (patches, outputs, jnp.bfloat16)),
        layout,
        (channels,),
    )
    reduced = reduced.reshape(height // 2, breadth // 2, outputs)
    grad_summed, grad_mixed = pixel_call(
        mlp_backward_kernel,
        live,
        (mixed, summed, cotangent.reshape(patches, outputs), weight_in, weight_out, weight_quad),
        ("rows", "rows", "rows", "whole", "whole", "whole"),
        ((pixels, channels, jnp.bfloat16), (pixels, channels, jnp.bfloat16)),
        layout,
        (channels,),
    )
    grad_image = depthwise(
        halo_pieces(grad_mixed.reshape(height, breadth, channels), reach),
        taps,
        reach,
        base=grad_summed.reshape(height, breadth, channels),
        flip=True,
    )
    return (reduced, grad_image)


def solution(mesh):
    in_specs = (
        P("row", "col", None),
        P(),
        P(),
        P(),
        P(),
        P("row", "col"),
        P("row", None, None),
        P("row", "col"),
        P("row", "col"),
        P("row", "col", None),
    )
    out_specs = (P("row", "col", None), P("row", "col", None))
    return jax.shard_map(
        on_device, mesh=mesh, in_specs=in_specs, out_specs=out_specs, check_vma=False
    )
```
